32 devices in a mesh: seq: 8 (over z, x), grp: 4 (over y, core).
Axes of the slice: x: 2, y: 2, z: 4, core: 2. Of those that a mesh axis runs over, the one named last changes fastest.
Arguments:
- xbc_in: bfloat16 [4096, 4352], P(('grp', 'seq')), parts along dimension 0, may hold values from -6 to 6
- conv_weight: float32 [4, 4352], replicated, may hold values from -3 to 3
- conv_bias: float32 [4352], replicated, may hold values from -2 to 2
- dt_raw: float32 [4096, 64], P(('grp', 'seq')), parts along dimension 0, may hold values from -6 to 358.4
- decay_rate: float32 [64], replicated, may hold values from 0.0001953125 to 0.08
- skip: float32 [64], replicated, may hold values from 0.5 to 2
- level_table: float32 [8, 12, 64], replicated, may hold values from 0.05 to 0.5
- group_class: int32 [64], P(('grp', 'seq')), parts along dimension 0, may hold values from 0 to 7
- cotangent: bfloat16 [4096, 4096], P(('grp', 'seq')), parts along dimension 0, may hold values from -6 to 6
Outputs:
- ssm_out: bfloat16 [4096, 4096], P(('grp', 'seq')), parts along dimension 0
- grad_c_in: float32 [4096, 128], P(('grp', 'seq')), parts along dimension 0
- level_update: float32 [32, 12, 64], P('grp'), parts along dimension 0
The draws below stay inside these ranges and needn't reach their ends.
There are 4 independent parts, one for each index of `grp`. The reference program is written for one: setup_inputs(seed, part) draws one part's arguments, and reference() takes and returns one part's arrays. A program takes and returns all parts, laid end to end along the dimension named above; an argument that names none is the same for every part. Nothing has to cross between parts.
All inputs are finite; a program needn't handle non-finite values.
Results may differ from the reference program's by a relative error of at most 0.0059.
Values may be sent and summed in bfloat16 or wider, within the bound.
No kernel may reach another device: no remote copies, remote signals or barrier semaphores. Data moves between devices by JAX's collectives and lax.ppermute only.
A program may use at most 128 MiB of HBM per device.

```python
import math
import jax
import jax.numpy as jnp
from jax import lax

H = 64
P_SIZE = 64
DSTATE = 128
CH = 64
KCONV = 4
LEVELS = 12
CLASSES = 8
SEQ_LEN = 1024
GROUPS = 16
CCH = 4352


def draw_decay_rate(key, part):
    first, second, third = jax.random.split(key, 3)
    lowest = math.log(0.2 / SEQ_LEN)
    middle = math.log(2.5 / SEQ_LEN)
    highest = math.log(0.08)
    share = 0.5
    chooser = jax.random.uniform(first, (H,), jnp.float32)
    slower = jnp.exp(jax.random.uniform(second, (H,), jnp.float32, minval=lowest, maxval=middle))
    faster = jnp.exp(jax.random.uniform(third, (H,), jnp.float32, minval=middle, maxval=highest))
    return jnp.where(chooser < share, slower, faster).astype(jnp.float32)


def draw_dt_raw(key, part):
    first, second = jax.random.split(key, 2)
    baseline = jnp.clip(jax.random.normal(first, (SEQ_LEN, H), jnp.float32), -6.0, 6.0)
    places = jax.random.randint(second, (4,), 0, SEQ_LEN)
    bursty = jnp.any(jnp.arange(SEQ_LEN)[:, None] == places[None, :], axis=1)
    return jnp.where(bursty[:, None], 0.35 * SEQ_LEN, baseline).astype(jnp.float32)


def plant(drawn, own_key, smallest, high):
    longest = drawn.shape.index(max(drawn.shape))
    spots = []
    for shift in (0, 1):
        where = [jax.random.randint(jax.random.fold_in(own_key, axis), (), 0, length) for axis, length in enumerate(drawn.shape)]
        where[longest] = (where[longest] + shift) % drawn.shape[longest]
        spots.append(tuple(where))
    return drawn.at[spots[0]].set(smallest).at[spots[1]].set(high)


def steps_of(key, extent, cuts, smallest, high):
    factor_of, own = 1.0, jax.random.fold_in(key, 6)
    for dim, parts in cuts:
        draws = jnp.exp(jax.random.uniform(jax.random.fold_in(own, dim), (parts,), jnp.float32, smallest / len(cuts), high / len(cuts)))
        factor_of = factor_of * jnp.repeat(draws, extent[dim] // parts).reshape([-1 if axis == dim else 1 for axis in range(len(extent))])
    return factor_of


def bell_draw(rng, extent, scale, bound, cuts=(), held_as=jnp.bfloat16):
    drawn = jax.random.normal(rng, extent, jnp.float32) * scale
    if len(cuts) > 0:
        drawn = steps_of(rng, extent, cuts, -0.22, 0.18) * drawn
    return jnp.clip(drawn, min=-bound, max=bound).astype(held_as)


def setup_inputs(seed: int = 0, part: int = 0) -> dict:
    key_list = jax.random.split(jax.random.key(seed), 10)
    part_keys = jax.random.split(jax.random.fold_in(key_list[9], part), 10)
    return {
        "xbc_in": bell_draw(part_keys[0], (SEQ_LEN, CCH), 1.0, 6.0, ((0, 8),)),
        "conv_weight": bell_draw(key_list[1], (KCONV, CCH), KCONV ** -0.5, 3.0, (), jnp.float32),
        "conv_bias": bell_draw(key_list[2], (CCH,), 0.3, 2.0, (), jnp.float32),
        "dt_raw": draw_dt_raw(jax.random.fold_in(jax.random.fold_in(key_list[9], part), 71), part),
        "decay_rate": draw_decay_rate(jax.random.fold_in(key_list[9], 71), part),
        "skip": jnp.clip(jnp.exp(jax.random.uniform(key_list[5], (H,), jnp.float32, math.log(0.5), math.log(2.0))), 0.5, 2.0),
        "level_table": jnp.clip(jnp.exp(jax.random.uniform(key_list[6], (CLASSES, LEVELS, H), jnp.float32, math.log(0.05), math.log(0.5))), 0.05, 0.5),
        "group_class": plant(jax.random.randint(part_keys[7], (GROUPS,), 0, CLASSES), jax.random.fold_in(part_keys[7], 1), 0, CLASSES - 1).astype(jnp.int32),
        "cotangent": bell_draw(part_keys[8], (SEQ_LEN, H * P_SIZE), 1.0, 6.0, ((0, 8),)),
    }


def contract(form, left, right):
    return jnp.einsum(form, left.astype(jnp.float32), right.astype(jnp.float32), precision=lax.Precision.HIGHEST)

def conv_forward(window, conv_weight, conv_bias, length):
    result = jnp.zeros((length, window.shape[1]), jnp.float32) + conv_bias[None, :]
    for offset in range(conv_weight.shape[0]):
        result = result + window[offset:offset + length].astype(jnp.float32) * conv_weight[offset][None, :]
    return result

def split_act(preact, heads, head_dim, state_dim):
    length = preact.shape[0]
    inner = heads * head_dim
    x_act = jax.nn.silu(preact[:, :inner]).astype(jnp.bfloat16).reshape(length, heads, head_dim)
    b_key = preact[:, inner:inner + state_dim].astype(jnp.bfloat16)
    c_query = preact[:, inner + state_dim:].astype(jnp.bfloat16)
    return (x_act, b_key, c_query)

def local_group(x_part, b_part, c_part, decay_part, grad_part, weight_zero):
    length = x_part.shape[0]
    state_dim = b_part.shape[1]
    cumul = jnp.cumsum(decay_part, axis=0)
    scores = contract('tn,sn->ts', c_part, b_part)
    causal = (jnp.arange(length)[:, None] >= jnp.arange(length)[None, :])[None]
    across = jnp.transpose(cumul)
    spread = across[:, :, None] - across[:, None, :]
    fading = jnp.where(causal, jnp.exp(jnp.where(causal, spread, 0.0)), 0.0)
    basic = fading * scores[None] / state_dim
    intra = (weight_zero[:, None, None] * basic).astype(jnp.bfloat16)
    y_inner = contract('hts,shp->thp', intra, x_part)
    x_faded = (x_part * jnp.exp(cumul[-1][None, :] - cumul)[:, :, None]).astype(jnp.bfloat16)
    group_state = contract('sn,shp->hnp', b_part, x_faded)
    products = contract('thp,shp->hts', grad_part, x_part)
    grad_weight = (lax.optimization_barrier(jnp.sum(weight_zero[:, None, None] * fading * products, axis=0)) / state_dim).astype(jnp.bfloat16)
    grad_inner = contract('ts,sn->tn', grad_weight, b_part)
    level_zero = lax.optimization_barrier(jnp.sum(basic * products, axis=(1, 2)))
    return (y_inner, group_state, cumul, grad_inner, level_zero)

def cross_group(fenwick, c_part, cumul, grad_part, weight_levels):
    state_dim = c_part.shape[1]
    mixed = jnp.einsum('lh,lhnp->hnp', weight_levels, fenwick, precision=lax.Precision.HIGHEST).astype(jnp.bfloat16)
    scaled = jnp.exp(cumul) / state_dim
    query_faded = (c_part[:, None, :] * scaled[:, :, None]).astype(jnp.bfloat16)
    y_cross = contract('thn,hnp->thp', query_faded, mixed)
    backed = contract('hnp,thp->thn', mixed, grad_part)
    grad_cross = lax.optimization_barrier(jnp.sum(backed * scaled[:, :, None], axis=1))
    gram = contract('thn,thp->hnp', query_faded, grad_part)
    level_rest = jnp.einsum('lhnp,hnp->lh', fenwick, gram, precision=lax.Precision.HIGHEST)
    return (y_cross, grad_cross, level_rest)

def advance(fenwick, group_state, group_decay, position):
    slots = jnp.arange(fenwick.shape[0], dtype=jnp.int32)
    digits = jnp.right_shift(position.astype(jnp.int32), slots) & 1
    trailing = jnp.cumprod(digits).astype(jnp.int32)
    carried = jnp.sum(trailing).astype(jnp.int32)
    faded = fenwick * jnp.exp(group_decay)[None, :, None, None]
    taken = trailing.astype(jnp.float32)[:, None, None, None]
    merged = group_state + lax.optimization_barrier(jnp.sum(faded * taken, axis=0))
    target = (slots == carried).astype(jnp.float32)[:, None, None, None]
    return faded * (1.0 - taken) + target * merged[None]

def reference(xbc_in, conv_weight, conv_bias, dt_raw, decay_rate, skip, level_table, group_class, cotangent):
    inner = H * P_SIZE
    window = jnp.concatenate([jnp.zeros((KCONV - 1, CCH), jnp.bfloat16), xbc_in], axis=0)
    preact = conv_forward(window, conv_weight, conv_bias, SEQ_LEN)
    x_act, b_key, c_query = split_act(preact, H, P_SIZE, DSTATE)
    log_decay = -decay_rate[None, :] * jax.nn.softplus(dt_raw)
    grad_out = cotangent.reshape(SEQ_LEN, H, P_SIZE)
    series = (x_act.reshape(GROUPS, CH, H, P_SIZE), b_key.reshape(GROUPS, CH, DSTATE), c_query.reshape(GROUPS, CH, DSTATE), log_decay.reshape(GROUPS, CH, H), grad_out.reshape(GROUPS, CH, H, P_SIZE), group_class, jnp.arange(GROUPS, dtype=jnp.int32))

    def group_step(carry, entry):
        fenwick, grads = carry
        x_part, b_part, c_part, decay_part, grad_part, klass, position = entry
        picked = (klass == jnp.arange(CLASSES, dtype=jnp.int32)).astype(jnp.float32)
        weight_row = jnp.einsum('k,klh->lh', picked, level_table, precision=lax.Precision.HIGHEST)
        y_inner, group_state, cumul, grad_inner, level_zero = local_group(x_part, b_part, c_part, decay_part, grad_part, weight_row[0])
        y_cross, grad_cross, level_rest = cross_group(fenwick, c_part, cumul, grad_part, weight_row[1:])
        output = (y_inner + y_cross + skip[None, :, None] * x_part).astype(jnp.bfloat16)
        level_full = jnp.concatenate([level_zero[None], level_rest], axis=0)
        grads = grads + picked[:, None, None] * level_full[None]
        fenwick = advance(fenwick, group_state, cumul[-1], position)
        return ((fenwick, grads), (output, grad_inner + grad_cross))
    start = (jnp.zeros((LEVELS - 1, H, DSTATE, P_SIZE), jnp.float32), jnp.zeros((CLASSES, LEVELS, H), jnp.float32))
    (fenwick, grads), (outputs, grad_query) = lax.scan(group_step, start, series)
    ssm_out = outputs.reshape(SEQ_LEN, inner)
    grad_query = grad_query.reshape(SEQ_LEN, DSTATE)
    extended = jnp.concatenate([grad_query, jnp.zeros((KCONV - 1, DSTATE), jnp.float32)], axis=0)
    query_taps = conv_weight[:, inner + DSTATE:]
    grad_c_in = jnp.zeros((SEQ_LEN, DSTATE), jnp.float32)
    for offset in range(KCONV):
        lag = KCONV - 1 - offset
        grad_c_in = grad_c_in + query_taps[offset][None, :] * extended[lag:lag + SEQ_LEN]
    level_update = level_table + grads / math.sqrt(SEQ_LEN)
    return (ssm_out, grad_c_in, level_update)
```

```python
import math

import jax
import jax.numpy as jnp
from jax import lax
from jax.sharding import PartitionSpec as P


def shifted(value, axis, steps):
    count = lax.axis_size(axis)
    leading, last = (max(0, -steps), min(count, count - steps))
    return lax.ppermute(value, axis, [(source, source + steps) for source in range(leading, last)])


def from_partner(value, axis, distance):
    mask = 2**distance
    pairs = [(source, source ^ mask) for source in range(lax.axis_size(axis))]
    return lax.ppermute(value, axis, pairs)


def upward(value, axis, distance):
    mask = 2**distance
    count = lax.axis_size(axis)
    pairs = [(source, source | mask) for source in range(count) if not source & mask]
    return lax.ppermute(value, axis, pairs)


def all_sum(value, axis):
    for distance in range(lax.axis_size(axis).bit_length() - 1):
        value = value + from_partner(value, axis, distance)
    return value


def contract(form, left, right):
    return jnp.einsum(form, left, right, preferred_element_type=jnp.float32)


def exact(form, left, right):
    return jnp.einsum(form, left, right, precision=lax.Precision.HIGHEST)


def conv_forward(window, conv_weight, conv_bias, length):
    result = jnp.zeros((length, window.shape[1]), jnp.float32) + conv_bias[None, :]
    for offset in range(conv_weight.shape[0]):
        result = (
            result
            + window[offset : offset + length].astype(jnp.float32) * conv_weight[offset][None, :]
        )
    return result


def split_act(preact, heads, head_dim, state_dim):
    length = preact.shape[0]
    inner = heads * head_dim
    x_act = jax.nn.silu(preact[:, :inner]).astype(jnp.bfloat16).reshape(length, heads, head_dim)
    b_key = preact[:, inner : inner + state_dim].astype(jnp.bfloat16)
    c_query = preact[:, inner + state_dim :].astype(jnp.bfloat16)
    return (x_act, b_key, c_query)


def local_group(x_part, b_part, c_part, decay_part, grad_part, weight_zero):
    length = x_part.shape[0]
    state_dim = b_part.shape[1]
    cumul = jnp.cumsum(decay_part, axis=0)
    scores = jnp.dot(c_part, b_part.T, preferred_element_type=jnp.float32)
    causal = (jnp.arange(length)[:, None] >= jnp.arange(length)[None, :])[None]
    across = jnp.transpose(cumul)
    spread = across[:, :, None] - across[:, None, :]
    fading = jnp.where(causal, jnp.exp(jnp.where(causal, spread, 0.0)), 0.0)
    basic = fading * scores[None] / state_dim
    intra = (weight_zero[:, None, None] * basic).astype(jnp.bfloat16)
    y_inner = contract("hts,shp->thp", intra, x_part)
    x_faded = (x_part * jnp.exp(cumul[-1][None, :] - cumul)[:, :, None]).astype(jnp.bfloat16)
    group_state = contract("sn,shp->hnp", b_part, x_faded)
    products = contract("thp,shp->hts", grad_part, x_part)
    grad_weight = (
        jnp.sum(weight_zero[:, None, None] * fading * products, axis=0) / state_dim
    ).astype(jnp.bfloat16)
    grad_inner = jnp.dot(grad_weight, b_part, preferred_element_type=jnp.float32)
    level_zero = jnp.sum(basic * products, axis=(1, 2))
    return (y_inner, group_state, cumul, grad_inner, level_zero)


def combine(block, block_decay, other, other_decay, leading, upper):
    grown = upper[..., None, None]
    found = grown * jnp.exp(leading)[..., None, None] * other
    joined = grown * (other * jnp.exp(block_decay)[..., None, None] + block) + (1.0 - grown) * (
        block * jnp.exp(other_decay)[..., None, None] + other
    )
    return (joined, block_decay + other_decay, leading + upper * other_decay, found)


def local(
    xbc_in, conv_weight, conv_bias, dt_raw, decay_rate, skip, level_table, group_class, cotangent
):
    length = xbc_in.shape[0]
    taps = conv_weight.shape[0]
    heads = dt_raw.shape[1]
    inner = cotangent.shape[1]
    head_dim = inner // heads
    state_dim = (xbc_in.shape[1] - inner) // 2
    classes = level_table.shape[0]
    levels = level_table.shape[1]
    groups = group_class.shape[0]
    group_len = length // groups
    edge_part = shifted(xbc_in[length - taps + 1 :], "seq", 1)
    window = jnp.concatenate([edge_part, xbc_in], axis=0)
    preact = conv_forward(window, conv_weight, conv_bias, length)
    x_act, b_key, c_query = split_act(preact, heads, head_dim, state_dim)
    log_decay = -decay_rate[None, :] * jax.nn.softplus(dt_raw)
    grad_out = cotangent.reshape(length, heads, head_dim)
    picked = (group_class[:, None] == jnp.arange(classes, dtype=jnp.int32)[None, :]).astype(
        jnp.float32
    )
    weight_rows = exact("gk,klh->glh", picked, level_table)
    x_groups = x_act.reshape(groups, group_len, heads, head_dim)
    c_groups = c_query.reshape(groups, group_len, state_dim)
    grad_groups = grad_out.reshape(groups, group_len, heads, head_dim)
    y_inner, states, cumuls, grad_inner, level_zero = jax.vmap(local_group)(
        x_groups,
        b_key.reshape(groups, group_len, state_dim),
        c_groups,
        log_decay.reshape(groups, group_len, heads),
        grad_groups,
        weight_rows[:, 0],
    )
    totals = cumuls[:, -1]
    dev_decay = jnp.sum(totals, axis=0)
    later = dev_decay[None, :] - jnp.cumsum(totals, axis=0)
    dev_state = jnp.sum(jnp.exp(later)[:, :, None, None] * states, axis=0)
    devices = lax.axis_size("seq")
    depth = devices.bit_length() - 1
    myself = lax.axis_index("seq")
    block, block_decay = (dev_state, dev_decay)
    leading = jnp.zeros_like(dev_decay)
    found_all = []
    for bit_pos in range(depth):
        if bit_pos == depth - 1:
            sent = upward(block.astype(jnp.bfloat16), "seq", bit_pos)
            other, other_decay = (sent.astype(jnp.float32), jnp.zeros_like(block_decay))
        else:
            sent, other_decay = from_partner((block.astype(jnp.bfloat16), block_decay), "seq", bit_pos)
            other = sent.astype(jnp.float32)
        upper = jnp.zeros_like(dev_decay) + (jnp.right_shift(myself, bit_pos) & 1).astype(
            jnp.float32
        )
        block, block_decay, leading, found = combine(
            block, block_decay, other, other_decay, leading, upper
        )
        found_all.append(found)
    cross = jnp.stack(found_all, axis=0)
    low_levels = groups.bit_length() - 1
    local_ids = jnp.arange(groups, dtype=jnp.int32)
    differ = jnp.bitwise_xor(local_ids[:, None], local_ids[None, :])
    lower = local_ids[:, None] > local_ids[None, :]
    slot_of = jnp.zeros((groups, groups), jnp.int32)
    onehot = (
        (slot_of[:, :, None] == jnp.arange(low_levels, dtype=jnp.int32)[None, None, :])
        & lower[:, :, None]
    ).astype(jnp.float32)
    before = jnp.cumsum(totals, axis=0) - totals
    gap = before[:, None, :] - before[None, :, :] - totals[None, :, :]
    below = lower[:, :, None]
    fade_pairs = jnp.where(below, jnp.exp(jnp.where(below, gap, 0.0)), 0.0)
    local_weight = exact("cds,csh->cdh", onehot, weight_rows[:, 1 : 1 + low_levels]) * fade_pairs
    lead_fade = jnp.exp(before)
    cross_weight = weight_rows[:, 1 + low_levels : 1 + low_levels + depth] * lead_fade[:, None, :]
    terms = [local_weight[:, d, :, None, None] * states[d][None] for d in range(groups)]
    terms += [cross_weight[:, l, :, None, None] * cross[l][None] for l in range(depth)]
    mixed = sum(terms[1:], terms[0]).astype(jnp.bfloat16)
    scaled = jnp.exp(cumuls) / state_dim
    query_faded = (c_groups[:, :, None, :] * scaled[:, :, :, None]).astype(jnp.bfloat16)
    y_cross = contract("cthn,chnp->cthp", query_faded, mixed)
    backed = contract("chnp,cthp->cthn", mixed, grad_groups)
    grad_cross = jnp.sum(backed * scaled[:, :, :, None], axis=2)
    gram = contract("cthn,cthp->chnp", query_faded, grad_groups)
    inner_pairs = jnp.sum(states[None] * gram[:, None], axis=(3, 4))
    level_local = exact("cds,cdh->csh", onehot, fade_pairs * inner_pairs)
    level_cross = lead_fade[:, None, :] * jnp.sum(cross[None] * gram[:, None], axis=(3, 4))
    level_rest = jnp.concatenate(
        [
            level_local,
            level_cross,
            jnp.zeros((groups, levels - 1 - low_levels - depth, heads), jnp.float32),
        ],
        axis=1,
    )
    grads = exact("ck,clh->klh", picked, level_rest)
    ssm_out = (
        (y_inner + y_cross + skip[None, None, :, None] * x_groups)
        .astype(jnp.bfloat16)
        .reshape(length, inner)
    )
    grad_query = (grad_inner + grad_cross).reshape(length, state_dim)
    after_rows = shifted(grad_query[: taps - 1], "seq", -1)
    extended = jnp.concatenate([grad_query, after_rows], axis=0)
    query_taps = conv_weight[:, inner + state_dim :]
    grad_c_in = jnp.zeros((length, state_dim), jnp.float32)
    for offset in range(taps):
        lagged = taps - 1 - offset
        grad_c_in = grad_c_in + query_taps[offset][None, :] * extended[lagged : lagged + length]
    grad_first = exact("gk,gh->kh", picked, level_zero)
    local_grads = jnp.concatenate([grad_first[:, None, :], grads], axis=1)
    summed = all_sum(local_grads, "seq")
    level_update = level_table + summed / math.sqrt(length * devices)
    return (ssm_out, grad_c_in, level_update)


def solution(mesh):
    placed = (
        P(("grp", "seq"), None),
        P(),
        P(),
        P(("grp", "seq"), None),
        P(),
        P(),
        P(),
        P(("grp", "seq")),
        P(("grp", "seq"), None),
    )
    return jax.shard_map(
        local,
        mesh=mesh,
        in_specs=placed,
        out_specs=(P(("grp", "seq"), None), P(("grp", "seq"), None), P("grp", None, None)),
        check_vma=False,
    )
```

```python
import math

import jax
import jax.numpy as jnp
from jax import lax
from jax.sharding import PartitionSpec as P


def shifted(value, axis, steps):
    count = lax.axis_size(axis)
    leading, last = (max(0, -steps), min(count, count - steps))
    return lax.ppermute(value, axis, [(source, source + steps) for source in range(leading, last)])


def from_partner(value, axis, distance):
    mask = 2**distance
    pairs = [(source, source ^ mask) for source in range(lax.axis_size(axis))]
    return lax.ppermute(value, axis, pairs)


def upward(value, axis, distance):
    mask = 2**distance
    count = lax.axis_size(axis)
    pairs = [(source, source | mask) for source in range(count) if not source & mask]
    return lax.ppermute(value, axis, pairs)


def all_sum(value, axis):
    for distance in range(lax.axis_size(axis).bit_length() - 1):
        value = value + from_partner(value, axis, distance)
    return value


def contract(form, left, right):
    return jnp.einsum(form, left, right, preferred_element_type=jnp.float32)


def exact(form, left, right):
    return jnp.einsum(form, left, right, precision=lax.Precision.HIGHEST)


def conv_forward(window, conv_weight, conv_bias, length):
    result = jnp.zeros((length, window.shape[1]), jnp.float32) + conv_bias[None, :]
    for offset in range(conv_weight.shape[0]):
        result = (
            result
            + window[offset : offset + length].astype(jnp.float32) * conv_weight[offset][None, :]
        )
    return result


def split_act(preact, heads, head_dim, state_dim):
    length = preact.shape[0]
    inner = heads * head_dim
    x_act = jax.nn.silu(preact[:, :inner]).astype(jnp.bfloat16).reshape(length, heads, head_dim)
    b_key = preact[:, inner : inner + state_dim].astype(jnp.bfloat16)
    c_query = preact[:, inner + state_dim :].astype(jnp.bfloat16)
    return (x_act, b_key, c_query)


def local_group(x_part, b_part, c_part, decay_part, grad_part, weight_zero):
    length = x_part.shape[0]
    state_dim = b_part.shape[1]
    cumul = jnp.cumsum(decay_part, axis=0)
    scores = jnp.dot(c_part, b_part.T, preferred_element_type=jnp.float32)
    causal = (jnp.arange(length)[:, None] >= jnp.arange(length)[None, :])[None]
    across = jnp.transpose(cumul)
    spread = across[:, :, None] - across[:, None, :]
    fading = jnp.where(causal, jnp.exp(jnp.where(causal, spread, 0.0)), 0.0)
    basic = fading * scores[None] / state_dim
    intra = (weight_zero[:, None, None] * basic).astype(jnp.bfloat16)
    y_inner = contract("hts,shp->thp", intra, x_part)
    products = contract("thp,shp->hts", grad_part, x_part)
    grad_weight = (
        jnp.sum(weight_zero[:, None, None] * fading * products, axis=0) / state_dim
    ).astype(jnp.bfloat16)
    grad_inner = jnp.dot(grad_weight, b_part, preferred_element_type=jnp.float32)
    level_zero = jnp.sum(basic * products, axis=(1, 2))
    return (y_inner, cumul, grad_inner, level_zero)


def combine(block, block_decay, other, other_decay, leading, upper, head_dim):
    grown = upper
    found = grown * lanes(jnp.exp(leading), head_dim) * other
    joined = grown * (other * lanes(jnp.exp(block_decay), head_dim) + block) + (1.0 - grown) * (
        block * lanes(jnp.exp(other_decay), head_dim) + other
    )
    return (joined, block_decay + other_decay, leading + upper * other_decay, found)


def lanes(per_head, head_dim):
    return jnp.repeat(per_head, head_dim, axis=-1)


def per_head(value, head_dim):
    return jnp.sum(value.reshape(value.shape[:-1] + (-1, head_dim)), axis=-1)


def local(
    xbc_in, conv_weight, conv_bias, dt_raw, decay_rate, skip, level_table, group_class, cotangent
):
    length = xbc_in.shape[0]
    taps = conv_weight.shape[0]
    heads = dt_raw.shape[1]
    inner = cotangent.shape[1]
    head_dim = inner // heads
    state_dim = (xbc_in.shape[1] - inner) // 2
    classes = level_table.shape[0]
    levels = level_table.shape[1]
    groups = group_class.shape[0]
    group_len = length // groups
    edge_part = shifted(xbc_in[length - taps + 1 :], "seq", 1)
    window = jnp.concatenate([edge_part, xbc_in], axis=0)
    preact = conv_forward(window, conv_weight, conv_bias, length)
    x_act, b_key, c_query = split_act(preact, heads, head_dim, state_dim)
    log_decay = -decay_rate[None, :] * jax.nn.softplus(dt_raw)
    grad_out = cotangent.reshape(length, heads, head_dim)
    picked = (group_class[:, None] == jnp.arange(classes, dtype=jnp.int32)[None, :]).astype(
        jnp.float32
    )
    weight_rows = exact("gk,klh->glh", picked, level_table)
    x_groups = x_act.reshape(groups, group_len, heads, head_dim)
    c_groups = c_query.reshape(groups, group_len, state_dim)
    grad_groups = grad_out.reshape(groups, group_len, heads, head_dim)
    y_inner, cumuls, grad_inner, level_zero = jax.vmap(local_group)(
        x_groups,
        b_key.reshape(groups, group_len, state_dim),
        c_groups,
        log_decay.reshape(groups, group_len, heads),
        grad_groups,
        weight_rows[:, 0],
    )
    x_flat = x_act.reshape(groups, group_len, inner)
    b_groups = b_key.reshape(groups, group_len, state_dim)
    g_flat = cotangent.reshape(groups, group_len, inner)
    ending = lanes(jnp.exp(cumuls[:, -1:, :] - cumuls), head_dim)
    x_faded = (x_flat * ending).astype(jnp.bfloat16)
    states = contract("gtn,gtq->gnq", b_groups, x_faded)
    totals = cumuls[:, -1]
    dev_decay = jnp.sum(totals, axis=0)
    later = dev_decay[None, :] - jnp.cumsum(totals, axis=0)
    dev_state = jnp.sum(lanes(jnp.exp(later), head_dim)[:, None, :] * states, axis=0)
    devices = lax.axis_size("seq")
    depth = devices.bit_length() - 1
    myself = lax.axis_index("seq")
    block, block_decay = (dev_state, dev_decay)
    leading = jnp.zeros_like(dev_decay)
    found_all = []
    for bit_pos in range(depth):
        if bit_pos == depth - 1:
            sent = upward(block.astype(jnp.bfloat16), "seq", bit_pos)
            other, other_decay = (sent.astype(jnp.float32), jnp.zeros_like(block_decay))
        else:
            sent, other_decay = from_partner((block.astype(jnp.bfloat16), block_decay), "seq", bit_pos)
            other = sent.astype(jnp.float32)
        upper = (jnp.right_shift(myself, bit_pos) & 1).astype(jnp.float32)
        block, block_decay, leading, found = combine(
            block, block_decay, other, other_decay, leading, upper, head_dim
        )
        found_all.append(found)
    cross = jnp.stack(found_all, axis=0)
    low_levels = groups.bit_length() - 1
    local_ids = jnp.arange(groups, dtype=jnp.int32)
    differ = jnp.bitwise_xor(local_ids[:, None], local_ids[None, :])
    lower = local_ids[:, None] > local_ids[None, :]
    slot_of = jnp.zeros((groups, groups), jnp.int32)
    onehot = (
        (slot_of[:, :, None] == jnp.arange(low_levels, dtype=jnp.int32)[None, None, :])
        & lower[:, :, None]
    ).astype(jnp.float32)
    before = jnp.cumsum(totals, axis=0) - totals
    gap = before[:, None, :] - before[None, :, :] - totals[None, :, :]
    below = lower[:, :, None]
    fade_pairs = jnp.where(below, jnp.exp(jnp.where(below, gap, 0.0)), 0.0)
    local_weight = exact("cds,csh->cdh", onehot, weight_rows[:, 1 : 1 + low_levels]) * fade_pairs
    lead_fade = jnp.exp(before)
    cross_weight = weight_rows[:, 1 + low_levels : 1 + low_levels + depth] * lead_fade[:, None, :]
    terms = [lanes(local_weight[:, d], head_dim)[:, None, :] * states[d][None] for d in range(groups)]
    terms += [lanes(cross_weight[:, l], head_dim)[:, None, :] * cross[l][None] for l in range(depth)]
    mixed = sum(terms[1:], terms[0]).astype(jnp.bfloat16)
    scaled = lanes(jnp.exp(cumuls) / state_dim, head_dim)
    y_cross = scaled * contract("ctn,cnq->ctq", c_groups, mixed)
    grad_scaled = scaled * g_flat
    grad_cross = exact("ctq,cnq->ctn", grad_scaled, mixed.astype(jnp.float32))
    gram = exact("ctn,ctq->cnq", c_groups.astype(jnp.float32), grad_scaled)
    inner_pairs = jnp.stack(
        [jnp.stack([per_head(jnp.sum(states[d] * gram[c], axis=0), head_dim) for d in range(groups)]) for c in range(groups)]
    )
    cross_pairs = jnp.stack(
        [jnp.stack([per_head(jnp.sum(cross[l] * gram[c], axis=0), head_dim) for l in range(depth)]) for c in range(groups)]
    )
    level_local = exact("cds,cdh->csh", onehot, fade_pairs * inner_pairs)
    level_cross = lead_fade[:, None, :] * cross_pairs
    level_rest = jnp.concatenate(
        [
            level_local,
            level_cross,
            jnp.zeros((groups, levels - 1 - low_levels - depth, heads), jnp.float32),
        ],
        axis=1,
    )
    grads = exact("ck,clh->klh", picked, level_rest)
    ssm_out = (
        (y_inner.reshape(groups, group_len, inner) + y_cross + lanes(skip, head_dim) * x_flat)
        .astype(jnp.bfloat16)
        .reshape(length, inner)
    )
    grad_query = (grad_inner + grad_cross).reshape(length, state_dim)
    after_rows = shifted(grad_query[: taps - 1], "seq", -1)
    extended = jnp.concatenate([grad_query, after_rows], axis=0)
    query_taps = conv_weight[:, inner + state_dim :]
    grad_c_in = jnp.zeros((length, state_dim), jnp.float32)
    for offset in range(taps):
        lagged = taps - 1 - offset
        grad_c_in = grad_c_in + query_taps[offset][None, :] * extended[lagged : lagged + length]
    grad_first = exact("gk,gh->kh", picked, level_zero)
    local_grads = jnp.concatenate([grad_first[:, None, :], grads], axis=1)
    summed = all_sum(local_grads, "seq")
    level_update = level_table + summed / math.sqrt(length * devices)
    return (ssm_out, grad_c_in, level_update)


def solution(mesh):
    placed = (
        P(("grp", "seq"), None),
        P(),
        P(),
        P(("grp", "seq"), None),
        P(),
        P(),
        P(),
        P(("grp", "seq")),
        P(("grp", "seq"), None),
    )
    return jax.shard_map(
        local,
        mesh=mesh,
        in_specs=placed,
        out_specs=(P(("grp", "seq"), None), P(("grp", "seq"), None), P("grp", None, None)),
        check_vma=False,
    )
```

```python
import math

import jax
import jax.numpy as jnp
from jax import lax
from jax.sharding import PartitionSpec as P


def shifted(value, axis, steps):
    count = lax.axis_size(axis)
    leading, last = (max(0, -steps), min(count, count - steps))
    return lax.ppermute(value, axis, [(source, source + steps) for source in range(leading, last)])


def from_partner(value, axis, distance):
    mask = 2**distance
    pairs = [(source, source ^ mask) for source in range(lax.axis_size(axis))]
    return lax.ppermute(value, axis, pairs)


def upward(value, axis, distance):
    mask = 2**distance
    count = lax.axis_size(axis)
    pairs = [(source, source | mask) for source in range(count) if not source & mask]
    return lax.ppermute(value, axis, pairs)


def all_sum(value, axis):
    for distance in range(lax.axis_size(axis).bit_length() - 1):
        value = value + from_partner(value, axis, distance)
    return value


def contract(form, left, right):
    return jnp.einsum(form, left, right, preferred_element_type=jnp.float32)


def exact(form, left, right):
    return jnp.einsum(form, left, right, precision=lax.Precision.HIGHEST)


def conv_forward(window, conv_weight, conv_bias, length):
    result = jnp.zeros((length, window.shape[1]), jnp.float32) + conv_bias[None, :]
    for offset in range(conv_weight.shape[0]):
        result = (
            result
            + window[offset : offset + length].astype(jnp.float32) * conv_weight[offset][None, :]
        )
    return result


def split_act(preact, heads, head_dim, state_dim):
    length = preact.shape[0]
    inner = heads * head_dim
    x_act = jax.nn.silu(preact[:, :inner]).astype(jnp.bfloat16).reshape(length, heads, head_dim)
    b_key = preact[:, inner : inner + state_dim].astype(jnp.bfloat16)
    c_query = preact[:, inner + state_dim :].astype(jnp.bfloat16)
    return (x_act, b_key, c_query)


def local_group(x_part, b_part, c_part, decay_part, grad_part, weight_zero):
    length = x_part.shape[0]
    state_dim = b_part.shape[1]
    cumul = jnp.cumsum(decay_part, axis=0)
    scores = jnp.dot(c_part, b_part.T, preferred_element_type=jnp.float32)
    causal = (jnp.arange(length)[:, None] >= jnp.arange(length)[None, :])[None]
    across = jnp.transpose(cumul)
    spread = across[:, :, None] - across[:, None, :]
    fading = jnp.where(causal, jnp.exp(jnp.where(causal, spread, 0.0)), 0.0)
    basic = fading * scores[None] / state_dim
    intra = (weight_zero[:, None, None] * basic).astype(jnp.bfloat16)
    y_inner = contract("hts,shp->thp", intra, x_part)
    x_faded = (x_part * jnp.exp(cumul[-1][None, :] - cumul)[:, :, None]).astype(jnp.bfloat16)
    group_state = contract("sn,shp->hnp", b_part, x_faded)
    products = contract("thp,shp->hts", grad_part, x_part)
    grad_weight = (
        jnp.sum(weight_zero[:, None, None] * fading * products, axis=0) / state_dim
    ).astype(jnp.bfloat16)
    grad_inner = jnp.dot(grad_weight, b_part, preferred_element_type=jnp.float32)
    level_zero = jnp.sum(basic * products, axis=(1, 2))
    return (y_inner, group_state, cumul, grad_inner, level_zero)


def combine(block, block_decay, other, other_decay, leading, upper):
    grown = upper[..., None, None]
    found = grown * jnp.exp(leading)[..., None, None] * other
    joined = grown * (other * jnp.exp(block_decay)[..., None, None] + block) + (1.0 - grown) * (
        block * jnp.exp(other_decay)[..., None, None] + other
    )
    return (joined, block_decay + other_decay, leading + upper * other_decay, found)


def local(
    xbc_in, conv_weight, conv_bias, dt_raw, decay_rate, skip, level_table, group_class, cotangent
):
    length = xbc_in.shape[0]
    taps = conv_weight.shape[0]
    heads = dt_raw.shape[1]
    inner = cotangent.shape[1]
    head_dim = inner // heads
    state_dim = (xbc_in.shape[1] - inner) // 2
    classes = level_table.shape[0]
    levels = level_table.shape[1]
    groups = group_class.shape[0]
    group_len = length // groups
    edge_part = shifted(xbc_in[length - taps + 1 :], "seq", 1)
    window = jnp.concatenate([edge_part, xbc_in], axis=0)
    preact = conv_forward(window, conv_weight, conv_bias, length)
    x_act, b_key, c_query = split_act(preact, heads, head_dim, state_dim)
    log_decay = -decay_rate[None, :] * jax.nn.softplus(dt_raw)
    grad_out = cotangent.reshape(length, heads, head_dim)
    picked = (group_class[:, None] == jnp.arange(classes, dtype=jnp.int32)[None, :]).astype(
        jnp.float32
    )
    weight_rows = exact("gk,klh->glh", picked, level_table)
    x_groups = x_act.reshape(groups, group_len, heads, head_dim)
    c_groups = c_query.reshape(groups, group_len, state_dim)
    grad_groups = grad_out.reshape(groups, group_len, heads, head_dim)
    y_inner, states, cumuls, grad_inner, level_zero = jax.vmap(local_group)(
        x_groups,
        b_key.reshape(groups, group_len, state_dim),
        c_groups,
        log_decay.reshape(groups, group_len, heads),
        grad_groups,
        weight_rows[:, 0],
    )
    totals = cumuls[:, -1]
    dev_decay = jnp.sum(totals, axis=0)
    later = dev_decay[None, :] - jnp.cumsum(totals, axis=0)
    dev_state = jnp.sum(jnp.exp(later)[:, :, None, None] * states, axis=0)
    devices = lax.axis_size("seq")
    depth = devices.bit_length() - 1
    myself = lax.axis_index("seq")
    block, block_decay = (dev_state, dev_decay)
    leading = jnp.zeros_like(dev_decay)
    found_all = []
    for bit_pos in range(depth):
        if bit_pos == depth - 1:
            sent = upward(block.astype(jnp.bfloat16), "seq", bit_pos)
            other, other_decay = (sent.astype(jnp.float32), jnp.zeros_like(block_decay))
        else:
            sent, other_decay = from_partner((block.astype(jnp.bfloat16), block_decay), "seq", bit_pos)
            other = sent.astype(jnp.float32)
        upper = jnp.zeros_like(dev_decay) + (jnp.right_shift(myself, bit_pos) & 1).astype(
            jnp.float32
        )
        block, block_decay, leading, found = combine(
            block, block_decay, other, other_decay, leading, upper
        )
        found_all.append(found)
    cross = jnp.stack(found_all, axis=0)
    low_levels = groups.bit_length() - 1
    local_ids = jnp.arange(groups, dtype=jnp.int32)
    differ = jnp.bitwise_xor(local_ids[:, None], local_ids[None, :])
    lower = local_ids[:, None] > local_ids[None, :]
    slot_of = jnp.zeros((groups, groups), jnp.int32)
    onehot = (
        (slot_of[:, :, None] == jnp.arange(low_levels, dtype=jnp.int32)[None, None, :])
        & lower[:, :, None]
    ).astype(jnp.float32)
    before = jnp.cumsum(totals, axis=0) - totals
    gap = before[:, None, :] - before[None, :, :] - totals[None, :, :]
    below = lower[:, :, None]
    fade_pairs = jnp.where(below, jnp.exp(jnp.where(below, gap, 0.0)), 0.0)
    local_weight = exact("cds,csh->cdh", onehot, weight_rows[:, 1 : 1 + low_levels]) * fade_pairs
    lead_fade = jnp.exp(before)
    cross_weight = weight_rows[:, 1 + low_levels : 1 + low_levels + depth] * lead_fade[:, None, :]
    terms = [local_weight[:, d, :, None, None] * states[d][None] for d in range(groups)]
    terms += [cross_weight[:, l, :, None, None] * cross[l][None] for l in range(depth)]
    mixed = sum(terms[1:], terms[0]).astype(jnp.bfloat16)
    scaled = jnp.exp(cumuls) / state_dim
    query_faded = (c_groups[:, :, None, :] * scaled[:, :, :, None]).astype(jnp.bfloat16)
    gram = contract("cthn,cthp->chnp", query_faded, grad_groups)
    inner_pairs = jnp.sum(states[None] * gram[:, None], axis=(3, 4))
    level_local = exact("cds,cdh->csh", onehot, fade_pairs * inner_pairs)
    level_cross = lead_fade[:, None, :] * jnp.sum(cross[None] * gram[:, None], axis=(3, 4))
    level_rest = jnp.concatenate(
        [
            level_local,
            level_cross,
            jnp.zeros((groups, levels - 1 - low_levels - depth, heads), jnp.float32),
        ],
        axis=1,
    )
    grads = exact("ck,clh->klh", picked, level_rest)
    grad_first = exact("gk,gh->kh", picked, level_zero)
    local_grads = jnp.concatenate([grad_first[:, None, :], grads], axis=1)
    summed = all_sum(local_grads, "seq")
    summed, mixed, y_inner, x_groups = lax.optimization_barrier((summed, mixed, y_inner, x_groups))
    y_cross = contract("cthn,chnp->cthp", query_faded, mixed)
    backed = contract("chnp,cthp->cthn", mixed, grad_groups)
    grad_cross = jnp.sum(backed * scaled[:, :, :, None], axis=2)
    ssm_out = (
        (y_inner + y_cross + skip[None, None, :, None] * x_groups)
        .astype(jnp.bfloat16)
        .reshape(length, inner)
    )
    grad_query = (grad_inner + grad_cross).reshape(length, state_dim)
    after_rows = shifted(grad_query[: taps - 1], "seq", -1)
    extended = jnp.concatenate([grad_query, after_rows], axis=0)
    query_taps = conv_weight[:, inner + state_dim :]
    grad_c_in = jnp.zeros((length, state_dim), jnp.float32)
    for offset in range(taps):
        lagged = taps - 1 - offset
        grad_c_in = grad_c_in + query_taps[offset][None, :] * extended[lagged : lagged + length]
    level_update = level_table + summed / math.sqrt(length * devices)
    return (ssm_out, grad_c_in, level_update)


def solution(mesh):
    placed = (
        P(("grp", "seq"), None),
        P(),
        P(),
        P(("grp", "seq"), None),
        P(),
        P(),
        P(),
        P(("grp", "seq")),
        P(("grp", "seq"), None),
    )
    return jax.shard_map(
        local,
        mesh=mesh,
        in_specs=placed,
        out_specs=(P(("grp", "seq"), None), P(("grp", "seq"), None), P("grp", None, None)),
        check_vma=False,
    )
```

```python
import math

import jax
import jax.numpy as jnp
from jax import lax
from jax.sharding import PartitionSpec as P


def shifted(value, axis, steps):
    count = lax.axis_size(axis)
    leading, last = (max(0, -steps), min(count, count - steps))
    return lax.ppermute(value, axis, [(source, source + steps) for source in range(leading, last)])


def from_partner(value, axis, distance):
    mask = 2**distance
    pairs = [(source, source ^ mask) for source in range(lax.axis_size(axis))]
    return lax.ppermute(value, axis, pairs)


def upward(value, axis, distance):
    mask = 2**distance
    count = lax.axis_size(axis)
    pairs = [(source, source | mask) for source in range(count) if not source & mask]
    return lax.ppermute(value, axis, pairs)


def all_sum(value, axis):
    for distance in range(lax.axis_size(axis).bit_length() - 1):
        value = value + from_partner(value, axis, distance)
    return value


def contract(form, left, right):
    return jnp.einsum(form, left, right, preferred_element_type=jnp.float32)


def exact(form, left, right):
    return jnp.einsum(form, left, right, precision=lax.Precision.HIGHEST)


def conv_forward(window, conv_weight, conv_bias, length):
    result = jnp.zeros((length, window.shape[1]), jnp.float32) + conv_bias[None, :]
    for offset in range(conv_weight.shape[0]):
        result = (
            result
            + window[offset : offset + length].astype(jnp.float32) * conv_weight[offset][None, :]
        )
    return result


def split_act(preact, heads, head_dim, state_dim):
    length = preact.shape[0]
    inner = heads * head_dim
    x_act = jax.nn.silu(preact[:, :inner]).astype(jnp.bfloat16).reshape(length, heads, head_dim)
    b_key = preact[:, inner : inner + state_dim].astype(jnp.bfloat16)
    c_query = preact[:, inner + state_dim :].astype(jnp.bfloat16)
    return (x_act, b_key, c_query)


def local_group(x_part, b_part, c_part, decay_part, grad_part, weight_zero):
    length = x_part.shape[0]
    state_dim = b_part.shape[1]
    cumul = jnp.cumsum(decay_part, axis=0)
    scores = jnp.dot(c_part, b_part.T, preferred_element_type=jnp.float32)
    causal = (jnp.arange(length)[:, None] >= jnp.arange(length)[None, :])[None]
    across = jnp.transpose(cumul)
    spread = across[:, :, None] - across[:, None, :]
    fading = jnp.where(causal, jnp.exp(jnp.where(causal, spread, 0.0)), 0.0)
    basic = fading * scores[None] / state_dim
    intra = (weight_zero[:, None, None] * basic).astype(jnp.bfloat16)
    y_inner = contract("hts,shp->thp", intra, x_part)
    x_faded = (x_part * jnp.exp(cumul[-1][None, :] - cumul)[:, :, None]).astype(jnp.bfloat16)
    group_state = contract("sn,shp->hnp", b_part, x_faded)
    products = contract("thp,shp->hts", grad_part, x_part)
    grad_weight = (
        jnp.sum(weight_zero[:, None, None] * fading * products, axis=0) / state_dim
    ).astype(jnp.bfloat16)
    grad_inner = jnp.dot(grad_weight, b_part, preferred_element_type=jnp.float32)
    level_zero = jnp.sum(basic * products, axis=(1, 2))
    return (y_inner, group_state, cumul, grad_inner, level_zero)


def combine(block, block_decay, other, other_decay, leading, upper):
    grown = upper[..., None, None]
    found = grown * jnp.exp(leading)[..., None, None] * other
    joined = grown * (other * jnp.exp(block_decay)[..., None, None] + block) + (1.0 - grown) * (
        block * jnp.exp(other_decay)[..., None, None] + other
    )
    return (joined, block_decay + other_decay, leading + upper * other_decay, found)


def local(
    xbc_in, conv_weight, conv_bias, dt_raw, decay_rate, skip, level_table, group_class, cotangent
):
    length = xbc_in.shape[0]
    taps = conv_weight.shape[0]
    heads = dt_raw.shape[1]
    inner = cotangent.shape[1]
    head_dim = inner // heads
    state_dim = (xbc_in.shape[1] - inner) // 2
    classes = level_table.shape[0]
    levels = level_table.shape[1]
    groups = group_class.shape[0]
    group_len = length // groups
    edge_part = shifted(xbc_in[length - taps + 1 :], "seq", 1)
    window = jnp.concatenate([edge_part, xbc_in], axis=0)
    preact = conv_forward(window, conv_weight, conv_bias, length)
    x_act, b_key, c_query = split_act(preact, heads, head_dim, state_dim)
    log_decay = -decay_rate[None, :] * jax.nn.softplus(dt_raw)
    grad_out = cotangent.reshape(length, heads, head_dim)
    picked = (group_class[:, None] == jnp.arange(classes, dtype=jnp.int32)[None, :]).astype(
        jnp.float32
    )
    weight_rows = exact("gk,klh->glh", picked, level_table)
    x_groups = x_act.reshape(groups, group_len, heads, head_dim)
    c_groups = c_query.reshape(groups, group_len, state_dim)
    grad_groups = grad_out.reshape(groups, group_len, heads, head_dim)
    y_inner, states, cumuls, grad_inner, level_zero = jax.vmap(local_group)(
        x_groups,
        b_key.reshape(groups, group_len, state_dim),
        c_groups,
        log_decay.reshape(groups, group_len, heads),
        grad_groups,
        weight_rows[:, 0],
    )
    totals = cumuls[:, -1]
    dev_decay = jnp.sum(totals, axis=0)
    later = dev_decay[None, :] - jnp.cumsum(totals, axis=0)
    dev_state = jnp.sum(jnp.exp(later)[:, :, None, None] * states, axis=0)
    devices = lax.axis_size("seq")
    depth = devices.bit_length() - 1
    myself = lax.axis_index("seq")
    block, block_decay = (dev_state, dev_decay)
    leading = jnp.zeros_like(dev_decay)
    found_all = []
    for bit_pos in range(depth):
        if bit_pos == depth - 1:
            sent = upward(block.astype(jnp.bfloat16), "seq", bit_pos)
            other, other_decay = (sent.astype(jnp.float32), jnp.zeros_like(block_decay))
        else:
            sent, other_decay = from_partner((block.astype(jnp.bfloat16), block_decay), "seq", bit_pos)
            other = sent.astype(jnp.float32)
        upper = jnp.zeros_like(dev_decay) + (jnp.right_shift(myself, bit_pos) & 1).astype(
            jnp.float32
        )
        block, block_decay, leading, found = combine(
            block, block_decay, other, other_decay, leading, upper
        )
        found_all.append(found)
    cross = jnp.stack(found_all, axis=0)
    low_levels = groups.bit_length() - 1
    local_ids = jnp.arange(groups, dtype=jnp.int32)
    differ = jnp.bitwise_xor(local_ids[:, None], local_ids[None, :])
    lower = local_ids[:, None] > local_ids[None, :]
    slot_of = jnp.zeros((groups, groups), jnp.int32)
    onehot = (
        (slot_of[:, :, None] == jnp.arange(low_levels, dtype=jnp.int32)[None, None, :])
        & lower[:, :, None]
    ).astype(jnp.float32)
    before = jnp.cumsum(totals, axis=0) - totals
    gap = before[:, None, :] - before[None, :, :] - totals[None, :, :]
    below = lower[:, :, None]
    fade_pairs = jnp.where(below, jnp.exp(jnp.where(below, gap, 0.0)), 0.0)
    local_weight = exact("cds,csh->cdh", onehot, weight_rows[:, 1 : 1 + low_levels]) * fade_pairs
    lead_fade = jnp.exp(before)
    cross_weight = weight_rows[:, 1 + low_levels : 1 + low_levels + depth] * lead_fade[:, None, :]
    terms = [local_weight[:, d, :, None, None] * states[d][None] for d in range(groups)]
    terms += [cross_weight[:, l, :, None, None] * cross[l][None] for l in range(depth)]
    mixed = sum(terms[1:], terms[0]).astype(jnp.bfloat16)
    scaled = jnp.exp(cumuls) / state_dim
    query_faded = (c_groups[:, :, None, :] * scaled[:, :, :, None]).astype(jnp.bfloat16)
    y_cross = contract("cthn,chnp->cthp", query_faded, mixed)
    backed = contract("chnp,cthp->cthn", mixed, grad_groups)
    grad_cross = jnp.sum(backed * scaled[:, :, :, None], axis=2)
    gram = contract("cthn,cthp->chnp", query_faded, grad_groups)
    inner_pairs = jnp.sum(states[None] * gram[:, None], axis=(3, 4))
    level_local = exact("cds,cdh->csh", onehot, fade_pairs * inner_pairs)
    level_cross = lead_fade[:, None, :] * jnp.sum(cross[None] * gram[:, None], axis=(3, 4))
    level_rest = jnp.concatenate(
        [
            level_local,
            level_cross,
            jnp.zeros((groups, levels - 1 - low_levels - depth, heads), jnp.float32),
        ],
        axis=1,
    )
    grads = exact("ck,clh->klh", picked, level_rest)
    ssm_out = (
        (y_inner + y_cross + skip[None, None, :, None] * x_groups)
        .astype(jnp.bfloat16)
        .reshape(length, inner)
    )
    grad_query = (grad_inner + grad_cross).reshape(length, state_dim)
    after_rows = shifted(grad_query[: taps - 1], "seq", -1)
    extended = jnp.concatenate([grad_query, after_rows], axis=0)
    query_taps = conv_weight[:, inner + state_dim :]
    grad_c_in = jnp.zeros((length, state_dim), jnp.float32)
    for offset in range(taps):
        lagged = taps - 1 - offset
        grad_c_in = grad_c_in + query_taps[offset][None, :] * extended[lagged : lagged + length]
    grad_first = exact("gk,gh->kh", picked, level_zero)
    local_grads = jnp.concatenate([grad_first[:, None, :], grads], axis=1)
    local_grads, ssm_out, grad_c_in = lax.optimization_barrier((local_grads, ssm_out, grad_c_in))
    summed = all_sum(local_grads, "seq")
    level_update = level_table + summed / math.sqrt(length * devices)
    return (ssm_out, grad_c_in, level_update)


def solution(mesh):
    placed = (
        P(("grp", "seq"), None),
        P(),
        P(),
        P(("grp", "seq"), None),
        P(),
        P(),
        P(),
        P(("grp", "seq")),
        P(("grp", "seq"), None),
    )
    return jax.shard_map(
        local,
        mesh=mesh,
        in_specs=placed,
        out_specs=(P(("grp", "seq"), None), P(("grp", "seq"), None), P("grp", None, None)),
        check_vma=False,
    )
```

```python
import math

import jax
import jax.numpy as jnp
from jax import lax
from jax.sharding import PartitionSpec as P


def shifted(value, axis, steps):
    count = lax.axis_size(axis)
    leading, last = (max(0, -steps), min(count, count - steps))
    return lax.ppermute(value, axis, [(source, source + steps) for source in range(leading, last)])


def from_partner(value, axis, distance):
    mask = 2**distance
    pairs = [(source, source ^ mask) for source in range(lax.axis_size(axis))]
    return lax.ppermute(value, axis, pairs)


def upward(value, axis, distance):
    mask = 2**distance
    count = lax.axis_size(axis)
    pairs = [(source, source | mask) for source in range(count) if not source & mask]
    return lax.ppermute(value, axis, pairs)


def all_sum(value, axis):
    for distance in range(lax.axis_size(axis).bit_length() - 1):
        value = value + from_partner(value, axis, distance)
    return value


def contract(form, left, right):
    return jnp.einsum(form, left, right, preferred_element_type=jnp.float32)


def exact(form, left, right):
    return jnp.einsum(form, left, right, precision=lax.Precision.HIGHEST)


def conv_forward(window, conv_weight, conv_bias, length):
    result = jnp.zeros((length, window.shape[1]), jnp.float32) + conv_bias[None, :]
    for offset in range(conv_weight.shape[0]):
        result = (
            result
            + window[offset : offset + length].astype(jnp.float32) * conv_weight[offset][None, :]
        )
    return result


def split_act(preact, heads, head_dim, state_dim):
    length = preact.shape[0]
    inner = heads * head_dim
    x_act = jax.nn.silu(preact[:, :inner]).astype(jnp.bfloat16).reshape(length, heads, head_dim)
    b_key = preact[:, inner : inner + state_dim].astype(jnp.bfloat16)
    c_query = preact[:, inner + state_dim :].astype(jnp.bfloat16)
    return (x_act, b_key, c_query)


def local_group(x_part, b_part, c_part, decay_part, grad_part, weight_zero):
    length = x_part.shape[0]
    state_dim = b_part.shape[1]
    cumul = jnp.cumsum(decay_part, axis=0)
    scores = jnp.dot(c_part, b_part.T, preferred_element_type=jnp.float32)
    causal = (jnp.arange(length)[:, None] >= jnp.arange(length)[None, :])[None]
    across = jnp.transpose(cumul)
    spread = across[:, :, None] - across[:, None, :]
    fading = jnp.where(causal, jnp.exp(jnp.where(causal, spread, 0.0)), 0.0)
    basic = fading * scores[None] / state_dim
    intra = (weight_zero[:, None, None] * basic).astype(jnp.bfloat16)
    y_inner = contract("hts,shp->thp", intra, x_part)
    x_faded = (x_part * jnp.exp(cumul[-1][None, :] - cumul)[:, :, None]).astype(jnp.bfloat16)
    group_state = contract("sn,shp->hnp", b_part, x_faded)
    products = contract("thp,shp->hts", grad_part, x_part)
    grad_weight = (
        jnp.sum(weight_zero[:, None, None] * fading * products, axis=0) / state_dim
    ).astype(jnp.bfloat16)
    grad_inner = jnp.dot(grad_weight, b_part, preferred_element_type=jnp.float32)
    level_zero = jnp.sum(basic * products, axis=(1, 2))
    return (y_inner, group_state, cumul, grad_inner, level_zero)


def combine(block, block_decay, other, other_decay, leading, upper):
    grown = upper[..., None, None]
    found = grown * jnp.exp(leading)[..., None, None] * other
    joined = grown * (other * jnp.exp(block_decay)[..., None, None] + block) + (1.0 - grown) * (
        block * jnp.exp(other_decay)[..., None, None] + other
    )
    return (joined, block_decay + other_decay, leading + upper * other_decay, found)


def relay(value, axis, bit_pos):
    half = 2**bit_pos
    step = half // 2
    first = lax.ppermute(value, axis, [(source, source + step) for source in range(half - step, half)])
    second = lax.ppermute(first, axis, [(source, source + step) for source in range(half, half + step)])
    return first + second


def exchange(block, block_decay, depth, myself):
    leading = jnp.zeros_like(block_decay)
    found_all = []
    for bit_pos in range(depth):
        if bit_pos == depth - 1:
            if bit_pos == 0:
                sent = upward(block.astype(jnp.bfloat16), "seq", bit_pos)
            else:
                sent = relay(block.astype(jnp.bfloat16), "seq", bit_pos)
            other, other_decay = (sent.astype(jnp.float32), jnp.zeros_like(block_decay))
        else:
            sent, other_decay = from_partner((block.astype(jnp.bfloat16), block_decay), "seq", bit_pos)
            other = sent.astype(jnp.float32)
        upper = jnp.zeros_like(block_decay) + (jnp.right_shift(myself, bit_pos) & 1).astype(
            jnp.float32
        )
        block, block_decay, leading, found = combine(
            block, block_decay, other, other_decay, leading, upper
        )
        found_all.append(found)
    return jnp.stack(found_all, axis=0)


def local(
    xbc_in, conv_weight, conv_bias, dt_raw, decay_rate, skip, level_table, group_class, cotangent
):
    length = xbc_in.shape[0]
    taps = conv_weight.shape[0]
    heads = dt_raw.shape[1]
    inner = cotangent.shape[1]
    head_dim = inner // heads
    state_dim = (xbc_in.shape[1] - inner) // 2
    classes = level_table.shape[0]
    levels = level_table.shape[1]
    groups = group_class.shape[0]
    group_len = length // groups
    edge_part = shifted(xbc_in[length - taps + 1 :], "seq", 1)
    window = jnp.concatenate([edge_part, xbc_in], axis=0)
    preact = conv_forward(window, conv_weight, conv_bias, length)
    x_act, b_key, c_query = split_act(preact, heads, head_dim, state_dim)
    log_decay = -decay_rate[None, :] * jax.nn.softplus(dt_raw)
    grad_out = cotangent.reshape(length, heads, head_dim)
    picked = (group_class[:, None] == jnp.arange(classes, dtype=jnp.int32)[None, :]).astype(
        jnp.float32
    )
    weight_rows = exact("gk,klh->glh", picked, level_table)
    x_groups = x_act.reshape(groups, group_len, heads, head_dim)
    c_groups = c_query.reshape(groups, group_len, state_dim)
    grad_groups = grad_out.reshape(groups, group_len, heads, head_dim)
    y_inner, states, cumuls, grad_inner, level_zero = jax.vmap(local_group)(
        x_groups,
        b_key.reshape(groups, group_len, state_dim),
        c_groups,
        log_decay.reshape(groups, group_len, heads),
        grad_groups,
        weight_rows[:, 0],
    )
    totals = cumuls[:, -1]
    dev_decay = jnp.sum(totals, axis=0)
    later = dev_decay[None, :] - jnp.cumsum(totals, axis=0)
    dev_state = jnp.sum(jnp.exp(later)[:, :, None, None] * states, axis=0)
    devices = lax.axis_size("seq")
    depth = devices.bit_length() - 1
    myself = lax.axis_index("seq")
    chunks = 2 if heads % 2 == 0 else 1
    width = heads // chunks
    pieces = [
        exchange(dev_state[k * width : (k + 1) * width], dev_decay[k * width : (k + 1) * width], depth, myself)
        for k in range(chunks)
    ]
    cross = jnp.concatenate(pieces, axis=1)
    low_levels = groups.bit_length() - 1
    local_ids = jnp.arange(groups, dtype=jnp.int32)
    differ = jnp.bitwise_xor(local_ids[:, None], local_ids[None, :])
    lower = local_ids[:, None] > local_ids[None, :]
    slot_of = jnp.zeros((groups, groups), jnp.int32)
    onehot = (
        (slot_of[:, :, None] == jnp.arange(low_levels, dtype=jnp.int32)[None, None, :])
        & lower[:, :, None]
    ).astype(jnp.float32)
    before = jnp.cumsum(totals, axis=0) - totals
    gap = before[:, None, :] - before[None, :, :] - totals[None, :, :]
    below = lower[:, :, None]
    fade_pairs = jnp.where(below, jnp.exp(jnp.where(below, gap, 0.0)), 0.0)
    local_weight = exact("cds,csh->cdh", onehot, weight_rows[:, 1 : 1 + low_levels]) * fade_pairs
    lead_fade = jnp.exp(before)
    cross_weight = weight_rows[:, 1 + low_levels : 1 + low_levels + depth] * lead_fade[:, None, :]
    terms = [local_weight[:, d, :, None, None] * states[d][None] for d in range(groups)]
    terms += [cross_weight[:, l, :, None, None] * cross[l][None] for l in range(depth)]
    mixed = sum(terms[1:], terms[0]).astype(jnp.bfloat16)
    scaled = jnp.exp(cumuls) / state_dim
    query_faded = (c_groups[:, :, None, :] * scaled[:, :, :, None]).astype(jnp.bfloat16)
    y_cross = contract("cthn,chnp->cthp", query_faded, mixed)
    backed = contract("chnp,cthp->cthn", mixed, grad_groups)
    grad_cross = jnp.sum(backed * scaled[:, :, :, None], axis=2)
    gram = contract("cthn,cthp->chnp", query_faded, grad_groups)
    inner_pairs = jnp.sum(states[None] * gram[:, None], axis=(3, 4))
    level_local = exact("cds,cdh->csh", onehot, fade_pairs * inner_pairs)
    level_cross = lead_fade[:, None, :] * jnp.sum(cross[None] * gram[:, None], axis=(3, 4))
    level_rest = jnp.concatenate(
        [
            level_local,
            level_cross,
            jnp.zeros((groups, levels - 1 - low_levels - depth, heads), jnp.float32),
        ],
        axis=1,
    )
    grads = exact("ck,clh->klh", picked, level_rest)
    ssm_out = (
        (y_inner + y_cross + skip[None, None, :, None] * x_groups)
        .astype(jnp.bfloat16)
        .reshape(length, inner)
    )
    grad_query = (grad_inner + grad_cross).reshape(length, state_dim)
    after_rows = shifted(grad_query[: taps - 1], "seq", -1)
    extended = jnp.concatenate([grad_query, after_rows], axis=0)
    query_taps = conv_weight[:, inner + state_dim :]
    grad_c_in = jnp.zeros((length, state_dim), jnp.float32)
    for offset in range(taps):
        lagged = taps - 1 - offset
        grad_c_in = grad_c_in + query_taps[offset][None, :] * extended[lagged : lagged + length]
    grad_first = exact("gk,gh->kh", picked, level_zero)
    local_grads = jnp.concatenate([grad_first[:, None, :], grads], axis=1)
    summed = all_sum(local_grads, "seq")
    level_update = level_table + summed / math.sqrt(length * devices)
    return (ssm_out, grad_c_in, level_update)


def solution(mesh):
    placed = (
        P(("grp", "seq"), None),
        P(),
        P(),
        P(("grp", "seq"), None),
        P(),
        P(),
        P(),
        P(("grp", "seq")),
        P(("grp", "seq"), None),
    )
    return jax.shard_map(
        local,
        mesh=mesh,
        in_specs=placed,
        out_specs=(P(("grp", "seq"), None), P(("grp", "seq"), None), P("grp", None, None)),
        check_vma=False,
    )
```

```python
import math

import jax
import jax.numpy as jnp
from jax import lax
from jax.sharding import PartitionSpec as P


def shifted(value, axis, steps):
    count = lax.axis_size(axis)
    leading, last = (max(0, -steps), min(count, count - steps))
    return lax.ppermute(value, axis, [(source, source + steps) for source in range(leading, last)])


def from_partner(value, axis, distance):
    mask = 2**distance
    pairs = [(source, source ^ mask) for source in range(lax.axis_size(axis))]
    return lax.ppermute(value, axis, pairs)


def upward(value, axis, distance):
    mask = 2**distance
    count = lax.axis_size(axis)
    pairs = [(source, source | mask) for source in range(count) if not source & mask]
    return lax.ppermute(value, axis, pairs)


def all_sum(value, axis):
    for distance in range(lax.axis_size(axis).bit_length() - 1):
        value = value + from_partner(value, axis, distance)
    return value


def contract(form, left, right):
    return jnp.einsum(form, left, right, preferred_element_type=jnp.float32)


def exact(form, left, right):
    return jnp.einsum(form, left, right, precision=lax.Precision.HIGHEST)


def conv_forward(window, conv_weight, conv_bias, length):
    result = jnp.zeros((length, window.shape[1]), jnp.float32) + conv_bias[None, :]
    for offset in range(conv_weight.shape[0]):
        result = (
            result
            + window[offset : offset + length].astype(jnp.float32) * conv_weight[offset][None, :]
        )
    return result


def split_act(preact, heads, head_dim, state_dim):
    length = preact.shape[0]
    inner = heads * head_dim
    x_act = jax.nn.silu(preact[:, :inner]).astype(jnp.bfloat16).reshape(length, heads, head_dim)
    b_key = preact[:, inner : inner + state_dim].astype(jnp.bfloat16)
    c_query = preact[:, inner + state_dim :].astype(jnp.bfloat16)
    return (x_act, b_key, c_query)


def local_group(x_part, b_part, c_part, decay_part, grad_part, weight_zero):
    length = x_part.shape[0]
    state_dim = b_part.shape[1]
    cumul = jnp.cumsum(decay_part, axis=0)
    scores = jnp.dot(c_part, b_part.T, preferred_element_type=jnp.float32)
    causal = (jnp.arange(length)[:, None] >= jnp.arange(length)[None, :])[None]
    across = jnp.transpose(cumul)
    spread = across[:, :, None] - across[:, None, :]
    fading = jnp.where(causal, jnp.exp(jnp.where(causal, spread, 0.0)), 0.0)
    basic = fading * scores[None] / state_dim
    intra = (weight_zero[:, None, None] * basic).astype(jnp.bfloat16)
    y_inner = contract("hts,shp->thp", intra, x_part)
    x_faded = (x_part * jnp.exp(cumul[-1][None, :] - cumul)[:, :, None]).astype(jnp.bfloat16)
    group_state = contract("sn,shp->hnp", b_part, x_faded)
    products = contract("thp,shp->hts", grad_part, x_part)
    grad_weight = (
        jnp.sum(weight_zero[:, None, None] * fading * products, axis=0) / state_dim
    ).astype(jnp.bfloat16)
    grad_inner = jnp.dot(grad_weight, b_part, preferred_element_type=jnp.float32)
    level_zero = jnp.sum(basic * products, axis=(1, 2))
    return (y_inner, group_state, cumul, grad_inner, level_zero)


def combine(block, block_decay, other, other_decay, leading, upper):
    grown = upper[..., None, None]
    found = grown * jnp.exp(leading)[..., None, None] * other
    joined = grown * (other * jnp.exp(block_decay)[..., None, None] + block) + (1.0 - grown) * (
        block * jnp.exp(other_decay)[..., None, None] + other
    )
    return (joined, block_decay + other_decay, leading + upper * other_decay, found)


def relay(value, axis, bit_pos):
    half = 2**bit_pos
    step = half // 2
    first = lax.ppermute(value, axis, [(source, source + step) for source in range(half - step, half)])
    second = lax.ppermute(first, axis, [(source, source + step) for source in range(half, half + step)])
    return first + second


def exchange(block, block_decay, depth, myself):
    leading = jnp.zeros_like(block_decay)
    found_all = []
    for bit_pos in range(depth):
        if bit_pos == depth - 1:
            if bit_pos == 0:
                sent = upward(block.astype(jnp.bfloat16), "seq", bit_pos)
            else:
                sent = relay(block.astype(jnp.bfloat16), "seq", bit_pos)
            other, other_decay = (sent.astype(jnp.float32), jnp.zeros_like(block_decay))
        else:
            sent, other_decay = from_partner((block.astype(jnp.bfloat16), block_decay), "seq", bit_pos)
            other = sent.astype(jnp.float32)
        upper = jnp.zeros_like(block_decay) + (jnp.right_shift(myself, bit_pos) & 1).astype(
            jnp.float32
        )
        block, block_decay, leading, found = combine(
            block, block_decay, other, other_decay, leading, upper
        )
        found_all.append(found)
    return jnp.stack(found_all, axis=0)


def local(
    xbc_in, conv_weight, conv_bias, dt_raw, decay_rate, skip, level_table, group_class, cotangent
):
    length = xbc_in.shape[0]
    taps = conv_weight.shape[0]
    heads = dt_raw.shape[1]
    inner = cotangent.shape[1]
    head_dim = inner // heads
    state_dim = (xbc_in.shape[1] - inner) // 2
    classes = level_table.shape[0]
    levels = level_table.shape[1]
    groups = group_class.shape[0]
    group_len = length // groups
    edge_part = shifted(xbc_in[length - taps + 1 :], "seq", 1)
    window = jnp.concatenate([edge_part, xbc_in], axis=0)
    preact = conv_forward(window, conv_weight, conv_bias, length)
    x_act, b_key, c_query = split_act(preact, heads, head_dim, state_dim)
    log_decay = -decay_rate[None, :] * jax.nn.softplus(dt_raw)
    grad_out = cotangent.reshape(length, heads, head_dim)
    picked = (group_class[:, None] == jnp.arange(classes, dtype=jnp.int32)[None, :]).astype(
        jnp.float32
    )
    weight_rows = exact("gk,klh->glh", picked, level_table)
    x_groups = x_act.reshape(groups, group_len, heads, head_dim)
    c_groups = c_query.reshape(groups, group_len, state_dim)
    grad_groups = grad_out.reshape(groups, group_len, heads, head_dim)
    y_inner, states, cumuls, grad_inner, level_zero = jax.vmap(local_group)(
        x_groups,
        b_key.reshape(groups, group_len, state_dim),
        c_groups,
        log_decay.reshape(groups, group_len, heads),
        grad_groups,
        weight_rows[:, 0],
    )
    totals = cumuls[:, -1]
    dev_decay = jnp.sum(totals, axis=0)
    later = dev_decay[None, :] - jnp.cumsum(totals, axis=0)
    dev_state = jnp.sum(jnp.exp(later)[:, :, None, None] * states, axis=0)
    devices = lax.axis_size("seq")
    depth = devices.bit_length() - 1
    myself = lax.axis_index("seq")
    chunks = 4 if heads % 4 == 0 else 1
    width = heads // chunks
    pieces = [
        exchange(dev_state[k * width : (k + 1) * width], dev_decay[k * width : (k + 1) * width], depth, myself)
        for k in range(chunks)
    ]
    cross = jnp.concatenate(pieces, axis=1)
    low_levels = groups.bit_length() - 1
    local_ids = jnp.arange(groups, dtype=jnp.int32)
    differ = jnp.bitwise_xor(local_ids[:, None], local_ids[None, :])
    lower = local_ids[:, None] > local_ids[None, :]
    slot_of = jnp.zeros((groups, groups), jnp.int32)
    onehot = (
        (slot_of[:, :, None] == jnp.arange(low_levels, dtype=jnp.int32)[None, None, :])
        & lower[:, :, None]
    ).astype(jnp.float32)
    before = jnp.cumsum(totals, axis=0) - totals
    gap = before[:, None, :] - before[None, :, :] - totals[None, :, :]
    below = lower[:, :, None]
    fade_pairs = jnp.where(below, jnp.exp(jnp.where(below, gap, 0.0)), 0.0)
    local_weight = exact("cds,csh->cdh", onehot, weight_rows[:, 1 : 1 + low_levels]) * fade_pairs
    lead_fade = jnp.exp(before)
    cross_weight = weight_rows[:, 1 + low_levels : 1 + low_levels + depth] * lead_fade[:, None, :]
    terms = [local_weight[:, d, :, None, None] * states[d][None] for d in range(groups)]
    terms += [cross_weight[:, l, :, None, None] * cross[l][None] for l in range(depth)]
    mixed = sum(terms[1:], terms[0]).astype(jnp.bfloat16)
    scaled = jnp.exp(cumuls) / state_dim
    query_faded = (c_groups[:, :, None, :] * scaled[:, :, :, None]).astype(jnp.bfloat16)
    y_cross = contract("cthn,chnp->cthp", query_faded, mixed)
    backed = contract("chnp,cthp->cthn", mixed, grad_groups)
    grad_cross = jnp.sum(backed * scaled[:, :, :, None], axis=2)
    gram = contract("cthn,cthp->chnp", query_faded, grad_groups)
    inner_pairs = jnp.sum(states[None] * gram[:, None], axis=(3, 4))
    level_local = exact("cds,cdh->csh", onehot, fade_pairs * inner_pairs)
    level_cross = lead_fade[:, None, :] * jnp.sum(cross[None] * gram[:, None], axis=(3, 4))
    level_rest = jnp.concatenate(
        [
            level_local,
            level_cross,
            jnp.zeros((groups, levels - 1 - low_levels - depth, heads), jnp.float32),
        ],
        axis=1,
    )
    grads = exact("ck,clh->klh", picked, level_rest)
    ssm_out = (
        (y_inner + y_cross + skip[None, None, :, None] * x_groups)
        .astype(jnp.bfloat16)
        .reshape(length, inner)
    )
    grad_query = (grad_inner + grad_cross).reshape(length, state_dim)
    after_rows = shifted(grad_query[: taps - 1], "seq", -1)
    extended = jnp.concatenate([grad_query, after_rows], axis=0)
    query_taps = conv_weight[:, inner + state_dim :]
    grad_c_in = jnp.zeros((length, state_dim), jnp.float32)
    for offset in range(taps):
        lagged = taps - 1 - offset
        grad_c_in = grad_c_in + query_taps[offset][None, :] * extended[lagged : lagged + length]
    grad_first = exact("gk,gh->kh", picked, level_zero)
    local_grads = jnp.concatenate([grad_first[:, None, :], grads], axis=1)
    summed = all_sum(local_grads, "seq")
    level_update = level_table + summed / math.sqrt(length * devices)
    return (ssm_out, grad_c_in, level_update)


def solution(mesh):
    placed = (
        P(("grp", "seq"), None),
        P(),
        P(),
        P(("grp", "seq"), None),
        P(),
        P(),
        P(),
        P(("grp", "seq")),
        P(("grp", "seq"), None),
    )
    return jax.shard_map(
        local,
        mesh=mesh,
        in_specs=placed,
        out_specs=(P(("grp", "seq"), None), P(("grp", "seq"), None), P("grp", None, None)),
        check_vma=False,
    )
```

```python
import math

import jax
import jax.numpy as jnp
from jax import lax
from jax.sharding import PartitionSpec as P


def shifted(value, axis, steps):
    count = lax.axis_size(axis)
    leading, last = (max(0, -steps), min(count, count - steps))
    return lax.ppermute(value, axis, [(source, source + steps) for source in range(leading, last)])


def from_partner(value, axis, distance):
    mask = 2**distance
    pairs = [(source, source ^ mask) for source in range(lax.axis_size(axis))]
    return lax.ppermute(value, axis, pairs)


def upward(value, axis, distance):
    mask = 2**distance
    count = lax.axis_size(axis)
    pairs = [(source, source | mask) for source in range(count) if not source & mask]
    return lax.ppermute(value, axis, pairs)


def all_sum(value, axis):
    for distance in range(lax.axis_size(axis).bit_length() - 1):
        value = value + from_partner(value, axis, distance)
    return value


def contract(form, left, right):
    return jnp.einsum(form, left, right, preferred_element_type=jnp.float32)


def exact(form, left, right):
    return jnp.einsum(form, left, right, precision=lax.Precision.HIGHEST)


def conv_forward(window, conv_weight, conv_bias, length):
    result = jnp.zeros((length, window.shape[1]), jnp.float32) + conv_bias[None, :]
    for offset in range(conv_weight.shape[0]):
        result = (
            result
            + window[offset : offset + length].astype(jnp.float32) * conv_weight[offset][None, :]
        )
    return result


def split_act(preact, heads, head_dim, state_dim):
    length = preact.shape[0]
    inner = heads * head_dim
    x_act = jax.nn.silu(preact[:, :inner]).astype(jnp.bfloat16).reshape(length, heads, head_dim)
    b_key = preact[:, inner : inner + state_dim].astype(jnp.bfloat16)
    c_query = preact[:, inner + state_dim :].astype(jnp.bfloat16)
    return (x_act, b_key, c_query)


def group_state_of(x_part, b_part, decay_part):
    cumul = jnp.cumsum(decay_part, axis=0)
    x_faded = (x_part * jnp.exp(cumul[-1][None, :] - cumul)[:, :, None]).astype(jnp.bfloat16)
    group_state = contract("sn,shp->hnp", b_part, x_faded)
    return (group_state, cumul)


def local_group(x_part, b_part, c_part, cumul, grad_part, weight_zero):
    length = x_part.shape[0]
    state_dim = b_part.shape[1]
    scores = jnp.dot(c_part, b_part.T, preferred_element_type=jnp.float32)
    causal = (jnp.arange(length)[:, None] >= jnp.arange(length)[None, :])[None]
    across = jnp.transpose(cumul)
    spread = across[:, :, None] - across[:, None, :]
    fading = jnp.where(causal, jnp.exp(jnp.where(causal, spread, 0.0)), 0.0)
    basic = fading * scores[None] / state_dim
    intra = (weight_zero[:, None, None] * basic).astype(jnp.bfloat16)
    y_inner = contract("hts,shp->thp", intra, x_part)
    products = contract("thp,shp->hts", grad_part, x_part)
    grad_weight = (
        jnp.sum(weight_zero[:, None, None] * fading * products, axis=0) / state_dim
    ).astype(jnp.bfloat16)
    grad_inner = jnp.dot(grad_weight, b_part, preferred_element_type=jnp.float32)
    level_zero = jnp.sum(basic * products, axis=(1, 2))
    return (y_inner, grad_inner, level_zero)


def combine(block, block_decay, other, other_decay, leading, upper):
    grown = upper[..., None, None]
    found = grown * jnp.exp(leading)[..., None, None] * other
    joined = grown * (other * jnp.exp(block_decay)[..., None, None] + block) + (1.0 - grown) * (
        block * jnp.exp(other_decay)[..., None, None] + other
    )
    return (joined, block_decay + other_decay, leading + upper * other_decay, found)


def relay(value, axis, bit_pos):
    half = 2**bit_pos
    step = half // 2
    first = lax.ppermute(value, axis, [(source, source + step) for source in range(half - step, half)])
    second = lax.ppermute(first, axis, [(source, source + step) for source in range(half, half + step)])
    return first + second


def exchange(block, block_decay, depth, myself):
    leading = jnp.zeros_like(block_decay)
    found_all = []
    first = None
    for bit_pos in range(depth):
        if bit_pos == depth - 1:
            if bit_pos == 0:
                sent = upward(block.astype(jnp.bfloat16), "seq", bit_pos)
            else:
                sent = relay(block.astype(jnp.bfloat16), "seq", bit_pos)
            other, other_decay = (sent.astype(jnp.float32), jnp.zeros_like(block_decay))
        else:
            sent, other_decay = from_partner((block.astype(jnp.bfloat16), block_decay), "seq", bit_pos)
            other = sent.astype(jnp.float32)
        first = sent if first is None else first
        upper = jnp.zeros_like(block_decay) + (jnp.right_shift(myself, bit_pos) & 1).astype(
            jnp.float32
        )
        block, block_decay, leading, found = combine(
            block, block_decay, other, other_decay, leading, upper
        )
        found_all.append(found)
    first = block if first is None else first
    return (jnp.stack(found_all, axis=0), first)


def local(
    xbc_in, conv_weight, conv_bias, dt_raw, decay_rate, skip, level_table, group_class, cotangent
):
    length = xbc_in.shape[0]
    taps = conv_weight.shape[0]
    heads = dt_raw.shape[1]
    inner = cotangent.shape[1]
    head_dim = inner // heads
    state_dim = (xbc_in.shape[1] - inner) // 2
    classes = level_table.shape[0]
    levels = level_table.shape[1]
    groups = group_class.shape[0]
    group_len = length // groups
    edge_part = shifted(xbc_in[length - taps + 1 :], "seq", 1)
    window = jnp.concatenate([edge_part, xbc_in], axis=0)
    preact = conv_forward(window, conv_weight, conv_bias, length)
    x_act, b_key, c_query = split_act(preact, heads, head_dim, state_dim)
    log_decay = -decay_rate[None, :] * jax.nn.softplus(dt_raw)
    grad_out = cotangent.reshape(length, heads, head_dim)
    picked = (group_class[:, None] == jnp.arange(classes, dtype=jnp.int32)[None, :]).astype(
        jnp.float32
    )
    weight_rows = exact("gk,klh->glh", picked, level_table)
    x_groups = x_act.reshape(groups, group_len, heads, head_dim)
    c_groups = c_query.reshape(groups, group_len, state_dim)
    grad_groups = grad_out.reshape(groups, group_len, heads, head_dim)
    b_groups = b_key.reshape(groups, group_len, state_dim)
    states, cumuls = jax.vmap(group_state_of)(
        x_groups, b_groups, log_decay.reshape(groups, group_len, heads)
    )
    totals = cumuls[:, -1]
    dev_decay = jnp.sum(totals, axis=0)
    later = dev_decay[None, :] - jnp.cumsum(totals, axis=0)
    dev_state = jnp.sum(jnp.exp(later)[:, :, None, None] * states, axis=0)
    devices = lax.axis_size("seq")
    depth = devices.bit_length() - 1
    myself = lax.axis_index("seq")
    chunks = 2 if heads % 2 == 0 else 1
    width = heads // chunks
    pieces = [
        exchange(dev_state[k * width : (k + 1) * width], dev_decay[k * width : (k + 1) * width], depth, myself)
        for k in range(chunks)
    ]
    cross = jnp.concatenate([piece for piece, _ in pieces], axis=1)
    late_cotangent = lax.optimization_barrier((cotangent, pieces[0][1]))[0]
    grad_groups = late_cotangent.reshape(groups, group_len, heads, head_dim)
    y_inner, grad_inner, level_zero = jax.vmap(local_group)(
        x_groups, b_groups, c_groups, cumuls, grad_groups, weight_rows[:, 0]
    )
    low_levels = groups.bit_length() - 1
    local_ids = jnp.arange(groups, dtype=jnp.int32)
    differ = jnp.bitwise_xor(local_ids[:, None], local_ids[None, :])
    lower = local_ids[:, None] > local_ids[None, :]
    slot_of = jnp.zeros((groups, groups), jnp.int32)
    onehot = (
        (slot_of[:, :, None] == jnp.arange(low_levels, dtype=jnp.int32)[None, None, :])
        & lower[:, :, None]
    ).astype(jnp.float32)
    before = jnp.cumsum(totals, axis=0) - totals
    gap = before[:, None, :] - before[None, :, :] - totals[None, :, :]
    below = lower[:, :, None]
    fade_pairs = jnp.where(below, jnp.exp(jnp.where(below, gap, 0.0)), 0.0)
    local_weight = exact("cds,csh->cdh", onehot, weight_rows[:, 1 : 1 + low_levels]) * fade_pairs
    lead_fade = jnp.exp(before)
    cross_weight = weight_rows[:, 1 + low_levels : 1 + low_levels + depth] * lead_fade[:, None, :]
    terms = [local_weight[:, d, :, None, None] * states[d][None] for d in range(groups)]
    terms += [cross_weight[:, l, :, None, None] * cross[l][None] for l in range(depth)]
    mixed = sum(terms[1:], terms[0]).astype(jnp.bfloat16)
    scaled = jnp.exp(cumuls) / state_dim
    query_faded = (c_groups[:, :, None, :] * scaled[:, :, :, None]).astype(jnp.bfloat16)
    y_cross = contract("cthn,chnp->cthp", query_faded, mixed)
    backed = contract("chnp,cthp->cthn", mixed, grad_groups)
    grad_cross = jnp.sum(backed * scaled[:, :, :, None], axis=2)
    gram = contract("cthn,cthp->chnp", query_faded, grad_groups)
    inner_pairs = jnp.sum(states[None] * gram[:, None], axis=(3, 4))
    level_local = exact("cds,cdh->csh", onehot, fade_pairs * inner_pairs)
    level_cross = lead_fade[:, None, :] * jnp.sum(cross[None] * gram[:, None], axis=(3, 4))
    level_rest = jnp.concatenate(
        [
            level_local,
            level_cross,
            jnp.zeros((groups, levels - 1 - low_levels - depth, heads), jnp.float32),
        ],
        axis=1,
    )
    grads = exact("ck,clh->klh", picked, level_rest)
    ssm_out = (
        (y_inner + y_cross + skip[None, None, :, None] * x_groups)
        .astype(jnp.bfloat16)
        .reshape(length, inner)
    )
    grad_query = (grad_inner + grad_cross).reshape(length, state_dim)
    after_rows = shifted(grad_query[: taps - 1], "seq", -1)
    extended = jnp.concatenate([grad_query, after_rows], axis=0)
    query_taps = conv_weight[:, inner + state_dim :]
    grad_c_in = jnp.zeros((length, state_dim), jnp.float32)
    for offset in range(taps):
        lagged = taps - 1 - offset
        grad_c_in = grad_c_in + query_taps[offset][None, :] * extended[lagged : lagged + length]
    grad_first = exact("gk,gh->kh", picked, level_zero)
    local_grads = jnp.concatenate([grad_first[:, None, :], grads], axis=1)
    summed = all_sum(local_grads, "seq")
    level_update = level_table + summed / math.sqrt(length * devices)
    return (ssm_out, grad_c_in, level_update)


def solution(mesh):
    placed = (
        P(("grp", "seq"), None),
        P(),
        P(),
        P(("grp", "seq"), None),
        P(),
        P(),
        P(),
        P(("grp", "seq")),
        P(("grp", "seq"), None),
    )
    return jax.shard_map(
        local,
        mesh=mesh,
        in_specs=placed,
        out_specs=(P(("grp", "seq"), None), P(("grp", "seq"), None), P("grp", None, None)),
        check_vma=False,
    )
```

```python
import math

import jax
import jax.numpy as jnp
from jax import lax
from jax.sharding import PartitionSpec as P


def shifted(value, axis, steps):
    count = lax.axis_size(axis)
    leading, last = (max(0, -steps), min(count, count - steps))
    return lax.ppermute(value, axis, [(source, source + steps) for source in range(leading, last)])


def from_partner(value, axis, distance):
    mask = 2**distance
    pairs = [(source, source ^ mask) for source in range(lax.axis_size(axis))]
    return lax.ppermute(value, axis, pairs)


def upward(value, axis, distance):
    mask = 2**distance
    count = lax.axis_size(axis)
    pairs = [(source, source | mask) for source in range(count) if not source & mask]
    return lax.ppermute(value, axis, pairs)


def all_sum(value, axis):
    for distance in range(lax.axis_size(axis).bit_length() - 1):
        value = value + from_partner(value, axis, distance)
    return value


def contract(form, left, right):
    return jnp.einsum(form, left, right, preferred_element_type=jnp.float32)


def exact(form, left, right):
    return jnp.einsum(form, left, right, precision=lax.Precision.HIGHEST)


def conv_forward(window, conv_weight, conv_bias, length):
    result = jnp.zeros((length, window.shape[1]), jnp.float32) + conv_bias[None, :]
    for offset in range(conv_weight.shape[0]):
        result = (
            result
            + window[offset : offset + length].astype(jnp.float32) * conv_weight[offset][None, :]
        )
    return result


def split_act(preact, heads, head_dim, state_dim):
    length = preact.shape[0]
    inner = heads * head_dim
    x_act = jax.nn.silu(preact[:, :inner]).astype(jnp.bfloat16).reshape(length, heads, head_dim)
    b_key = preact[:, inner : inner + state_dim].astype(jnp.bfloat16)
    c_query = preact[:, inner + state_dim :].astype(jnp.bfloat16)
    return (x_act, b_key, c_query)


def lanes(per_head, head_dim):
    return jnp.repeat(per_head, head_dim, axis=-1)


def per_head(value, head_dim):
    return jnp.sum(value.reshape(value.shape[:-1] + (-1, head_dim)), axis=-1)


def spread(per_head_values, heads, head_dim):
    places = jnp.arange(heads * head_dim, dtype=jnp.int32)[None, :] // head_dim
    expand = (places == jnp.arange(heads, dtype=jnp.int32)[:, None]).astype(jnp.float32)
    return exact("...h,hq->...q", per_head_values, expand)


def group_state_of(x_part, b_part, decay_part):
    cumul = jnp.cumsum(decay_part, axis=0)
    x_faded = (x_part * jnp.exp(cumul[-1][None, :] - cumul)[:, :, None]).astype(jnp.bfloat16)
    group_state = contract("sn,shp->hnp", b_part, x_faded)
    return (group_state, cumul)


def local_group(x_part, b_part, c_part, cumul, grad_part, weight_zero):
    length = x_part.shape[0]
    state_dim = b_part.shape[1]
    scores = jnp.dot(c_part, b_part.T, preferred_element_type=jnp.float32)
    causal = (jnp.arange(length)[:, None] >= jnp.arange(length)[None, :])[None]
    across = jnp.transpose(cumul)
    spread = across[:, :, None] - across[:, None, :]
    fading = jnp.where(causal, jnp.exp(jnp.where(causal, spread, 0.0)), 0.0)
    basic = fading * scores[None] / state_dim
    intra = (weight_zero[:, None, None] * basic).astype(jnp.bfloat16)
    y_inner = contract("hts,shp->thp", intra, x_part)
    products = contract("thp,shp->hts", grad_part, x_part)
    grad_weight = (
        jnp.sum(weight_zero[:, None, None] * fading * products, axis=0) / state_dim
    ).astype(jnp.bfloat16)
    grad_inner = jnp.dot(grad_weight, b_part, preferred_element_type=jnp.float32)
    level_zero = jnp.sum(basic * products, axis=(1, 2))
    return (y_inner, grad_inner, level_zero)


def combine(block, block_decay, other, other_decay, leading, upper):
    head_dim = block.shape[-1] // block_decay.shape[-1]
    grown = upper
    found = grown * lanes(jnp.exp(leading), head_dim) * other
    joined = grown * (other * lanes(jnp.exp(block_decay), head_dim) + block) + (1.0 - grown) * (
        block * lanes(jnp.exp(other_decay), head_dim) + other
    )
    return (joined, block_decay + other_decay, leading + upper * other_decay, found)


def relay(value, axis, bit_pos):
    half = 2**bit_pos
    step = half // 2
    first = lax.ppermute(value, axis, [(source, source + step) for source in range(half - step, half)])
    second = lax.ppermute(first, axis, [(source, source + step) for source in range(half, half + step)])
    return first + second


def exchange(block, block_decay, depth, myself):
    leading = jnp.zeros_like(block_decay)
    found_all = []
    first = None
    for bit_pos in range(depth):
        if bit_pos == depth - 1:
            if bit_pos == 0:
                sent = upward(block.astype(jnp.bfloat16), "seq", bit_pos)
            else:
                sent = relay(block.astype(jnp.bfloat16), "seq", bit_pos)
            other, other_decay = (sent.astype(jnp.float32), jnp.zeros_like(block_decay))
        else:
            sent, other_decay = from_partner((block.astype(jnp.bfloat16), block_decay), "seq", bit_pos)
            other = sent.astype(jnp.float32)
        first = sent if first is None else first
        upper = (jnp.right_shift(myself, bit_pos) & 1).astype(jnp.float32)
        block, block_decay, leading, found = combine(
            block, block_decay, other, other_decay, leading, upper
        )
        found_all.append(found)
    first = block if first is None else first
    return (jnp.stack(found_all, axis=0), first)


def local(
    xbc_in, conv_weight, conv_bias, dt_raw, decay_rate, skip, level_table, group_class, cotangent
):
    length = xbc_in.shape[0]
    taps = conv_weight.shape[0]
    heads = dt_raw.shape[1]
    inner = cotangent.shape[1]
    head_dim = inner // heads
    state_dim = (xbc_in.shape[1] - inner) // 2
    classes = level_table.shape[0]
    levels = level_table.shape[1]
    groups = group_class.shape[0]
    group_len = length // groups
    edge_part = shifted(xbc_in[length - taps + 1 :], "seq", 1)
    window = jnp.concatenate([edge_part, xbc_in], axis=0)
    preact = conv_forward(window, conv_weight, conv_bias, length)
    x_act, b_key, c_query = split_act(preact, heads, head_dim, state_dim)
    log_decay = -decay_rate[None, :] * jax.nn.softplus(dt_raw)
    grad_out = cotangent.reshape(length, heads, head_dim)
    picked = (group_class[:, None] == jnp.arange(classes, dtype=jnp.int32)[None, :]).astype(
        jnp.float32
    )
    weight_rows = exact("gk,klh->glh", picked, level_table)
    x_groups = x_act.reshape(groups, group_len, heads, head_dim)
    c_groups = c_query.reshape(groups, group_len, state_dim)
    grad_groups = grad_out.reshape(groups, group_len, heads, head_dim)
    b_groups = b_key.reshape(groups, group_len, state_dim)
    cumuls = jnp.cumsum(log_decay.reshape(groups, group_len, heads), axis=1)
    x_flat = x_act.reshape(groups, group_len, inner)
    ending = spread(jnp.exp(cumuls[:, -1:, :] - cumuls), heads, head_dim)
    x_faded = (x_flat * ending).astype(jnp.bfloat16)
    states = contract("gtn,gtq->gnq", b_groups, x_faded)
    totals = cumuls[:, -1]
    dev_decay = jnp.sum(totals, axis=0)
    later = dev_decay[None, :] - jnp.cumsum(totals, axis=0)
    dev_state = jnp.sum(lanes(jnp.exp(later), head_dim)[:, None, :] * states, axis=0)
    devices = lax.axis_size("seq")
    depth = devices.bit_length() - 1
    myself = lax.axis_index("seq")
    chunks = 2 if heads % 2 == 0 else 1
    width = heads // chunks
    pieces = [
        exchange(
            dev_state[:, k * width * head_dim : (k + 1) * width * head_dim],
            dev_decay[k * width : (k + 1) * width],
            depth,
            myself,
        )
        for k in range(chunks)
    ]
    cross = jnp.concatenate([piece for piece, _ in pieces], axis=2)
    late_cotangent = lax.optimization_barrier((cotangent, pieces[0][1]))[0]
    grad_groups = late_cotangent.reshape(groups, group_len, heads, head_dim)
    g_flat = late_cotangent.reshape(groups, group_len, inner)
    y_inner, grad_inner, level_zero = jax.vmap(local_group)(
        x_groups, b_groups, c_groups, cumuls, grad_groups, weight_rows[:, 0]
    )
    low_levels = groups.bit_length() - 1
    local_ids = jnp.arange(groups, dtype=jnp.int32)
    differ = jnp.bitwise_xor(local_ids[:, None], local_ids[None, :])
    lower = local_ids[:, None] > local_ids[None, :]
    slot_of = jnp.zeros((groups, groups), jnp.int32)
    onehot = (
        (slot_of[:, :, None] == jnp.arange(low_levels, dtype=jnp.int32)[None, None, :])
        & lower[:, :, None]
    ).astype(jnp.float32)
    before = jnp.cumsum(totals, axis=0) - totals
    gap = before[:, None, :] - before[None, :, :] - totals[None, :, :]
    below = lower[:, :, None]
    fade_pairs = jnp.where(below, jnp.exp(jnp.where(below, gap, 0.0)), 0.0)
    local_weight = exact("cds,csh->cdh", onehot, weight_rows[:, 1 : 1 + low_levels]) * fade_pairs
    lead_fade = jnp.exp(before)
    cross_weight = weight_rows[:, 1 + low_levels : 1 + low_levels + depth] * lead_fade[:, None, :]
    terms = [lanes(local_weight[:, d], head_dim)[:, None, :] * states[d][None] for d in range(groups)]
    terms += [lanes(cross_weight[:, l], head_dim)[:, None, :] * cross[l][None] for l in range(depth)]
    mixed = sum(terms[1:], terms[0]).astype(jnp.bfloat16)
    scaled = spread(jnp.exp(cumuls) / state_dim, heads, head_dim)
    y_cross = scaled * contract("ctn,cnq->ctq", c_groups, mixed)
    grad_scaled = scaled * g_flat
    grad_cross = exact("ctq,cnq->ctn", grad_scaled, mixed.astype(jnp.float32))
    gram = exact("ctn,ctq->cnq", c_groups.astype(jnp.float32), grad_scaled)
    inner_pairs = jnp.stack(
        [jnp.stack([per_head(jnp.sum(states[d] * gram[c], axis=0), head_dim) for d in range(groups)]) for c in range(groups)]
    )
    cross_pairs = jnp.stack(
        [jnp.stack([per_head(jnp.sum(cross[l] * gram[c], axis=0), head_dim) for l in range(depth)]) for c in range(groups)]
    )
    level_local = exact("cds,cdh->csh", onehot, fade_pairs * inner_pairs)
    level_cross = lead_fade[:, None, :] * cross_pairs
    level_rest = jnp.concatenate(
        [
            level_local,
            level_cross,
            jnp.zeros((groups, levels - 1 - low_levels - depth, heads), jnp.float32),
        ],
        axis=1,
    )
    grads = exact("ck,clh->klh", picked, level_rest)
    ssm_out = (
        (y_inner.reshape(groups, group_len, inner) + y_cross + lanes(skip, head_dim) * x_flat)
        .astype(jnp.bfloat16)
        .reshape(length, inner)
    )
    grad_query = (grad_inner + grad_cross).reshape(length, state_dim)
    after_rows = shifted(grad_query[: taps - 1], "seq", -1)
    extended = jnp.concatenate([grad_query, after_rows], axis=0)
    query_taps = conv_weight[:, inner + state_dim :]
    grad_c_in = jnp.zeros((length, state_dim), jnp.float32)
    for offset in range(taps):
        lagged = taps - 1 - offset
        grad_c_in = grad_c_in + query_taps[offset][None, :] * extended[lagged : lagged + length]
    grad_first = exact("gk,gh->kh", picked, level_zero)
    local_grads = jnp.concatenate([grad_first[:, None, :], grads], axis=1)
    summed = all_sum(local_grads, "seq")
    level_update = level_table + summed / math.sqrt(length * devices)
    return (ssm_out, grad_c_in, level_update)


def solution(mesh):
    placed = (
        P(("grp", "seq"), None),
        P(),
        P(),
        P(("grp", "seq"), None),
        P(),
        P(),
        P(),
        P(("grp", "seq")),
        P(("grp", "seq"), None),
    )
    return jax.shard_map(
        local,
        mesh=mesh,
        in_specs=placed,
        out_specs=(P(("grp", "seq"), None), P(("grp", "seq"), None), P("grp", None, None)),
        check_vma=False,
    )
```

```python
import math

import jax
import jax.numpy as jnp
from jax import lax
from jax.sharding import PartitionSpec as P


def shifted(value, axis, steps):
    count = lax.axis_size(axis)
    leading, last = (max(0, -steps), min(count, count - steps))
    return lax.ppermute(value, axis, [(source, source + steps) for source in range(leading, last)])


def from_partner(value, axis, distance):
    mask = 2**distance
    pairs = [(source, source ^ mask) for source in range(lax.axis_size(axis))]
    return lax.ppermute(value, axis, pairs)


def upward(value, axis, distance):
    mask = 2**distance
    count = lax.axis_size(axis)
    pairs = [(source, source | mask) for source in range(count) if not source & mask]
    return lax.ppermute(value, axis, pairs)


def all_sum(value, axis):
    for distance in range(lax.axis_size(axis).bit_length() - 1):
        value = value + from_partner(value, axis, distance)
    return value


def contract(form, left, right):
    return jnp.einsum(form, left, right, preferred_element_type=jnp.float32)


def exact(form, left, right):
    return jnp.einsum(form, left, right, precision=lax.Precision.HIGHEST)


def conv_forward(window, conv_weight, conv_bias, length):
    result = jnp.zeros((length, window.shape[1]), jnp.float32) + conv_bias[None, :]
    for offset in range(conv_weight.shape[0]):
        result = (
            result
            + window[offset : offset + length].astype(jnp.float32) * conv_weight[offset][None, :]
        )
    return result


def split_act(preact, heads, head_dim, state_dim):
    length = preact.shape[0]
    inner = heads * head_dim
    x_act = jax.nn.silu(preact[:, :inner]).astype(jnp.bfloat16).reshape(length, heads, head_dim)
    b_key = preact[:, inner : inner + state_dim].astype(jnp.bfloat16)
    c_query = preact[:, inner + state_dim :].astype(jnp.bfloat16)
    return (x_act, b_key, c_query)


def group_state_of(x_part, b_part, decay_part):
    cumul = jnp.cumsum(decay_part, axis=0)
    x_faded = (x_part * jnp.exp(cumul[-1][None, :] - cumul)[:, :, None]).astype(jnp.bfloat16)
    group_state = contract("sn,shp->hnp", b_part, x_faded)
    return (group_state, cumul)


def local_group(x_part, b_part, c_part, cumul, grad_part, weight_zero):
    length = x_part.shape[0]
    state_dim = b_part.shape[1]
    scores = jnp.dot(c_part, b_part.T, preferred_element_type=jnp.float32)
    causal = (jnp.arange(length)[:, None] >= jnp.arange(length)[None, :])[None]
    across = jnp.transpose(cumul)
    spread = across[:, :, None] - across[:, None, :]
    fading = jnp.where(causal, jnp.exp(jnp.where(causal, spread, 0.0)), 0.0)
    basic = fading * scores[None] / state_dim
    intra = (weight_zero[:, None, None] * basic).astype(jnp.bfloat16)
    y_inner = contract("hts,shp->thp", intra, x_part)
    products = contract("thp,shp->hts", grad_part, x_part)
    grad_weight = (
        jnp.sum(weight_zero[:, None, None] * fading * products, axis=0) / state_dim
    ).astype(jnp.bfloat16)
    grad_inner = jnp.dot(grad_weight, b_part, preferred_element_type=jnp.float32)
    level_zero = jnp.sum(basic * products, axis=(1, 2))
    return (y_inner, grad_inner, level_zero)


def combine(block, block_decay, other, other_decay, leading, upper):
    grown = upper[..., None, None]
    found = grown * jnp.exp(leading)[..., None, None] * other
    joined = grown * (other * jnp.exp(block_decay)[..., None, None] + block) + (1.0 - grown) * (
        block * jnp.exp(other_decay)[..., None, None] + other
    )
    return (joined, block_decay + other_decay, leading + upper * other_decay, found)


def relay(value, axis, bit_pos):
    half = 2**bit_pos
    step = half // 2
    first = lax.ppermute(value, axis, [(source, source + step) for source in range(half - step, half)])
    second = lax.ppermute(first, axis, [(source, source + step) for source in range(half, half + step)])
    return first + second


def exchange(block, block_decay, depth, myself):
    leading = jnp.zeros_like(block_decay)
    found_all = []
    first = None
    for bit_pos in range(depth):
        if bit_pos == depth - 1:
            if bit_pos == 0:
                sent = upward(block.astype(jnp.bfloat16), "seq", bit_pos)
            else:
                sent = relay(block.astype(jnp.bfloat16), "seq", bit_pos)
            other, other_decay = (sent.astype(jnp.float32), jnp.zeros_like(block_decay))
        elif bit_pos == depth - 2:
            sent, other_decay = upward((block.astype(jnp.bfloat16), block_decay), "seq", bit_pos)
            other = sent.astype(jnp.float32)
        else:
            sent, other_decay = from_partner((block.astype(jnp.bfloat16), block_decay), "seq", bit_pos)
            other = sent.astype(jnp.float32)
        first = sent if first is None else first
        upper = jnp.zeros_like(block_decay) + (jnp.right_shift(myself, bit_pos) & 1).astype(
            jnp.float32
        )
        block, block_decay, leading, found = combine(
            block, block_decay, other, other_decay, leading, upper
        )
        found_all.append(found)
    first = block if first is None else first
    return (jnp.stack(found_all, axis=0), first)


def local(
    xbc_in, conv_weight, conv_bias, dt_raw, decay_rate, skip, level_table, group_class, cotangent
):
    length = xbc_in.shape[0]
    taps = conv_weight.shape[0]
    heads = dt_raw.shape[1]
    inner = cotangent.shape[1]
    head_dim = inner // heads
    state_dim = (xbc_in.shape[1] - inner) // 2
    classes = level_table.shape[0]
    levels = level_table.shape[1]
    groups = group_class.shape[0]
    group_len = length // groups
    edge_part = shifted(xbc_in[length - taps + 1 :], "seq", 1)
    window = jnp.concatenate([edge_part, xbc_in], axis=0)
    preact = conv_forward(window, conv_weight, conv_bias, length)
    x_act, b_key, c_query = split_act(preact, heads, head_dim, state_dim)
    log_decay = -decay_rate[None, :] * jax.nn.softplus(dt_raw)
    grad_out = cotangent.reshape(length, heads, head_dim)
    picked = (group_class[:, None] == jnp.arange(classes, dtype=jnp.int32)[None, :]).astype(
        jnp.float32
    )
    weight_rows = exact("gk,klh->glh", picked, level_table)
    x_groups = x_act.reshape(groups, group_len, heads, head_dim)
    c_groups = c_query.reshape(groups, group_len, state_dim)
    grad_groups = grad_out.reshape(groups, group_len, heads, head_dim)
    b_groups = b_key.reshape(groups, group_len, state_dim)
    states, cumuls = jax.vmap(group_state_of)(
        x_groups, b_groups, log_decay.reshape(groups, group_len, heads)
    )
    totals = cumuls[:, -1]
    dev_decay = jnp.sum(totals, axis=0)
    later = dev_decay[None, :] - jnp.cumsum(totals, axis=0)
    dev_state = jnp.sum(jnp.exp(later)[:, :, None, None] * states, axis=0)
    devices = lax.axis_size("seq")
    depth = devices.bit_length() - 1
    myself = lax.axis_index("seq")
    chunks = 2 if heads % 2 == 0 else 1
    width = heads // chunks
    pieces = [
        exchange(dev_state[k * width : (k + 1) * width], dev_decay[k * width : (k + 1) * width], depth, myself)
        for k in range(chunks)
    ]
    cross = jnp.concatenate([piece for piece, _ in pieces], axis=1)
    late_cotangent = lax.optimization_barrier((cotangent, pieces[0][1]))[0]
    grad_groups = late_cotangent.reshape(groups, group_len, heads, head_dim)
    y_inner, grad_inner, level_zero = jax.vmap(local_group)(
        x_groups, b_groups, c_groups, cumuls, grad_groups, weight_rows[:, 0]
    )
    low_levels = groups.bit_length() - 1
    local_ids = jnp.arange(groups, dtype=jnp.int32)
    differ = jnp.bitwise_xor(local_ids[:, None], local_ids[None, :])
    lower = local_ids[:, None] > local_ids[None, :]
    slot_of = jnp.zeros((groups, groups), jnp.int32)
    onehot = (
        (slot_of[:, :, None] == jnp.arange(low_levels, dtype=jnp.int32)[None, None, :])
        & lower[:, :, None]
    ).astype(jnp.float32)
    before = jnp.cumsum(totals, axis=0) - totals
    gap = before[:, None, :] - before[None, :, :] - totals[None, :, :]
    below = lower[:, :, None]
    fade_pairs = jnp.where(below, jnp.exp(jnp.where(below, gap, 0.0)), 0.0)
    local_weight = exact("cds,csh->cdh", onehot, weight_rows[:, 1 : 1 + low_levels]) * fade_pairs
    lead_fade = jnp.exp(before)
    cross_weight = weight_rows[:, 1 + low_levels : 1 + low_levels + depth] * lead_fade[:, None, :]
    terms = [local_weight[:, d, :, None, None] * states[d][None] for d in range(groups)]
    terms += [cross_weight[:, l, :, None, None] * cross[l][None] for l in range(depth)]
    mixed = sum(terms[1:], terms[0]).astype(jnp.bfloat16)
    scaled = jnp.exp(cumuls) / state_dim
    query_faded = (c_groups[:, :, None, :] * scaled[:, :, :, None]).astype(jnp.bfloat16)
    y_cross = contract("cthn,chnp->cthp", query_faded, mixed)
    backed = contract("chnp,cthp->cthn", mixed, grad_groups)
    grad_cross = jnp.sum(backed * scaled[:, :, :, None], axis=2)
    gram = contract("cthn,cthp->chnp", query_faded, grad_groups)
    inner_pairs = jnp.sum(states[None] * gram[:, None], axis=(3, 4))
    level_local = exact("cds,cdh->csh", onehot, fade_pairs * inner_pairs)
    level_cross = lead_fade[:, None, :] * jnp.sum(cross[None] * gram[:, None], axis=(3, 4))
    level_rest = jnp.concatenate(
        [
            level_local,
            level_cross,
            jnp.zeros((groups, levels - 1 - low_levels - depth, heads), jnp.float32),
        ],
        axis=1,
    )
    grads = exact("ck,clh->klh", picked, level_rest)
    ssm_out = (
        (y_inner + y_cross + skip[None, None, :, None] * x_groups)
        .astype(jnp.bfloat16)
        .reshape(length, inner)
    )
    grad_query = (grad_inner + grad_cross).reshape(length, state_dim)
    after_rows = shifted(grad_query[: taps - 1], "seq", -1)
    extended = jnp.concatenate([grad_query, after_rows], axis=0)
    query_taps = conv_weight[:, inner + state_dim :]
    grad_c_in = jnp.zeros((length, state_dim), jnp.float32)
    for offset in range(taps):
        lagged = taps - 1 - offset
        grad_c_in = grad_c_in + query_taps[offset][None, :] * extended[lagged : lagged + length]
    grad_first = exact("gk,gh->kh", picked, level_zero)
    local_grads = jnp.concatenate([grad_first[:, None, :], grads], axis=1)
    summed = all_sum(local_grads, "seq")
    level_update = level_table + summed / math.sqrt(length * devices)
    return (ssm_out, grad_c_in, level_update)


def solution(mesh):
    placed = (
        P(("grp", "seq"), None),
        P(),
        P(),
        P(("grp", "seq"), None),
        P(),
        P(),
        P(),
        P(("grp", "seq")),
        P(("grp", "seq"), None),
    )
    return jax.shard_map(
        local,
        mesh=mesh,
        in_specs=placed,
        out_specs=(P(("grp", "seq"), None), P(("grp", "seq"), None), P("grp", None, None)),
        check_vma=False,
    )
```

```python
import math

import jax
import jax.numpy as jnp
from jax import lax
from jax.sharding import PartitionSpec as P


def shifted(value, axis, steps):
    count = lax.axis_size(axis)
    leading, last = (max(0, -steps), min(count, count - steps))
    return lax.ppermute(value, axis, [(source, source + steps) for source in range(leading, last)])


def from_partner(value, axis, distance):
    mask = 2**distance
    pairs = [(source, source ^ mask) for source in range(lax.axis_size(axis))]
    return lax.ppermute(value, axis, pairs)


def upward(value, axis, distance):
    mask = 2**distance
    count = lax.axis_size(axis)
    pairs = [(source, source | mask) for source in range(count) if not source & mask]
    return lax.ppermute(value, axis, pairs)


def all_sum(value, axis):
    for distance in range(lax.axis_size(axis).bit_length() - 1):
        value = value + from_partner(value, axis, distance)
    return value


def contract(form, left, right):
    return jnp.einsum(form, left, right, preferred_element_type=jnp.float32)


def exact(form, left, right):
    return jnp.einsum(form, left, right, precision=lax.Precision.HIGHEST)


def conv_forward(window, conv_weight, conv_bias, length):
    result = jnp.zeros((length, window.shape[1]), jnp.float32) + conv_bias[None, :]
    for offset in range(conv_weight.shape[0]):
        result = (
            result
            + window[offset : offset + length].astype(jnp.float32) * conv_weight[offset][None, :]
        )
    return result


def split_act(preact, heads, head_dim, state_dim):
    length = preact.shape[0]
    inner = heads * head_dim
    x_act = jax.nn.silu(preact[:, :inner]).astype(jnp.bfloat16).reshape(length, heads, head_dim)
    b_key = preact[:, inner : inner + state_dim].astype(jnp.bfloat16)
    c_query = preact[:, inner + state_dim :].astype(jnp.bfloat16)
    return (x_act, b_key, c_query)


def group_state_of(x_part, b_part, decay_part):
    cumul = jnp.cumsum(decay_part, axis=0)
    x_faded = (x_part * jnp.exp(cumul[-1][None, :] - cumul)[:, :, None]).astype(jnp.bfloat16)
    group_state = contract("sn,shp->hnp", b_part, x_faded)
    return (group_state, cumul)


def local_group(x_part, b_part, c_part, cumul, grad_part, weight_zero):
    length = x_part.shape[0]
    state_dim = b_part.shape[1]
    scores = jnp.dot(c_part, b_part.T, preferred_element_type=jnp.float32)
    causal = (jnp.arange(length)[:, None] >= jnp.arange(length)[None, :])[None]
    across = jnp.transpose(cumul)
    spread = across[:, :, None] - across[:, None, :]
    fading = jnp.where(causal, jnp.exp(jnp.where(causal, spread, 0.0)), 0.0)
    basic = fading * scores[None] / state_dim
    intra = (weight_zero[:, None, None] * basic).astype(jnp.bfloat16)
    y_inner = contract("hts,shp->thp", intra, x_part)
    products = contract("thp,shp->hts", grad_part, x_part)
    grad_weight = (
        jnp.sum(weight_zero[:, None, None] * fading * products, axis=0) / state_dim
    ).astype(jnp.bfloat16)
    grad_inner = jnp.dot(grad_weight, b_part, preferred_element_type=jnp.float32)
    level_zero = jnp.sum(basic * products, axis=(1, 2))
    return (y_inner, grad_inner, level_zero)


def combine(block, block_decay, other, other_decay, leading, upper):
    grown = upper[..., None, None]
    found = grown * jnp.exp(leading)[..., None, None] * other
    joined = grown * (other * jnp.exp(block_decay)[..., None, None] + block) + (1.0 - grown) * (
        block * jnp.exp(other_decay)[..., None, None] + other
    )
    return (joined, block_decay + other_decay, leading + upper * other_decay, found)


def relay(value, axis, bit_pos):
    half = 2**bit_pos
    step = half // 2
    first = lax.ppermute(value, axis, [(source, source + step) for source in range(half - step, half)])
    second = lax.ppermute(first, axis, [(source, source + step) for source in range(half, half + step)])
    return first + second


def exchange(block, block_decay, depth, myself):
    leading = jnp.zeros_like(block_decay)
    found_all = []
    first = None
    for bit_pos in range(depth):
        if bit_pos == depth - 1:
            if bit_pos == 0:
                sent = upward(block.astype(jnp.bfloat16), "seq", bit_pos)
            else:
                sent = relay(block.astype(jnp.bfloat16), "seq", bit_pos)
            other, other_decay = (sent.astype(jnp.float32), jnp.zeros_like(block_decay))
        else:
            sent, other_decay = from_partner((block.astype(jnp.bfloat16), block_decay), "seq", bit_pos)
            other = sent.astype(jnp.float32)
        first = sent if bit_pos < max(depth - 1, 1) else first
        upper = jnp.zeros_like(block_decay) + (jnp.right_shift(myself, bit_pos) & 1).astype(
            jnp.float32
        )
        block, block_decay, leading, found = combine(
            block, block_decay, other, other_decay, leading, upper
        )
        found_all.append(found)
    first = block if first is None else first
    return (jnp.stack(found_all, axis=0), first)


def local(
    xbc_in, conv_weight, conv_bias, dt_raw, decay_rate, skip, level_table, group_class, cotangent
):
    length = xbc_in.shape[0]
    taps = conv_weight.shape[0]
    heads = dt_raw.shape[1]
    inner = cotangent.shape[1]
    head_dim = inner // heads
    state_dim = (xbc_in.shape[1] - inner) // 2
    classes = level_table.shape[0]
    levels = level_table.shape[1]
    groups = group_class.shape[0]
    group_len = length // groups
    edge_part = shifted(xbc_in[length - taps + 1 :], "seq", 1)
    window = jnp.concatenate([edge_part, xbc_in], axis=0)
    preact = conv_forward(window, conv_weight, conv_bias, length)
    x_act, b_key, c_query = split_act(preact, heads, head_dim, state_dim)
    log_decay = -decay_rate[None, :] * jax.nn.softplus(dt_raw)
    grad_out = cotangent.reshape(length, heads, head_dim)
    picked = (group_class[:, None] == jnp.arange(classes, dtype=jnp.int32)[None, :]).astype(
        jnp.float32
    )
    weight_rows = exact("gk,klh->glh", picked, level_table)
    x_groups = x_act.reshape(groups, group_len, heads, head_dim)
    c_groups = c_query.reshape(groups, group_len, state_dim)
    grad_groups = grad_out.reshape(groups, group_len, heads, head_dim)
    b_groups = b_key.reshape(groups, group_len, state_dim)
    states, cumuls = jax.vmap(group_state_of)(
        x_groups, b_groups, log_decay.reshape(groups, group_len, heads)
    )
    totals = cumuls[:, -1]
    dev_decay = jnp.sum(totals, axis=0)
    later = dev_decay[None, :] - jnp.cumsum(totals, axis=0)
    dev_state = jnp.sum(jnp.exp(later)[:, :, None, None] * states, axis=0)
    devices = lax.axis_size("seq")
    depth = devices.bit_length() - 1
    myself = lax.axis_index("seq")
    chunks = 2 if heads % 2 == 0 else 1
    width = heads // chunks
    pieces = [
        exchange(dev_state[k * width : (k + 1) * width], dev_decay[k * width : (k + 1) * width], depth, myself)
        for k in range(chunks)
    ]
    cross = jnp.concatenate([piece for piece, _ in pieces], axis=1)
    late_cotangent = lax.optimization_barrier((cotangent, pieces[-1][1]))[0]
    grad_groups = late_cotangent.reshape(groups, group_len, heads, head_dim)
    y_inner, grad_inner, level_zero = jax.vmap(local_group)(
        x_groups, b_groups, c_groups, cumuls, grad_groups, weight_rows[:, 0]
    )
    low_levels = groups.bit_length() - 1
    local_ids = jnp.arange(groups, dtype=jnp.int32)
    differ = jnp.bitwise_xor(local_ids[:, None], local_ids[None, :])
    lower = local_ids[:, None] > local_ids[None, :]
    slot_of = jnp.zeros((groups, groups), jnp.int32)
    onehot = (
        (slot_of[:, :, None] == jnp.arange(low_levels, dtype=jnp.int32)[None, None, :])
        & lower[:, :, None]
    ).astype(jnp.float32)
    before = jnp.cumsum(totals, axis=0) - totals
    gap = before[:, None, :] - before[None, :, :] - totals[None, :, :]
    below = lower[:, :, None]
    fade_pairs = jnp.where(below, jnp.exp(jnp.where(below, gap, 0.0)), 0.0)
    local_weight = exact("cds,csh->cdh", onehot, weight_rows[:, 1 : 1 + low_levels]) * fade_pairs
    lead_fade = jnp.exp(before)
    cross_weight = weight_rows[:, 1 + low_levels : 1 + low_levels + depth] * lead_fade[:, None, :]
    terms = [local_weight[:, d, :, None, None] * states[d][None] for d in range(groups)]
    terms += [cross_weight[:, l, :, None, None] * cross[l][None] for l in range(depth)]
    mixed = sum(terms[1:], terms[0]).astype(jnp.bfloat16)
    scaled = jnp.exp(cumuls) / state_dim
    query_faded = (c_groups[:, :, None, :] * scaled[:, :, :, None]).astype(jnp.bfloat16)
    y_cross = contract("cthn,chnp->cthp", query_faded, mixed)
    backed = contract("chnp,cthp->cthn", mixed, grad_groups)
    grad_cross = jnp.sum(backed * scaled[:, :, :, None], axis=2)
    gram = contract("cthn,cthp->chnp", query_faded, grad_groups)
    inner_pairs = jnp.sum(states[None] * gram[:, None], axis=(3, 4))
    level_local = exact("cds,cdh->csh", onehot, fade_pairs * inner_pairs)
    level_cross = lead_fade[:, None, :] * jnp.sum(cross[None] * gram[:, None], axis=(3, 4))
    level_rest = jnp.concatenate(
        [
            level_local,
            level_cross,
            jnp.zeros((groups, levels - 1 - low_levels - depth, heads), jnp.float32),
        ],
        axis=1,
    )
    grads = exact("ck,clh->klh", picked, level_rest)
    ssm_out = (
        (y_inner + y_cross + skip[None, None, :, None] * x_groups)
        .astype(jnp.bfloat16)
        .reshape(length, inner)
    )
    grad_query = (grad_inner + grad_cross).reshape(length, state_dim)
    after_rows = shifted(grad_query[: taps - 1], "seq", -1)
    extended = jnp.concatenate([grad_query, after_rows], axis=0)
    query_taps = conv_weight[:, inner + state_dim :]
    grad_c_in = jnp.zeros((length, state_dim), jnp.float32)
    for offset in range(taps):
        lagged = taps - 1 - offset
        grad_c_in = grad_c_in + query_taps[offset][None, :] * extended[lagged : lagged + length]
    grad_first = exact("gk,gh->kh", picked, level_zero)
    local_grads = jnp.concatenate([grad_first[:, None, :], grads], axis=1)
    summed = all_sum(local_grads, "seq")
    level_update = level_table + summed / math.sqrt(length * devices)
    return (ssm_out, grad_c_in, level_update)


def solution(mesh):
    placed = (
        P(("grp", "seq"), None),
        P(),
        P(),
        P(("grp", "seq"), None),
        P(),
        P(),
        P(),
        P(("grp", "seq")),
        P(("grp", "seq"), None),
    )
    return jax.shard_map(
        local,
        mesh=mesh,
        in_specs=placed,
        out_specs=(P(("grp", "seq"), None), P(("grp", "seq"), None), P("grp", None, None)),
        check_vma=False,
    )
```

```python
import math

import jax
import jax.numpy as jnp
from jax import lax
from jax.sharding import PartitionSpec as P


def shifted(value, axis, steps):
    count = lax.axis_size(axis)
    leading, last = (max(0, -steps), min(count, count - steps))
    return lax.ppermute(value, axis, [(source, source + steps) for source in range(leading, last)])


def from_partner(value, axis, distance):
    mask = 2**distance
    pairs = [(source, source ^ mask) for source in range(lax.axis_size(axis))]
    return lax.ppermute(value, axis, pairs)


def upward(value, axis, distance):
    mask = 2**distance
    count = lax.axis_size(axis)
    pairs = [(source, source | mask) for source in range(count) if not source & mask]
    return lax.ppermute(value, axis, pairs)


def all_sum(value, axis):
    for distance in range(lax.axis_size(axis).bit_length() - 1):
        value = value + from_partner(value, axis, distance)
    return value


def contract(form, left, right):
    return jnp.einsum(form, left, right, preferred_element_type=jnp.float32)


def exact(form, left, right):
    return jnp.einsum(form, left, right, precision=lax.Precision.HIGHEST)


def conv_forward(window, conv_weight, conv_bias, length):
    result = jnp.zeros((length, window.shape[1]), jnp.float32) + conv_bias[None, :]
    for offset in range(conv_weight.shape[0]):
        result = (
            result
            + window[offset : offset + length].astype(jnp.float32) * conv_weight[offset][None, :]
        )
    return result


def split_act(preact, heads, head_dim, state_dim):
    length = preact.shape[0]
    inner = heads * head_dim
    x_act = jax.nn.silu(preact[:, :inner]).astype(jnp.bfloat16).reshape(length, heads, head_dim)
    b_key = preact[:, inner : inner + state_dim].astype(jnp.bfloat16)
    c_query = preact[:, inner + state_dim :].astype(jnp.bfloat16)
    return (x_act, b_key, c_query)


def group_state_of(x_part, b_part, decay_part):
    cumul = jnp.cumsum(decay_part, axis=0)
    x_faded = (x_part * jnp.exp(cumul[-1][None, :] - cumul)[:, :, None]).astype(jnp.bfloat16)
    group_state = contract("sn,shp->hnp", b_part, x_faded)
    return (group_state, cumul)


def local_group(x_part, b_part, c_part, cumul, grad_part, weight_zero):
    length = x_part.shape[0]
    state_dim = b_part.shape[1]
    scores = jnp.dot(c_part, b_part.T, preferred_element_type=jnp.float32)
    causal = (jnp.arange(length)[:, None] >= jnp.arange(length)[None, :])[None]
    across = jnp.transpose(cumul)
    spread = across[:, :, None] - across[:, None, :]
    fading = jnp.where(causal, jnp.exp(jnp.where(causal, spread, 0.0)), 0.0)
    basic = fading * scores[None] / state_dim
    intra = (weight_zero[:, None, None] * basic).astype(jnp.bfloat16)
    y_inner = contract("hts,shp->thp", intra, x_part)
    products = contract("thp,shp->hts", grad_part, x_part)
    grad_weight = (
        jnp.sum(weight_zero[:, None, None] * fading * products, axis=0) / state_dim
    ).astype(jnp.bfloat16)
    grad_inner = jnp.dot(grad_weight, b_part, preferred_element_type=jnp.float32)
    level_zero = jnp.sum(basic * products, axis=(1, 2))
    return (y_inner, grad_inner, level_zero)


def combine(block, block_decay, other, other_decay, leading, upper):
    grown = upper[..., None, None]
    found = grown * jnp.exp(leading)[..., None, None] * other
    joined = grown * (other * jnp.exp(block_decay)[..., None, None] + block) + (1.0 - grown) * (
        block * jnp.exp(other_decay)[..., None, None] + other
    )
    return (joined, block_decay + other_decay, leading + upper * other_decay, found)


def relay(value, axis, bit_pos):
    half = 2**bit_pos
    step = half // 2
    first = lax.ppermute(value, axis, [(source, source + step) for source in range(half - step, half)])
    second = lax.ppermute(first, axis, [(source, source + step) for source in range(half, half + step)])
    return first + second


def exchange(block, block_decay, depth, myself):
    leading = jnp.zeros_like(block_decay)
    found_all = []
    first = None
    for bit_pos in range(depth):
        if bit_pos == depth - 1:
            if bit_pos == 0:
                sent = upward(block.astype(jnp.bfloat16), "seq", bit_pos)
            else:
                sent = relay(block.astype(jnp.bfloat16), "seq", bit_pos)
            other, other_decay = (sent.astype(jnp.float32), jnp.zeros_like(block_decay))
        else:
            sent, other_decay = from_partner((block.astype(jnp.bfloat16), block_decay), "seq", bit_pos)
            other = sent.astype(jnp.float32)
        first = sent if first is None else first
        upper = jnp.zeros_like(block_decay) + (jnp.right_shift(myself, bit_pos) & 1).astype(
            jnp.float32
        )
        block, block_decay, leading, found = combine(
            block, block_decay, other, other_decay, leading, upper
        )
        found_all.append(found)
    first = block if first is None else first
    return (jnp.stack(found_all, axis=0), first)


def local(
    xbc_in, conv_weight, conv_bias, dt_raw, decay_rate, skip, level_table, group_class, cotangent
):
    length = xbc_in.shape[0]
    taps = conv_weight.shape[0]
    heads = dt_raw.shape[1]
    inner = cotangent.shape[1]
    head_dim = inner // heads
    state_dim = (xbc_in.shape[1] - inner) // 2
    classes = level_table.shape[0]
    levels = level_table.shape[1]
    groups = group_class.shape[0]
    group_len = length // groups
    edge_part = shifted(xbc_in[length - taps + 1 :], "seq", 1)
    window = jnp.concatenate([edge_part, xbc_in], axis=0)
    preact = conv_forward(window, conv_weight, conv_bias, length)
    x_act, b_key, c_query = split_act(preact, heads, head_dim, state_dim)
    log_decay = -decay_rate[None, :] * jax.nn.softplus(dt_raw)
    grad_out = cotangent.reshape(length, heads, head_dim)
    picked = (group_class[:, None] == jnp.arange(classes, dtype=jnp.int32)[None, :]).astype(
        jnp.float32
    )
    weight_rows = exact("gk,klh->glh", picked, level_table)
    x_groups = x_act.reshape(groups, group_len, heads, head_dim)
    c_groups = c_query.reshape(groups, group_len, state_dim)
    grad_groups = grad_out.reshape(groups, group_len, heads, head_dim)
    b_groups = b_key.reshape(groups, group_len, state_dim)
    states, cumuls = jax.vmap(group_state_of)(
        x_groups, b_groups, log_decay.reshape(groups, group_len, heads)
    )
    totals = cumuls[:, -1]
    dev_decay = jnp.sum(totals, axis=0)
    later = dev_decay[None, :] - jnp.cumsum(totals, axis=0)
    dev_state = jnp.sum(jnp.exp(later)[:, :, None, None] * states, axis=0)
    devices = lax.axis_size("seq")
    depth = devices.bit_length() - 1
    myself = lax.axis_index("seq")
    chunks = 2 if heads % 2 == 0 else 1
    width = heads // chunks
    pieces = [
        exchange(dev_state[k * width : (k + 1) * width], dev_decay[k * width : (k + 1) * width], depth, myself)
        for k in range(chunks)
    ]
    cross = jnp.concatenate([piece for piece, _ in pieces], axis=1)
    late_cotangent = lax.optimization_barrier((cotangent, pieces[0][1]))[0]
    grad_groups = late_cotangent.reshape(groups, group_len, heads, head_dim)
    y_inner, grad_inner, level_zero = jax.vmap(local_group)(
        x_groups, b_groups, c_groups, cumuls, grad_groups, weight_rows[:, 0]
    )
    low_levels = groups.bit_length() - 1
    local_ids = jnp.arange(groups, dtype=jnp.int32)
    differ = jnp.bitwise_xor(local_ids[:, None], local_ids[None, :])
    lower = local_ids[:, None] > local_ids[None, :]
    slot_of = jnp.zeros((groups, groups), jnp.int32)
    onehot = (
        (slot_of[:, :, None] == jnp.arange(low_levels, dtype=jnp.int32)[None, None, :])
        & lower[:, :, None]
    ).astype(jnp.float32)
    before = jnp.cumsum(totals, axis=0) - totals
    gap = before[:, None, :] - before[None, :, :] - totals[None, :, :]
    below = lower[:, :, None]
    fade_pairs = jnp.where(below, jnp.exp(jnp.where(below, gap, 0.0)), 0.0)
    local_weight = exact("cds,csh->cdh", onehot, weight_rows[:, 1 : 1 + low_levels]) * fade_pairs
    lead_fade = jnp.exp(before)
    cross_weight = weight_rows[:, 1 + low_levels : 1 + low_levels + depth] * lead_fade[:, None, :]
    terms = [local_weight[:, d, :, None, None] * states[d][None] for d in range(groups)]
    terms += [cross_weight[:, l, :, None, None] * cross[l][None] for l in range(depth)]
    mixed = sum(terms[1:], terms[0]).astype(jnp.bfloat16)
    scaled = jnp.exp(cumuls) / state_dim
    query_faded = (c_groups[:, :, None, :] * scaled[:, :, :, None]).astype(jnp.bfloat16)
    y_cross = contract("cthn,chnp->cthp", query_faded, mixed)
    backed = contract("chnp,cthp->cthn", mixed, grad_groups)
    grad_cross = jnp.sum(backed * scaled[:, :, :, None], axis=2)
    gram = contract("cthn,cthp->chnp", query_faded, grad_groups)
    inner_pairs = jnp.sum(states[None] * gram[:, None], axis=(3, 4))
    level_local = exact("cds,cdh->csh", onehot, fade_pairs * inner_pairs)
    level_cross = lead_fade[:, None, :] * jnp.sum(cross[None] * gram[:, None], axis=(3, 4))
    level_rest = jnp.concatenate(
        [
            level_local,
            level_cross,
            jnp.zeros((groups, levels - 1 - low_levels - depth, heads), jnp.float32),
        ],
        axis=1,
    )
    grads = exact("ck,clh->klh", picked, level_rest)
    ssm_out = (
        (y_inner + y_cross + skip[None, None, :, None] * x_groups)
        .astype(jnp.bfloat16)
        .reshape(length, inner)
    )
    grad_query = (grad_inner + grad_cross).reshape(length, state_dim)
    after_rows = shifted(grad_query[: taps - 1], "seq", -1)
    extended = jnp.concatenate([grad_query, after_rows], axis=0)
    query_taps = conv_weight[:, inner + state_dim :]
    grad_c_in = jnp.zeros((length, state_dim), jnp.float32)
    for offset in range(taps):
        lagged = taps - 1 - offset
        grad_c_in = grad_c_in + query_taps[offset][None, :] * extended[lagged : lagged + length]
    grad_first = exact("gk,gh->kh", picked, level_zero)
    local_grads = jnp.concatenate([grad_first[:, None, :], grads], axis=1)
    summed = lax.psum(local_grads, "seq")
    level_update = level_table + summed / math.sqrt(length * devices)
    return (ssm_out, grad_c_in, level_update)


def solution(mesh):
    placed = (
        P(("grp", "seq"), None),
        P(),
        P(),
        P(("grp", "seq"), None),
        P(),
        P(),
        P(),
        P(("grp", "seq")),
        P(("grp", "seq"), None),
    )
    return jax.shard_map(
        local,
        mesh=mesh,
        in_specs=placed,
        out_specs=(P(("grp", "seq"), None), P(("grp", "seq"), None), P("grp", None, None)),
        check_vma=False,
    )
```

```python
import math

import jax
import jax.numpy as jnp
from jax import lax
from jax.sharding import PartitionSpec as P


def shifted(value, axis, steps):
    count = lax.axis_size(axis)
    leading, last = (max(0, -steps), min(count, count - steps))
    return lax.ppermute(value, axis, [(source, source + steps) for source in range(leading, last)])


def from_partner(value, axis, distance):
    mask = 2**distance
    pairs = [(source, source ^ mask) for source in range(lax.axis_size(axis))]
    return lax.ppermute(value, axis, pairs)


def upward(value, axis, distance):
    mask = 2**distance
    count = lax.axis_size(axis)
    pairs = [(source, source | mask) for source in range(count) if not source & mask]
    return lax.ppermute(value, axis, pairs)


def all_sum(value, axis):
    for distance in range(lax.axis_size(axis).bit_length() - 1):
        value = value + from_partner(value, axis, distance)
    return value


def contract(form, left, right):
    return jnp.einsum(form, left, right, preferred_element_type=jnp.float32)


def exact(form, left, right):
    return jnp.einsum(form, left, right, precision=lax.Precision.HIGHEST)


def conv_forward(window, conv_weight, conv_bias, length):
    result = jnp.zeros((length, window.shape[1]), jnp.float32) + conv_bias[None, :]
    for offset in range(conv_weight.shape[0]):
        result = (
            result
            + window[offset : offset + length].astype(jnp.float32) * conv_weight[offset][None, :]
        )
    return result


def split_act(preact, heads, head_dim, state_dim):
    length = preact.shape[0]
    inner = heads * head_dim
    x_act = jax.nn.silu(preact[:, :inner]).astype(jnp.bfloat16).reshape(length, heads, head_dim)
    b_key = preact[:, inner : inner + state_dim].astype(jnp.bfloat16)
    c_query = preact[:, inner + state_dim :].astype(jnp.bfloat16)
    return (x_act, b_key, c_query)


def group_state_of(x_part, b_part, decay_part):
    cumul = jnp.cumsum(decay_part, axis=0)
    x_faded = (x_part * jnp.exp(cumul[-1][None, :] - cumul)[:, :, None]).astype(jnp.bfloat16)
    group_state = contract("sn,shp->hnp", b_part, x_faded)
    return (group_state, cumul)


def local_group(x_part, b_part, c_part, cumul, grad_part, weight_zero):
    length = x_part.shape[0]
    state_dim = b_part.shape[1]
    scores = jnp.dot(c_part, b_part.T, preferred_element_type=jnp.float32)
    causal = (jnp.arange(length)[:, None] >= jnp.arange(length)[None, :])[None]
    across = jnp.transpose(cumul)
    spread = across[:, :, None] - across[:, None, :]
    fading = jnp.where(causal, jnp.exp(jnp.where(causal, spread, 0.0)), 0.0)
    basic = fading * scores[None] / state_dim
    intra = (weight_zero[:, None, None] * basic).astype(jnp.bfloat16)
    y_inner = contract("hts,shp->thp", intra, x_part)
    products = contract("thp,shp->hts", grad_part, x_part)
    grad_weight = (
        jnp.sum(weight_zero[:, None, None] * fading * products, axis=0) / state_dim
    ).astype(jnp.bfloat16)
    grad_inner = jnp.dot(grad_weight, b_part, preferred_element_type=jnp.float32)
    level_zero = jnp.sum(basic * products, axis=(1, 2))
    return (y_inner, grad_inner, level_zero)


def combine(block, block_decay, other, other_decay, leading, upper):
    grown = upper[..., None, None]
    found = grown * jnp.exp(leading)[..., None, None] * other
    joined = grown * (other * jnp.exp(block_decay)[..., None, None] + block) + (1.0 - grown) * (
        block * jnp.exp(other_decay)[..., None, None] + other
    )
    return (joined, block_decay + other_decay, leading + upper * other_decay, found)


def relay(value, axis, bit_pos):
    half = 2**bit_pos
    step = half // 2
    parts = 2 if value.shape[0] % 2 == 0 else 1
    size = value.shape[0] // parts
    received = []
    for index in range(parts):
        piece = value[index * size : (index + 1) * size]
        first = lax.ppermute(piece, axis, [(source, source + step) for source in range(half - step, half)])
        second = lax.ppermute(first, axis, [(source, source + step) for source in range(half, half + step)])
        received.append(first + second)
    return jnp.concatenate(received, axis=0)


def exchange(block, block_decay, depth, myself):
    leading = jnp.zeros_like(block_decay)
    found_all = []
    first = None
    for bit_pos in range(depth):
        if bit_pos == depth - 1:
            if bit_pos == 0:
                sent = upward(block.astype(jnp.bfloat16), "seq", bit_pos)
            else:
                sent = relay(block.astype(jnp.bfloat16), "seq", bit_pos)
            other, other_decay = (sent.astype(jnp.float32), jnp.zeros_like(block_decay))
        else:
            sent, other_decay = from_partner((block.astype(jnp.bfloat16), block_decay), "seq", bit_pos)
            other = sent.astype(jnp.float32)
        first = sent if first is None else first
        upper = jnp.zeros_like(block_decay) + (jnp.right_shift(myself, bit_pos) & 1).astype(
            jnp.float32
        )
        block, block_decay, leading, found = combine(
            block, block_decay, other, other_decay, leading, upper
        )
        found_all.append(found)
    first = block if first is None else first
    return (jnp.stack(found_all, axis=0), first)


def local(
    xbc_in, conv_weight, conv_bias, dt_raw, decay_rate, skip, level_table, group_class, cotangent
):
    length = xbc_in.shape[0]
    taps = conv_weight.shape[0]
    heads = dt_raw.shape[1]
    inner = cotangent.shape[1]
    head_dim = inner // heads
    state_dim = (xbc_in.shape[1] - inner) // 2
    classes = level_table.shape[0]
    levels = level_table.shape[1]
    groups = group_class.shape[0]
    group_len = length // groups
    edge_part = shifted(xbc_in[length - taps + 1 :], "seq", 1)
    window = jnp.concatenate([edge_part, xbc_in], axis=0)
    preact = conv_forward(window, conv_weight, conv_bias, length)
    x_act, b_key, c_query = split_act(preact, heads, head_dim, state_dim)
    log_decay = -decay_rate[None, :] * jax.nn.softplus(dt_raw)
    grad_out = cotangent.reshape(length, heads, head_dim)
    picked = (group_class[:, None] == jnp.arange(classes, dtype=jnp.int32)[None, :]).astype(
        jnp.float32
    )
    weight_rows = exact("gk,klh->glh", picked, level_table)
    x_groups = x_act.reshape(groups, group_len, heads, head_dim)
    c_groups = c_query.reshape(groups, group_len, state_dim)
    grad_groups = grad_out.reshape(groups, group_len, heads, head_dim)
    b_groups = b_key.reshape(groups, group_len, state_dim)
    states, cumuls = jax.vmap(group_state_of)(
        x_groups, b_groups, log_decay.reshape(groups, group_len, heads)
    )
    totals = cumuls[:, -1]
    dev_decay = jnp.sum(totals, axis=0)
    later = dev_decay[None, :] - jnp.cumsum(totals, axis=0)
    dev_state = jnp.sum(jnp.exp(later)[:, :, None, None] * states, axis=0)
    devices = lax.axis_size("seq")
    depth = devices.bit_length() - 1
    myself = lax.axis_index("seq")
    chunks = 2 if heads % 2 == 0 else 1
    width = heads // chunks
    pieces = [
        exchange(dev_state[k * width : (k + 1) * width], dev_decay[k * width : (k + 1) * width], depth, myself)
        for k in range(chunks)
    ]
    cross = jnp.concatenate([piece for piece, _ in pieces], axis=1)
    late_cotangent = lax.optimization_barrier((cotangent, pieces[0][1]))[0]
    grad_groups = late_cotangent.reshape(groups, group_len, heads, head_dim)
    y_inner, grad_inner, level_zero = jax.vmap(local_group)(
        x_groups, b_groups, c_groups, cumuls, grad_groups, weight_rows[:, 0]
    )
    low_levels = groups.bit_length() - 1
    local_ids = jnp.arange(groups, dtype=jnp.int32)
    differ = jnp.bitwise_xor(local_ids[:, None], local_ids[None, :])
    lower = local_ids[:, None] > local_ids[None, :]
    slot_of = jnp.zeros((groups, groups), jnp.int32)
    onehot = (
        (slot_of[:, :, None] == jnp.arange(low_levels, dtype=jnp.int32)[None, None, :])
        & lower[:, :, None]
    ).astype(jnp.float32)
    before = jnp.cumsum(totals, axis=0) - totals
    gap = before[:, None, :] - before[None, :, :] - totals[None, :, :]
    below = lower[:, :, None]
    fade_pairs = jnp.where(below, jnp.exp(jnp.where(below, gap, 0.0)), 0.0)
    local_weight = exact("cds,csh->cdh", onehot, weight_rows[:, 1 : 1 + low_levels]) * fade_pairs
    lead_fade = jnp.exp(before)
    cross_weight = weight_rows[:, 1 + low_levels : 1 + low_levels + depth] * lead_fade[:, None, :]
    terms = [local_weight[:, d, :, None, None] * states[d][None] for d in range(groups)]
    terms += [cross_weight[:, l, :, None, None] * cross[l][None] for l in range(depth)]
    mixed = sum(terms[1:], terms[0]).astype(jnp.bfloat16)
    scaled = jnp.exp(cumuls) / state_dim
    query_faded = (c_groups[:, :, None, :] * scaled[:, :, :, None]).astype(jnp.bfloat16)
    y_cross = contract("cthn,chnp->cthp", query_faded, mixed)
    backed = contract("chnp,cthp->cthn", mixed, grad_groups)
    grad_cross = jnp.sum(backed * scaled[:, :, :, None], axis=2)
    gram = contract("cthn,cthp->chnp", query_faded, grad_groups)
    inner_pairs = jnp.sum(states[None] * gram[:, None], axis=(3, 4))
    level_local = exact("cds,cdh->csh", onehot, fade_pairs * inner_pairs)
    level_cross = lead_fade[:, None, :] * jnp.sum(cross[None] * gram[:, None], axis=(3, 4))
    level_rest = jnp.concatenate(
        [
            level_local,
            level_cross,
            jnp.zeros((groups, levels - 1 - low_levels - depth, heads), jnp.float32),
        ],
        axis=1,
    )
    grads = exact("ck,clh->klh", picked, level_rest)
    ssm_out = (
        (y_inner + y_cross + skip[None, None, :, None] * x_groups)
        .astype(jnp.bfloat16)
        .reshape(length, inner)
    )
    grad_query = (grad_inner + grad_cross).reshape(length, state_dim)
    after_rows = shifted(grad_query[: taps - 1], "seq", -1)
    extended = jnp.concatenate([grad_query, after_rows], axis=0)
    query_taps = conv_weight[:, inner + state_dim :]
    grad_c_in = jnp.zeros((length, state_dim), jnp.float32)
    for offset in range(taps):
        lagged = taps - 1 - offset
        grad_c_in = grad_c_in + query_taps[offset][None, :] * extended[lagged : lagged + length]
    grad_first = exact("gk,gh->kh", picked, level_zero)
    local_grads = jnp.concatenate([grad_first[:, None, :], grads], axis=1)
    summed = all_sum(local_grads, "seq")
    level_update = level_table + summed / math.sqrt(length * devices)
    return (ssm_out, grad_c_in, level_update)


def solution(mesh):
    placed = (
        P(("grp", "seq"), None),
        P(),
        P(),
        P(("grp", "seq"), None),
        P(),
        P(),
        P(),
        P(("grp", "seq")),
        P(("grp", "seq"), None),
    )
    return jax.shard_map(
        local,
        mesh=mesh,
        in_specs=placed,
        out_specs=(P(("grp", "seq"), None), P(("grp", "seq"), None), P("grp", None, None)),
        check_vma=False,
    )
```

```python
import math

import jax
import jax.numpy as jnp
from jax import lax
from jax.sharding import PartitionSpec as P


def shifted(value, axis, steps):
    count = lax.axis_size(axis)
    leading, last = (max(0, -steps), min(count, count - steps))
    return lax.ppermute(value, axis, [(source, source + steps) for source in range(leading, last)])


def from_partner(value, axis, distance):
    mask = 2**distance
    pairs = [(source, source ^ mask) for source in range(lax.axis_size(axis))]
    return lax.ppermute(value, axis, pairs)


def upward(value, axis, distance):
    mask = 2**distance
    count = lax.axis_size(axis)
    pairs = [(source, source | mask) for source in range(count) if not source & mask]
    return lax.ppermute(value, axis, pairs)


def all_sum(value, axis):
    for distance in range(lax.axis_size(axis).bit_length() - 1):
        value = value + from_partner(value, axis, distance)
    return value


def contract(form, left, right):
    return jnp.einsum(form, left, right, preferred_element_type=jnp.float32)


def exact(form, left, right):
    return jnp.einsum(form, left, right, precision=lax.Precision.HIGHEST)


def conv_forward(window, conv_weight, conv_bias, length):
    result = jnp.zeros((length, window.shape[1]), jnp.float32) + conv_bias[None, :]
    for offset in range(conv_weight.shape[0]):
        result = (
            result
            + window[offset : offset + length].astype(jnp.float32) * conv_weight[offset][None, :]
        )
    return result


def split_act(preact, heads, head_dim, state_dim):
    length = preact.shape[0]
    inner = heads * head_dim
    x_act = jax.nn.silu(preact[:, :inner]).astype(jnp.bfloat16).reshape(length, heads, head_dim)
    b_key = preact[:, inner : inner + state_dim].astype(jnp.bfloat16)
    c_query = preact[:, inner + state_dim :].astype(jnp.bfloat16)
    return (x_act, b_key, c_query)


def group_state_of(x_part, b_part, decay_part):
    cumul = jnp.cumsum(decay_part, axis=0)
    x_faded = (x_part * jnp.exp(cumul[-1][None, :] - cumul)[:, :, None]).astype(jnp.bfloat16)
    group_state = contract("sn,shp->hnp", b_part, x_faded)
    return (group_state, cumul)


def local_group(x_part, b_part, c_part, cumul, grad_part, weight_zero):
    length = x_part.shape[0]
    state_dim = b_part.shape[1]
    scores = jnp.dot(c_part, b_part.T, preferred_element_type=jnp.float32)
    causal = (jnp.arange(length)[:, None] >= jnp.arange(length)[None, :])[None]
    across = jnp.transpose(cumul)
    spread = across[:, :, None] - across[:, None, :]
    fading = jnp.where(causal, jnp.exp(jnp.where(causal, spread, 0.0)), 0.0)
    basic = fading * scores[None] / state_dim
    intra = (weight_zero[:, None, None] * basic).astype(jnp.bfloat16)
    y_inner = contract("hts,shp->thp", intra, x_part)
    products = contract("thp,shp->hts", grad_part, x_part)
    grad_weight = (
        jnp.sum(weight_zero[:, None, None] * fading * products, axis=0) / state_dim
    ).astype(jnp.bfloat16)
    grad_inner = jnp.dot(grad_weight, b_part, preferred_element_type=jnp.float32)
    level_zero = jnp.sum(basic * products, axis=(1, 2))
    return (y_inner, grad_inner, level_zero)


def combine(block, block_decay, other, other_decay, leading, upper):
    grown = upper[..., None, None]
    found = grown * jnp.exp(leading)[..., None, None] * other
    joined = grown * (other * jnp.exp(block_decay)[..., None, None] + block) + (1.0 - grown) * (
        block * jnp.exp(other_decay)[..., None, None] + other
    )
    return (joined, block_decay + other_decay, leading + upper * other_decay, found)


def relay(value, axis, bit_pos):
    half = 2**bit_pos
    step = half // 2
    parts = 2 if value.shape[0] % 2 == 0 else 1
    size = value.shape[0] // parts
    received = []
    for index in range(parts):
        piece = value[index * size : (index + 1) * size]
        first = lax.ppermute(piece, axis, [(source, source + step) for source in range(half - step, half)])
        second = lax.ppermute(first, axis, [(source, source + step) for source in range(half, half + step)])
        received.append(first + second)
    return jnp.concatenate(received, axis=0)


def exchange(block, block_decay, depth, myself):
    leading = jnp.zeros_like(block_decay)
    found_all = []
    first = None
    for bit_pos in range(depth):
        if bit_pos == depth - 1:
            if bit_pos == 0:
                sent = upward(block.astype(jnp.bfloat16), "seq", bit_pos)
            else:
                sent = relay(block.astype(jnp.bfloat16), "seq", bit_pos)
            other, other_decay = (sent.astype(jnp.float32), jnp.zeros_like(block_decay))
        else:
            sent, other_decay = from_partner((block.astype(jnp.bfloat16), block_decay), "seq", bit_pos)
            other = sent.astype(jnp.float32)
        first = sent if first is None else first
        upper = jnp.zeros_like(block_decay) + (jnp.right_shift(myself, bit_pos) & 1).astype(
            jnp.float32
        )
        block, block_decay, leading, found = combine(
            block, block_decay, other, other_decay, leading, upper
        )
        found_all.append(found)
    first = block if first is None else first
    return (jnp.stack(found_all, axis=0), first)


def local(
    xbc_in, conv_weight, conv_bias, dt_raw, decay_rate, skip, level_table, group_class, cotangent
):
    length = xbc_in.shape[0]
    taps = conv_weight.shape[0]
    heads = dt_raw.shape[1]
    inner = cotangent.shape[1]
    head_dim = inner // heads
    state_dim = (xbc_in.shape[1] - inner) // 2
    classes = level_table.shape[0]
    levels = level_table.shape[1]
    groups = group_class.shape[0]
    group_len = length // groups
    edge_part = shifted(xbc_in[length - taps + 1 :], "seq", 1)
    window = jnp.concatenate([edge_part, xbc_in], axis=0)
    preact = conv_forward(window, conv_weight, conv_bias, length)
    x_act, b_key, c_query = split_act(preact, heads, head_dim, state_dim)
    log_decay = -decay_rate[None, :] * jax.nn.softplus(dt_raw)
    grad_out = cotangent.reshape(length, heads, head_dim)
    picked = (group_class[:, None] == jnp.arange(classes, dtype=jnp.int32)[None, :]).astype(
        jnp.float32
    )
    weight_rows = exact("gk,klh->glh", picked, level_table)
    x_groups = x_act.reshape(groups, group_len, heads, head_dim)
    c_groups = c_query.reshape(groups, group_len, state_dim)
    grad_groups = grad_out.reshape(groups, group_len, heads, head_dim)
    b_groups = b_key.reshape(groups, group_len, state_dim)
    states, cumuls = jax.vmap(group_state_of)(
        x_groups, b_groups, log_decay.reshape(groups, group_len, heads)
    )
    totals = cumuls[:, -1]
    dev_decay = jnp.sum(totals, axis=0)
    later = dev_decay[None, :] - jnp.cumsum(totals, axis=0)
    dev_state = jnp.sum(jnp.exp(later)[:, :, None, None] * states, axis=0)
    devices = lax.axis_size("seq")
    depth = devices.bit_length() - 1
    myself = lax.axis_index("seq")
    chunks = 2 if heads % 2 == 0 else 1
    width = heads // chunks
    pieces = [
        exchange(dev_state[k * width : (k + 1) * width], dev_decay[k * width : (k + 1) * width], depth, myself)
        for k in range(chunks)
    ]
    cross = jnp.concatenate([piece for piece, _ in pieces], axis=1)
    late_cotangent = lax.optimization_barrier((cotangent, pieces[0][1]))[0]
    grad_groups = late_cotangent.reshape(groups, group_len, heads, head_dim)
    y_inner, grad_inner, level_zero = jax.vmap(local_group)(
        x_groups, b_groups, c_groups, cumuls, grad_groups, weight_rows[:, 0]
    )
    low_levels = groups.bit_length() - 1
    local_ids = jnp.arange(groups, dtype=jnp.int32)
    differ = jnp.bitwise_xor(local_ids[:, None], local_ids[None, :])
    lower = local_ids[:, None] > local_ids[None, :]
    slot_of = jnp.zeros((groups, groups), jnp.int32)
    onehot = (
        (slot_of[:, :, None] == jnp.arange(low_levels, dtype=jnp.int32)[None, None, :])
        & lower[:, :, None]
    ).astype(jnp.float32)
    before = jnp.cumsum(totals, axis=0) - totals
    gap = before[:, None, :] - before[None, :, :] - totals[None, :, :]
    below = lower[:, :, None]
    fade_pairs = jnp.where(below, jnp.exp(jnp.where(below, gap, 0.0)), 0.0)
    local_weight = exact("cds,csh->cdh", onehot, weight_rows[:, 1 : 1 + low_levels]) * fade_pairs
    lead_fade = jnp.exp(before)
    cross_weight = weight_rows[:, 1 + low_levels : 1 + low_levels + depth] * lead_fade[:, None, :]
    scaled = jnp.exp(cumuls) / state_dim
    query_faded = (c_groups[:, :, None, :] * scaled[:, :, :, None]).astype(jnp.bfloat16)
    gram = contract("cthn,cthp->chnp", query_faded, grad_groups)
    inner_pairs = jnp.sum(states[None] * gram[:, None], axis=(3, 4))
    level_local = exact("cds,cdh->csh", onehot, fade_pairs * inner_pairs)
    level_cross = lead_fade[:, None, :] * jnp.sum(cross[None] * gram[:, None], axis=(3, 4))
    level_rest = jnp.concatenate(
        [
            level_local,
            level_cross,
            jnp.zeros((groups, levels - 1 - low_levels - depth, heads), jnp.float32),
        ],
        axis=1,
    )
    grads = exact("ck,clh->klh", picked, level_rest)
    grad_first = exact("gk,gh->kh", picked, level_zero)
    local_grads = jnp.concatenate([grad_first[:, None, :], grads], axis=1)
    local_grads, states, cross = lax.optimization_barrier((local_grads, states, cross))
    terms = [local_weight[:, d, :, None, None] * states[d][None] for d in range(groups)]
    terms += [cross_weight[:, l, :, None, None] * cross[l][None] for l in range(depth)]
    mixed = sum(terms[1:], terms[0]).astype(jnp.bfloat16)
    y_cross = contract("cthn,chnp->cthp", query_faded, mixed)
    backed = contract("chnp,cthp->cthn", mixed, grad_groups)
    grad_cross = jnp.sum(backed * scaled[:, :, :, None], axis=2)
    ssm_out = (
        (y_inner + y_cross + skip[None, None, :, None] * x_groups)
        .astype(jnp.bfloat16)
        .reshape(length, inner)
    )
    grad_query = (grad_inner + grad_cross).reshape(length, state_dim)
    after_rows = shifted(grad_query[: taps - 1], "seq", -1)
    extended = jnp.concatenate([grad_query, after_rows], axis=0)
    query_taps = conv_weight[:, inner + state_dim :]
    grad_c_in = jnp.zeros((length, state_dim), jnp.float32)
    for offset in range(taps):
        lagged = taps - 1 - offset
        grad_c_in = grad_c_in + query_taps[offset][None, :] * extended[lagged : lagged + length]
    summed = all_sum(local_grads, "seq")
    level_update = level_table + summed / math.sqrt(length * devices)
    return (ssm_out, grad_c_in, level_update)


def solution(mesh):
    placed = (
        P(("grp", "seq"), None),
        P(),
        P(),
        P(("grp", "seq"), None),
        P(),
        P(),
        P(),
        P(("grp", "seq")),
        P(("grp", "seq"), None),
    )
    return jax.shard_map(
        local,
        mesh=mesh,
        in_specs=placed,
        out_specs=(P(("grp", "seq"), None), P(("grp", "seq"), None), P("grp", None, None)),
        check_vma=False,
    )
```

```python
import math

import jax
import jax.numpy as jnp
from jax import lax
from jax.sharding import PartitionSpec as P


def shifted(value, axis, steps):
    count = lax.axis_size(axis)
    leading, last = (max(0, -steps), min(count, count - steps))
    return lax.ppermute(value, axis, [(source, source + steps) for source in range(leading, last)])


def from_partner(value, axis, distance):
    mask = 2**distance
    pairs = [(source, source ^ mask) for source in range(lax.axis_size(axis))]
    return lax.ppermute(value, axis, pairs)


def upward(value, axis, distance):
    mask = 2**distance
    count = lax.axis_size(axis)
    pairs = [(source, source | mask) for source in range(count) if not source & mask]
    return lax.ppermute(value, axis, pairs)


def all_sum(value, axis):
    for distance in range(lax.axis_size(axis).bit_length() - 1):
        value = value + from_partner(value, axis, distance)
    return value


def contract(form, left, right):
    return jnp.einsum(form, left, right, preferred_element_type=jnp.float32)


def exact(form, left, right):
    return jnp.einsum(form, left, right, precision=lax.Precision.HIGHEST)


def conv_forward(window, conv_weight, conv_bias, length):
    result = jnp.zeros((length, window.shape[1]), jnp.float32) + conv_bias[None, :]
    for offset in range(conv_weight.shape[0]):
        result = (
            result
            + window[offset : offset + length].astype(jnp.float32) * conv_weight[offset][None, :]
        )
    return result


def split_act(preact, heads, head_dim, state_dim):
    length = preact.shape[0]
    inner = heads * head_dim
    x_act = jax.nn.silu(preact[:, :inner]).astype(jnp.bfloat16).reshape(length, heads, head_dim)
    b_key = preact[:, inner : inner + state_dim].astype(jnp.bfloat16)
    c_query = preact[:, inner + state_dim :].astype(jnp.bfloat16)
    return (x_act, b_key, c_query)


def group_state_of(x_part, b_part, decay_part):
    cumul = jnp.cumsum(decay_part, axis=0)
    x_faded = (x_part * jnp.exp(cumul[-1][None, :] - cumul)[:, :, None]).astype(jnp.bfloat16)
    group_state = contract("sn,shp->hnp", b_part, x_faded)
    return (group_state, cumul)


def local_group(x_part, b_part, c_part, cumul, grad_part, weight_zero):
    length = x_part.shape[0]
    state_dim = b_part.shape[1]
    scores = jnp.dot(c_part, b_part.T, preferred_element_type=jnp.float32)
    causal = (jnp.arange(length)[:, None] >= jnp.arange(length)[None, :])[None]
    across = jnp.transpose(cumul)
    spread = across[:, :, None] - across[:, None, :]
    fading = jnp.where(causal, jnp.exp(jnp.where(causal, spread, 0.0)), 0.0)
    basic = fading * scores[None] / state_dim
    intra = (weight_zero[:, None, None] * basic).astype(jnp.bfloat16)
    y_inner = contract("hts,shp->thp", intra, x_part)
    products = contract("thp,shp->hts", grad_part, x_part)
    grad_weight = (
        jnp.sum(weight_zero[:, None, None] * fading * products, axis=0) / state_dim
    ).astype(jnp.bfloat16)
    grad_inner = jnp.dot(grad_weight, b_part, preferred_element_type=jnp.float32)
    level_zero = jnp.sum(basic * products, axis=(1, 2))
    return (y_inner, grad_inner, level_zero)


def combine(block, block_decay, other, other_decay, leading, upper):
    grown = upper[..., None, None]
    found = grown * jnp.exp(leading)[..., None, None] * other
    joined = grown * (other * jnp.exp(block_decay)[..., None, None] + block) + (1.0 - grown) * (
        block * jnp.exp(other_decay)[..., None, None] + other
    )
    return (joined, block_decay + other_decay, leading + upper * other_decay, found)


def relay(value, axis, bit_pos):
    half = 2**bit_pos
    step = half // 2
    parts = 2 if value.shape[0] % 2 == 0 else 1
    size = value.shape[0] // parts
    received = []
    for index in range(parts):
        piece = value[index * size : (index + 1) * size]
        first = lax.ppermute(piece, axis, [(source, source + step) for source in range(half - step, half)])
        second = lax.ppermute(first, axis, [(source, source + step) for source in range(half, half + step)])
        received.append(first + second)
    return jnp.concatenate(received, axis=0)


def exchange(block, block_decay, depth, myself):
    leading = jnp.zeros_like(block_decay)
    found_all = []
    first = None
    for bit_pos in range(depth):
        if bit_pos == depth - 1:
            if bit_pos == 0:
                sent = upward(block.astype(jnp.bfloat16), "seq", bit_pos)
            else:
                sent = relay(block.astype(jnp.bfloat16), "seq", bit_pos)
            other, other_decay = (sent.astype(jnp.float32), jnp.zeros_like(block_decay))
        else:
            sent, other_decay = from_partner((block.astype(jnp.bfloat16), block_decay), "seq", bit_pos)
            other = sent.astype(jnp.float32)
        first = sent if first is None else first
        upper = jnp.zeros_like(block_decay) + (jnp.right_shift(myself, bit_pos) & 1).astype(
            jnp.float32
        )
        block, block_decay, leading, found = combine(
            block, block_decay, other, other_decay, leading, upper
        )
        found_all.append(found)
    first = block if first is None else first
    return (jnp.stack(found_all, axis=0), first)


def local(
    xbc_in, conv_weight, conv_bias, dt_raw, decay_rate, skip, level_table, group_class, cotangent
):
    length = xbc_in.shape[0]
    taps = conv_weight.shape[0]
    heads = dt_raw.shape[1]
    inner = cotangent.shape[1]
    head_dim = inner // heads
    state_dim = (xbc_in.shape[1] - inner) // 2
    classes = level_table.shape[0]
    levels = level_table.shape[1]
    groups = group_class.shape[0]
    group_len = length // groups
    edge_part = shifted(xbc_in[length - taps + 1 :], "seq", 1)
    window = jnp.concatenate([edge_part, xbc_in], axis=0)
    preact = conv_forward(window, conv_weight, conv_bias, length)
    x_act, b_key, c_query = split_act(preact, heads, head_dim, state_dim)
    log_decay = -decay_rate[None, :] * jax.nn.softplus(dt_raw)
    grad_out = cotangent.reshape(length, heads, head_dim)
    picked = (group_class[:, None] == jnp.arange(classes, dtype=jnp.int32)[None, :]).astype(
        jnp.float32
    )
    weight_rows = exact("gk,klh->glh", picked, level_table)
    x_groups = x_act.reshape(groups, group_len, heads, head_dim)
    c_groups = c_query.reshape(groups, group_len, state_dim)
    grad_groups = grad_out.reshape(groups, group_len, heads, head_dim)
    b_groups = b_key.reshape(groups, group_len, state_dim)
    states, cumuls = jax.vmap(group_state_of)(
        x_groups, b_groups, log_decay.reshape(groups, group_len, heads)
    )
    totals = cumuls[:, -1]
    dev_decay = jnp.sum(totals, axis=0)
    later = dev_decay[None, :] - jnp.cumsum(totals, axis=0)
    dev_state = jnp.sum(jnp.exp(later)[:, :, None, None] * states, axis=0)
    devices = lax.axis_size("seq")
    depth = devices.bit_length() - 1
    myself = lax.axis_index("seq")
    chunks = min(3, heads)
    bounds = [k * heads // chunks for k in range(chunks + 1)]
    pieces = [
        exchange(dev_state[low:high], dev_decay[low:high], depth, myself)
        for low, high in zip(bounds[:-1], bounds[1:])
    ]
    cross = jnp.concatenate([piece for piece, _ in pieces], axis=1)
    late_cotangent = lax.optimization_barrier((cotangent, pieces[0][1]))[0]
    grad_groups = late_cotangent.reshape(groups, group_len, heads, head_dim)
    y_inner, grad_inner, level_zero = jax.vmap(local_group)(
        x_groups, b_groups, c_groups, cumuls, grad_groups, weight_rows[:, 0]
    )
    low_levels = groups.bit_length() - 1
    local_ids = jnp.arange(groups, dtype=jnp.int32)
    differ = jnp.bitwise_xor(local_ids[:, None], local_ids[None, :])
    lower = local_ids[:, None] > local_ids[None, :]
    slot_of = jnp.zeros((groups, groups), jnp.int32)
    onehot = (
        (slot_of[:, :, None] == jnp.arange(low_levels, dtype=jnp.int32)[None, None, :])
        & lower[:, :, None]
    ).astype(jnp.float32)
    before = jnp.cumsum(totals, axis=0) - totals
    gap = before[:, None, :] - before[None, :, :] - totals[None, :, :]
    below = lower[:, :, None]
    fade_pairs = jnp.where(below, jnp.exp(jnp.where(below, gap, 0.0)), 0.0)
    local_weight = exact("cds,csh->cdh", onehot, weight_rows[:, 1 : 1 + low_levels]) * fade_pairs
    lead_fade = jnp.exp(before)
    cross_weight = weight_rows[:, 1 + low_levels : 1 + low_levels + depth] * lead_fade[:, None, :]
    terms = [local_weight[:, d, :, None, None] * states[d][None] for d in range(groups)]
    terms += [cross_weight[:, l, :, None, None] * cross[l][None] for l in range(depth)]
    mixed = sum(terms[1:], terms[0]).astype(jnp.bfloat16)
    scaled = jnp.exp(cumuls) / state_dim
    query_faded = (c_groups[:, :, None, :] * scaled[:, :, :, None]).astype(jnp.bfloat16)
    y_cross = contract("cthn,chnp->cthp", query_faded, mixed)
    backed = contract("chnp,cthp->cthn", mixed, grad_groups)
    grad_cross = jnp.sum(backed * scaled[:, :, :, None], axis=2)
    gram = contract("cthn,cthp->chnp", query_faded, grad_groups)
    inner_pairs = jnp.sum(states[None] * gram[:, None], axis=(3, 4))
    level_local = exact("cds,cdh->csh", onehot, fade_pairs * inner_pairs)
    level_cross = lead_fade[:, None, :] * jnp.sum(cross[None] * gram[:, None], axis=(3, 4))
    level_rest = jnp.concatenate(
        [
            level_local,
            level_cross,
            jnp.zeros((groups, levels - 1 - low_levels - depth, heads), jnp.float32),
        ],
        axis=1,
    )
    grads = exact("ck,clh->klh", picked, level_rest)
    ssm_out = (
        (y_inner + y_cross + skip[None, None, :, None] * x_groups)
        .astype(jnp.bfloat16)
        .reshape(length, inner)
    )
    grad_query = (grad_inner + grad_cross).reshape(length, state_dim)
    after_rows = shifted(grad_query[: taps - 1], "seq", -1)
    extended = jnp.concatenate([grad_query, after_rows], axis=0)
    query_taps = conv_weight[:, inner + state_dim :]
    grad_c_in = jnp.zeros((length, state_dim), jnp.float32)
    for offset in range(taps):
        lagged = taps - 1 - offset
        grad_c_in = grad_c_in + query_taps[offset][None, :] * extended[lagged : lagged + length]
    grad_first = exact("gk,gh->kh", picked, level_zero)
    local_grads = jnp.concatenate([grad_first[:, None, :], grads], axis=1)
    summed = all_sum(local_grads, "seq")
    level_update = level_table + summed / math.sqrt(length * devices)
    return (ssm_out, grad_c_in, level_update)


def solution(mesh):
    placed = (
        P(("grp", "seq"), None),
        P(),
        P(),
        P(("grp", "seq"), None),
        P(),
        P(),
        P(),
        P(("grp", "seq")),
        P(("grp", "seq"), None),
    )
    return jax.shard_map(
        local,
        mesh=mesh,
        in_specs=placed,
        out_specs=(P(("grp", "seq"), None), P(("grp", "seq"), None), P("grp", None, None)),
        check_vma=False,
    )
```

```python
import math

import jax
import jax.numpy as jnp
from jax import lax
from jax.sharding import PartitionSpec as P


def shifted(value, axis, steps):
    count = lax.axis_size(axis)
    leading, last = (max(0, -steps), min(count, count - steps))
    return lax.ppermute(value, axis, [(source, source + steps) for source in range(leading, last)])


def from_partner(value, axis, distance):
    mask = 2**distance
    pairs = [(source, source ^ mask) for source in range(lax.axis_size(axis))]
    return lax.ppermute(value, axis, pairs)


def upward(value, axis, distance):
    mask = 2**distance
    count = lax.axis_size(axis)
    pairs = [(source, source | mask) for source in range(count) if not source & mask]
    return lax.ppermute(value, axis, pairs)


def all_sum(value, axis):
    for distance in range(lax.axis_size(axis).bit_length() - 1):
        value = value + from_partner(value, axis, distance)
    return value


def contract(form, left, right):
    return jnp.einsum(form, left, right, preferred_element_type=jnp.float32)


def exact(form, left, right):
    return jnp.einsum(form, left, right, precision=lax.Precision.HIGHEST)


def conv_forward(window, conv_weight, conv_bias, length):
    result = jnp.zeros((length, window.shape[1]), jnp.float32) + conv_bias[None, :]
    for offset in range(conv_weight.shape[0]):
        result = (
            result
            + window[offset : offset + length].astype(jnp.float32) * conv_weight[offset][None, :]
        )
    return result


def split_act(preact, heads, head_dim, state_dim):
    length = preact.shape[0]
    inner = heads * head_dim
    x_act = jax.nn.silu(preact[:, :inner]).astype(jnp.bfloat16).reshape(length, heads, head_dim)
    b_key = preact[:, inner : inner + state_dim].astype(jnp.bfloat16)
    c_query = preact[:, inner + state_dim :].astype(jnp.bfloat16)
    return (x_act, b_key, c_query)


def group_state_of(x_part, b_part, decay_part):
    cumul = jnp.cumsum(decay_part, axis=0)
    x_faded = (x_part * jnp.exp(cumul[-1][None, :] - cumul)[:, :, None]).astype(jnp.bfloat16)
    group_state = contract("sn,shp->hnp", b_part, x_faded)
    return (group_state, cumul)


def local_group(x_part, b_part, c_part, cumul, grad_part, weight_zero):
    length = x_part.shape[0]
    state_dim = b_part.shape[1]
    scores = jnp.dot(c_part, b_part.T, preferred_element_type=jnp.float32)
    causal = (jnp.arange(length)[:, None] >= jnp.arange(length)[None, :])[None]
    across = jnp.transpose(cumul)
    spread = across[:, :, None] - across[:, None, :]
    fading = jnp.where(causal, jnp.exp(jnp.where(causal, spread, 0.0)), 0.0)
    basic = fading * scores[None] / state_dim
    intra = (weight_zero[:, None, None] * basic).astype(jnp.bfloat16)
    y_inner = contract("hts,shp->thp", intra, x_part)
    products = contract("thp,shp->hts", grad_part, x_part)
    grad_weight = (
        jnp.sum(weight_zero[:, None, None] * fading * products, axis=0) / state_dim
    ).astype(jnp.bfloat16)
    grad_inner = jnp.dot(grad_weight, b_part, preferred_element_type=jnp.float32)
    level_zero = jnp.sum(basic * products, axis=(1, 2))
    return (y_inner, grad_inner, level_zero)


def combine(block, block_decay, other, other_decay, leading, upper):
    grown = upper[..., None, None]
    found = grown * jnp.exp(leading)[..., None, None] * other
    joined = grown * (other * jnp.exp(block_decay)[..., None, None] + block) + (1.0 - grown) * (
        block * jnp.exp(other_decay)[..., None, None] + other
    )
    return (joined, block_decay + other_decay, leading + upper * other_decay, found)


def relay(value, axis, bit_pos):
    half = 2**bit_pos
    step = half // 2
    parts = 2 if value.shape[0] % 2 == 0 else 1
    size = value.shape[0] // parts
    received = []
    for index in range(parts):
        piece = value[index * size : (index + 1) * size]
        first = lax.ppermute(piece, axis, [(source, source + step) for source in range(half - step, half)])
        second = lax.ppermute(first, axis, [(source, source + step) for source in range(half, half + step)])
        received.append(first + second)
    return jnp.concatenate(received, axis=0)


def exchange(block, block_decay, depth, myself):
    leading = jnp.zeros_like(block_decay)
    found_all = []
    first = None
    for bit_pos in range(depth):
        if bit_pos == depth - 1:
            if bit_pos == 0:
                sent = upward(block.astype(jnp.bfloat16), "seq", bit_pos)
            else:
                sent = relay(block.astype(jnp.bfloat16), "seq", bit_pos)
            other, other_decay = (sent.astype(jnp.float32), jnp.zeros_like(block_decay))
        else:
            sent, other_decay = from_partner((block.astype(jnp.bfloat16), block_decay), "seq", bit_pos)
            other = sent.astype(jnp.float32)
        first = sent if first is None else first
        upper = jnp.zeros_like(block_decay) + (jnp.right_shift(myself, bit_pos) & 1).astype(
            jnp.float32
        )
        block, block_decay, leading, found = combine(
            block, block_decay, other, other_decay, leading, upper
        )
        found_all.append(found)
    first = block if first is None else first
    return (jnp.stack(found_all, axis=0), first)


def local(
    xbc_in, conv_weight, conv_bias, dt_raw, decay_rate, skip, level_table, group_class, cotangent
):
    length = xbc_in.shape[0]
    taps = conv_weight.shape[0]
    heads = dt_raw.shape[1]
    inner = cotangent.shape[1]
    head_dim = inner // heads
    state_dim = (xbc_in.shape[1] - inner) // 2
    classes = level_table.shape[0]
    levels = level_table.shape[1]
    groups = group_class.shape[0]
    group_len = length // groups
    edge_part = shifted(xbc_in[length - taps + 1 :], "seq", 1)
    window = jnp.concatenate([edge_part, xbc_in], axis=0)
    preact = conv_forward(window, conv_weight, conv_bias, length)
    x_act, b_key, c_query = split_act(preact, heads, head_dim, state_dim)
    log_decay = -decay_rate[None, :] * jax.nn.softplus(dt_raw)
    grad_out = cotangent.reshape(length, heads, head_dim)
    picked = (group_class[:, None] == jnp.arange(classes, dtype=jnp.int32)[None, :]).astype(
        jnp.float32
    )
    weight_rows = exact("gk,klh->glh", picked, level_table)
    x_groups = x_act.reshape(groups, group_len, heads, head_dim)
    c_groups = c_query.reshape(groups, group_len, state_dim)
    grad_groups = grad_out.reshape(groups, group_len, heads, head_dim)
    b_groups = b_key.reshape(groups, group_len, state_dim)
    states, cumuls = jax.vmap(group_state_of)(
        x_groups, b_groups, log_decay.reshape(groups, group_len, heads)
    )
    totals = cumuls[:, -1]
    dev_decay = jnp.sum(totals, axis=0)
    later = dev_decay[None, :] - jnp.cumsum(totals, axis=0)
    dev_state = jnp.sum(jnp.exp(later)[:, :, None, None] * states, axis=0)
    devices = lax.axis_size("seq")
    depth = devices.bit_length() - 1
    myself = lax.axis_index("seq")
    chunks = 2 if heads % 2 == 0 else 1
    width = heads // chunks
    pieces = [
        exchange(dev_state[k * width : (k + 1) * width], dev_decay[k * width : (k + 1) * width], depth, myself)
        for k in range(chunks)
    ]
    cross = jnp.concatenate([piece for piece, _ in pieces], axis=1)
    late_cotangent = lax.optimization_barrier((cotangent, pieces[0][1]))[0]
    grad_groups = late_cotangent.reshape(groups, group_len, heads, head_dim)
    y_inner, grad_inner, level_zero = jax.vmap(local_group)(
        x_groups, b_groups, c_groups, cumuls, grad_groups, weight_rows[:, 0]
    )
    low_levels = groups.bit_length() - 1
    local_ids = jnp.arange(groups, dtype=jnp.int32)
    differ = jnp.bitwise_xor(local_ids[:, None], local_ids[None, :])
    lower = local_ids[:, None] > local_ids[None, :]
    slot_of = jnp.zeros((groups, groups), jnp.int32)
    onehot = (
        (slot_of[:, :, None] == jnp.arange(low_levels, dtype=jnp.int32)[None, None, :])
        & lower[:, :, None]
    ).astype(jnp.float32)
    before = jnp.cumsum(totals, axis=0) - totals
    gap = before[:, None, :] - before[None, :, :] - totals[None, :, :]
    below = lower[:, :, None]
    fade_pairs = jnp.where(below, jnp.exp(jnp.where(below, gap, 0.0)), 0.0)
    local_weight = exact("cds,csh->cdh", onehot, weight_rows[:, 1 : 1 + low_levels]) * fade_pairs
    lead_fade = jnp.exp(before)
    cross_weight = weight_rows[:, 1 + low_levels : 1 + low_levels + depth] * lead_fade[:, None, :]
    scaled = jnp.exp(cumuls) / state_dim
    query_faded = (c_groups[:, :, None, :] * scaled[:, :, :, None]).astype(jnp.bfloat16)
    gram = contract("cthn,cthp->chnp", query_faded, grad_groups)
    inner_pairs = jnp.sum(states[None] * gram[:, None], axis=(3, 4))
    level_local = exact("cds,cdh->csh", onehot, fade_pairs * inner_pairs)
    level_cross = lead_fade[:, None, :] * jnp.sum(cross[None] * gram[:, None], axis=(3, 4))
    level_rest = jnp.concatenate(
        [
            level_local,
            level_cross,
            jnp.zeros((groups, levels - 1 - low_levels - depth, heads), jnp.float32),
        ],
        axis=1,
    )
    grads = exact("ck,clh->klh", picked, level_rest)
    grad_first = exact("gk,gh->kh", picked, level_zero)
    local_grads = jnp.concatenate([grad_first[:, None, :], grads], axis=1)
    partial = local_grads
    if depth > 0:
        partial = partial + from_partner(partial, "seq", 0)
    partial, states, cross = lax.optimization_barrier((partial, states, cross))
    terms = [local_weight[:, d, :, None, None] * states[d][None] for d in range(groups)]
    terms += [cross_weight[:, l, :, None, None] * cross[l][None] for l in range(depth)]
    mixed = sum(terms[1:], terms[0]).astype(jnp.bfloat16)
    y_cross = contract("cthn,chnp->cthp", query_faded, mixed)
    backed = contract("chnp,cthp->cthn", mixed, grad_groups)
    grad_cross = jnp.sum(backed * scaled[:, :, :, None], axis=2)
    ssm_out = (
        (y_inner + y_cross + skip[None, None, :, None] * x_groups)
        .astype(jnp.bfloat16)
        .reshape(length, inner)
    )
    grad_query = (grad_inner + grad_cross).reshape(length, state_dim)
    after_rows = shifted(grad_query[: taps - 1], "seq", -1)
    extended = jnp.concatenate([grad_query, after_rows], axis=0)
    query_taps = conv_weight[:, inner + state_dim :]
    grad_c_in = jnp.zeros((length, state_dim), jnp.float32)
    for offset in range(taps):
        lagged = taps - 1 - offset
        grad_c_in = grad_c_in + query_taps[offset][None, :] * extended[lagged : lagged + length]
    summed = partial
    for distance in range(1, depth):
        summed = summed + from_partner(summed, "seq", distance)
    level_update = level_table + summed / math.sqrt(length * devices)
    return (ssm_out, grad_c_in, level_update)


def solution(mesh):
    placed = (
        P(("grp", "seq"), None),
        P(),
        P(),
        P(("grp", "seq"), None),
        P(),
        P(),
        P(),
        P(("grp", "seq")),
        P(("grp", "seq"), None),
    )
    return jax.shard_map(
        local,
        mesh=mesh,
        in_specs=placed,
        out_specs=(P(("grp", "seq"), None), P(("grp", "seq"), None), P("grp", None, None)),
        check_vma=False,
    )
```

```python
import math

import jax
import jax.numpy as jnp
from jax import lax
from jax.sharding import PartitionSpec as P


def shifted(value, axis, steps):
    count = lax.axis_size(axis)
    leading, last = (max(0, -steps), min(count, count - steps))
    return lax.ppermute(value, axis, [(source, source + steps) for source in range(leading, last)])


def from_partner(value, axis, distance):
    mask = 2**distance
    pairs = [(source, source ^ mask) for source in range(lax.axis_size(axis))]
    return lax.ppermute(value, axis, pairs)


def upward(value, axis, distance):
    mask = 2**distance
    count = lax.axis_size(axis)
    pairs = [(source, source | mask) for source in range(count) if not source & mask]
    return lax.ppermute(value, axis, pairs)


def all_sum(value, axis):
    for distance in range(lax.axis_size(axis).bit_length() - 1):
        value = value + from_partner(value, axis, distance)
    return value


def contract(form, left, right):
    return jnp.einsum(form, left, right, preferred_element_type=jnp.float32)


def exact(form, left, right):
    return jnp.einsum(form, left, right, precision=lax.Precision.HIGHEST)


def conv_forward(window, conv_weight, conv_bias, length):
    result = jnp.zeros((length, window.shape[1]), jnp.float32) + conv_bias[None, :]
    for offset in range(conv_weight.shape[0]):
        result = (
            result
            + window[offset : offset + length].astype(jnp.float32) * conv_weight[offset][None, :]
        )
    return result


def split_act(preact, heads, head_dim, state_dim):
    length = preact.shape[0]
    inner = heads * head_dim
    x_act = jax.nn.silu(preact[:, :inner]).astype(jnp.bfloat16).reshape(length, heads, head_dim)
    b_key = preact[:, inner : inner + state_dim].astype(jnp.bfloat16)
    c_query = preact[:, inner + state_dim :].astype(jnp.bfloat16)
    return (x_act, b_key, c_query)


def group_state_of(x_part, b_part, decay_part):
    cumul = jnp.cumsum(decay_part, axis=0)
    x_faded = (x_part * jnp.exp(cumul[-1][None, :] - cumul)[:, :, None]).astype(jnp.bfloat16)
    group_state = contract("sn,shp->hnp", b_part, x_faded)
    return (group_state, cumul)


def local_group(x_part, b_part, c_part, cumul, grad_part, weight_zero):
    length = x_part.shape[0]
    state_dim = b_part.shape[1]
    scores = jnp.dot(c_part, b_part.T, preferred_element_type=jnp.float32)
    causal = (jnp.arange(length)[:, None] >= jnp.arange(length)[None, :])[None]
    across = jnp.transpose(cumul)
    spread = across[:, :, None] - across[:, None, :]
    fading = jnp.where(causal, jnp.exp(jnp.where(causal, spread, 0.0)), 0.0)
    basic = fading * scores[None] / state_dim
    intra = (weight_zero[:, None, None] * basic).astype(jnp.bfloat16)
    y_inner = contract("hts,shp->thp", intra, x_part)
    products = contract("thp,shp->hts", grad_part, x_part)
    grad_weight = (
        jnp.sum(weight_zero[:, None, None] * fading * products, axis=0) / state_dim
    ).astype(jnp.bfloat16)
    grad_inner = jnp.dot(grad_weight, b_part, preferred_element_type=jnp.float32)
    level_zero = jnp.sum(basic * products, axis=(1, 2))
    return (y_inner, grad_inner, level_zero)


def combine(block, block_decay, other, other_decay, leading, upper):
    grown = upper[..., None, None]
    found = grown * jnp.exp(leading)[..., None, None] * other
    joined = grown * (other * jnp.exp(block_decay)[..., None, None] + block) + (1.0 - grown) * (
        block * jnp.exp(other_decay)[..., None, None] + other
    )
    return (joined, block_decay + other_decay, leading + upper * other_decay, found)


def relay(value, axis, bit_pos):
    half = 2**bit_pos
    step = half // 2
    parts = 2 if value.shape[0] % 2 == 0 else 1
    size = value.shape[0] // parts
    received = []
    for index in range(parts):
        piece = value[index * size : (index + 1) * size]
        first = lax.ppermute(piece, axis, [(source, source + step) for source in range(half - step, half)])
        second = lax.ppermute(first, axis, [(source, source + step) for source in range(half, half + step)])
        received.append(first + second)
    return jnp.concatenate(received, axis=0)


def exchange(block, block_decay, depth, myself, decays):
    leading = jnp.zeros_like(block_decay)
    found_all = []
    first = None
    for bit_pos in range(depth):
        if bit_pos == depth - 1:
            if bit_pos == 0:
                sent = upward(block.astype(jnp.bfloat16), "seq", bit_pos)
            else:
                sent = relay(block.astype(jnp.bfloat16), "seq", bit_pos)
            other, other_decay = (sent.astype(jnp.float32), jnp.zeros_like(block_decay))
        else:
            sent = from_partner(block.astype(jnp.bfloat16), "seq", bit_pos)
            other, other_decay = (sent.astype(jnp.float32), decays[bit_pos])
        first = sent if first is None else first
        upper = jnp.zeros_like(block_decay) + (jnp.right_shift(myself, bit_pos) & 1).astype(
            jnp.float32
        )
        block, block_decay, leading, found = combine(
            block, block_decay, other, other_decay, leading, upper
        )
        found_all.append(found)
    first = block if first is None else first
    return (jnp.stack(found_all, axis=0), first)


def local(
    xbc_in, conv_weight, conv_bias, dt_raw, decay_rate, skip, level_table, group_class, cotangent
):
    length = xbc_in.shape[0]
    taps = conv_weight.shape[0]
    heads = dt_raw.shape[1]
    inner = cotangent.shape[1]
    head_dim = inner // heads
    state_dim = (xbc_in.shape[1] - inner) // 2
    classes = level_table.shape[0]
    levels = level_table.shape[1]
    groups = group_class.shape[0]
    group_len = length // groups
    edge_part = shifted(xbc_in[length - taps + 1 :], "seq", 1)
    window = jnp.concatenate([edge_part, xbc_in], axis=0)
    preact = conv_forward(window, conv_weight, conv_bias, length)
    x_act, b_key, c_query = split_act(preact, heads, head_dim, state_dim)
    log_decay = -decay_rate[None, :] * jax.nn.softplus(dt_raw)
    grad_out = cotangent.reshape(length, heads, head_dim)
    picked = (group_class[:, None] == jnp.arange(classes, dtype=jnp.int32)[None, :]).astype(
        jnp.float32
    )
    weight_rows = exact("gk,klh->glh", picked, level_table)
    x_groups = x_act.reshape(groups, group_len, heads, head_dim)
    c_groups = c_query.reshape(groups, group_len, state_dim)
    grad_groups = grad_out.reshape(groups, group_len, heads, head_dim)
    b_groups = b_key.reshape(groups, group_len, state_dim)
    states, cumuls = jax.vmap(group_state_of)(
        x_groups, b_groups, log_decay.reshape(groups, group_len, heads)
    )
    totals = cumuls[:, -1]
    dev_decay = jnp.sum(totals, axis=0)
    later = dev_decay[None, :] - jnp.cumsum(totals, axis=0)
    dev_state = jnp.sum(jnp.exp(later)[:, :, None, None] * states, axis=0)
    devices = lax.axis_size("seq")
    depth = devices.bit_length() - 1
    myself = lax.axis_index("seq")
    decays = []
    running = dev_decay
    for bit_pos in range(depth - 1):
        decays.append(from_partner(running, "seq", bit_pos))
        running = running + decays[-1]
    chunks = 2 if heads % 2 == 0 else 1
    width = heads // chunks
    pieces = [
        exchange(
            dev_state[k * width : (k + 1) * width],
            dev_decay[k * width : (k + 1) * width],
            depth,
            myself,
            [decay[k * width : (k + 1) * width] for decay in decays],
        )
        for k in range(chunks)
    ]
    cross = jnp.concatenate([piece for piece, _ in pieces], axis=1)
    late_cotangent = lax.optimization_barrier((cotangent, pieces[0][1]))[0]
    grad_groups = late_cotangent.reshape(groups, group_len, heads, head_dim)
    y_inner, grad_inner, level_zero = jax.vmap(local_group)(
        x_groups, b_groups, c_groups, cumuls, grad_groups, weight_rows[:, 0]
    )
    low_levels = groups.bit_length() - 1
    local_ids = jnp.arange(groups, dtype=jnp.int32)
    differ = jnp.bitwise_xor(local_ids[:, None], local_ids[None, :])
    lower = local_ids[:, None] > local_ids[None, :]
    slot_of = jnp.zeros((groups, groups), jnp.int32)
    onehot = (
        (slot_of[:, :, None] == jnp.arange(low_levels, dtype=jnp.int32)[None, None, :])
        & lower[:, :, None]
    ).astype(jnp.float32)
    before = jnp.cumsum(totals, axis=0) - totals
    gap = before[:, None, :] - before[None, :, :] - totals[None, :, :]
    below = lower[:, :, None]
    fade_pairs = jnp.where(below, jnp.exp(jnp.where(below, gap, 0.0)), 0.0)
    local_weight = exact("cds,csh->cdh", onehot, weight_rows[:, 1 : 1 + low_levels]) * fade_pairs
    lead_fade = jnp.exp(before)
    cross_weight = weight_rows[:, 1 + low_levels : 1 + low_levels + depth] * lead_fade[:, None, :]
    terms = [local_weight[:, d, :, None, None] * states[d][None] for d in range(groups)]
    terms += [cross_weight[:, l, :, None, None] * cross[l][None] for l in range(depth)]
    mixed = sum(terms[1:], terms[0]).astype(jnp.bfloat16)
    scaled = jnp.exp(cumuls) / state_dim
    query_faded = (c_groups[:, :, None, :] * scaled[:, :, :, None]).astype(jnp.bfloat16)
    y_cross = contract("cthn,chnp->cthp", query_faded, mixed)
    backed = contract("chnp,cthp->cthn", mixed, grad_groups)
    grad_cross = jnp.sum(backed * scaled[:, :, :, None], axis=2)
    gram = contract("cthn,cthp->chnp", query_faded, grad_groups)
    inner_pairs = jnp.sum(states[None] * gram[:, None], axis=(3, 4))
    level_local = exact("cds,cdh->csh", onehot, fade_pairs * inner_pairs)
    level_cross = lead_fade[:, None, :] * jnp.sum(cross[None] * gram[:, None], axis=(3, 4))
    level_rest = jnp.concatenate(
        [
            level_local,
            level_cross,
            jnp.zeros((groups, levels - 1 - low_levels - depth, heads), jnp.float32),
        ],
        axis=1,
    )
    grads = exact("ck,clh->klh", picked, level_rest)
    ssm_out = (
        (y_inner + y_cross + skip[None, None, :, None] * x_groups)
        .astype(jnp.bfloat16)
        .reshape(length, inner)
    )
    grad_query = (grad_inner + grad_cross).reshape(length, state_dim)
    after_rows = shifted(grad_query[: taps - 1], "seq", -1)
    extended = jnp.concatenate([grad_query, after_rows], axis=0)
    query_taps = conv_weight[:, inner + state_dim :]
    grad_c_in = jnp.zeros((length, state_dim), jnp.float32)
    for offset in range(taps):
        lagged = taps - 1 - offset
        grad_c_in = grad_c_in + query_taps[offset][None, :] * extended[lagged : lagged + length]
    grad_first = exact("gk,gh->kh", picked, level_zero)
    local_grads = jnp.concatenate([grad_first[:, None, :], grads], axis=1)
    summed = all_sum(local_grads, "seq")
    level_update = level_table + summed / math.sqrt(length * devices)
    return (ssm_out, grad_c_in, level_update)


def solution(mesh):
    placed = (
        P(("grp", "seq"), None),
        P(),
        P(),
        P(("grp", "seq"), None),
        P(),
        P(),
        P(),
        P(("grp", "seq")),
        P(("grp", "seq"), None),
    )
    return jax.shard_map(
        local,
        mesh=mesh,
        in_specs=placed,
        out_specs=(P(("grp", "seq"), None), P(("grp", "seq"), None), P("grp", None, None)),
        check_vma=False,
    )
```

```python
import math

import jax
import jax.numpy as jnp
from jax import lax
from jax.sharding import PartitionSpec as P


def shifted(value, axis, steps):
    count = lax.axis_size(axis)
    leading, last = (max(0, -steps), min(count, count - steps))
    return lax.ppermute(value, axis, [(source, source + steps) for source in range(leading, last)])


def from_partner(value, axis, distance):
    mask = 2**distance
    pairs = [(source, source ^ mask) for source in range(lax.axis_size(axis))]
    return lax.ppermute(value, axis, pairs)


def upward(value, axis, distance):
    mask = 2**distance
    count = lax.axis_size(axis)
    pairs = [(source, source | mask) for source in range(count) if not source & mask]
    return lax.ppermute(value, axis, pairs)


def all_sum(value, axis):
    for distance in range(lax.axis_size(axis).bit_length() - 1):
        value = value + from_partner(value, axis, distance)
    return value


def contract(form, left, right):
    return jnp.einsum(form, left, right, preferred_element_type=jnp.float32)


def exact(form, left, right):
    return jnp.einsum(form, left, right, precision=lax.Precision.HIGHEST)


def conv_forward(window, conv_weight, conv_bias, length):
    result = jnp.zeros((length, window.shape[1]), jnp.float32) + conv_bias[None, :]
    for offset in range(conv_weight.shape[0]):
        result = (
            result
            + window[offset : offset + length].astype(jnp.float32) * conv_weight[offset][None, :]
        )
    return result


def split_act(preact, heads, head_dim, state_dim):
    length = preact.shape[0]
    inner = heads * head_dim
    x_act = jax.nn.silu(preact[:, :inner]).astype(jnp.bfloat16).reshape(length, heads, head_dim)
    b_key = preact[:, inner : inner + state_dim].astype(jnp.bfloat16)
    c_query = preact[:, inner + state_dim :].astype(jnp.bfloat16)
    return (x_act, b_key, c_query)


def group_state_of(x_part, b_part, decay_part):
    cumul = jnp.cumsum(decay_part, axis=0)
    x_faded = (x_part * jnp.exp(cumul[-1][None, :] - cumul)[:, :, None]).astype(jnp.bfloat16)
    group_state = contract("sn,shp->hnp", b_part, x_faded)
    return (group_state, cumul)


def local_group(x_part, b_part, c_part, cumul, grad_part, weight_zero):
    length = x_part.shape[0]
    state_dim = b_part.shape[1]
    scores = jnp.dot(c_part, b_part.T, preferred_element_type=jnp.float32)
    causal = (jnp.arange(length)[:, None] >= jnp.arange(length)[None, :])[None]
    across = jnp.transpose(cumul)
    spread = across[:, :, None] - across[:, None, :]
    fading = jnp.where(causal, jnp.exp(jnp.where(causal, spread, 0.0)), 0.0)
    basic = fading * scores[None] / state_dim
    intra = (weight_zero[:, None, None] * basic).astype(jnp.bfloat16)
    y_inner = contract("hts,shp->thp", intra, x_part)
    products = contract("thp,shp->hts", grad_part, x_part)
    grad_weight = (
        jnp.sum(weight_zero[:, None, None] * fading * products, axis=0) / state_dim
    ).astype(jnp.bfloat16)
    grad_inner = jnp.dot(grad_weight, b_part, preferred_element_type=jnp.float32)
    level_zero = jnp.sum(basic * products, axis=(1, 2))
    return (y_inner, grad_inner, level_zero)


def combine(block, block_decay, other, other_decay, leading, upper):
    grown = upper[..., None, None]
    found = grown * jnp.exp(leading)[..., None, None] * other
    joined = grown * (other * jnp.exp(block_decay)[..., None, None] + block) + (1.0 - grown) * (
        block * jnp.exp(other_decay)[..., None, None] + other
    )
    return (joined, block_decay + other_decay, leading + upper * other_decay, found)


def relay(value, axis, bit_pos):
    half = 2**bit_pos
    step = half // 2
    parts = 1
    size = value.shape[0] // parts
    received = []
    for index in range(parts):
        piece = value[index * size : (index + 1) * size]
        first = lax.ppermute(piece, axis, [(source, source + step) for source in range(half - step, half)])
        second = lax.ppermute(first, axis, [(source, source + step) for source in range(half, half + step)])
        received.append(first + second)
    return jnp.concatenate(received, axis=0)


def exchange(block, block_decay, depth, myself, decays):
    leading = jnp.zeros_like(block_decay)
    found_all = []
    first = None
    for bit_pos in range(depth):
        if bit_pos == depth - 1:
            if bit_pos == 0:
                sent = upward(block.astype(jnp.bfloat16), "seq", bit_pos)
            else:
                sent = relay(block.astype(jnp.bfloat16), "seq", bit_pos)
            other, other_decay = (sent.astype(jnp.float32), jnp.zeros_like(block_decay))
        else:
            sent = from_partner(block.astype(jnp.bfloat16), "seq", bit_pos)
            other, other_decay = (sent.astype(jnp.float32), decays[bit_pos])
        first = sent if first is None else first
        upper = jnp.zeros_like(block_decay) + (jnp.right_shift(myself, bit_pos) & 1).astype(
            jnp.float32
        )
        block, block_decay, leading, found = combine(
            block, block_decay, other, other_decay, leading, upper
        )
        found_all.append(found)
    first = block if first is None else first
    return (jnp.stack(found_all, axis=0), first)


def local(
    xbc_in, conv_weight, conv_bias, dt_raw, decay_rate, skip, level_table, group_class, cotangent
):
    length = xbc_in.shape[0]
    taps = conv_weight.shape[0]
    heads = dt_raw.shape[1]
    inner = cotangent.shape[1]
    head_dim = inner // heads
    state_dim = (xbc_in.shape[1] - inner) // 2
    classes = level_table.shape[0]
    levels = level_table.shape[1]
    groups = group_class.shape[0]
    group_len = length // groups
    edge_part = shifted(xbc_in[length - taps + 1 :], "seq", 1)
    window = jnp.concatenate([edge_part, xbc_in], axis=0)
    preact = conv_forward(window, conv_weight, conv_bias, length)
    x_act, b_key, c_query = split_act(preact, heads, head_dim, state_dim)
    log_decay = -decay_rate[None, :] * jax.nn.softplus(dt_raw)
    grad_out = cotangent.reshape(length, heads, head_dim)
    picked = (group_class[:, None] == jnp.arange(classes, dtype=jnp.int32)[None, :]).astype(
        jnp.float32
    )
    weight_rows = exact("gk,klh->glh", picked, level_table)
    x_groups = x_act.reshape(groups, group_len, heads, head_dim)
    c_groups = c_query.reshape(groups, group_len, state_dim)
    grad_groups = grad_out.reshape(groups, group_len, heads, head_dim)
    b_groups = b_key.reshape(groups, group_len, state_dim)
    states, cumuls = jax.vmap(group_state_of)(
        x_groups, b_groups, log_decay.reshape(groups, group_len, heads)
    )
    totals = cumuls[:, -1]
    dev_decay = jnp.sum(totals, axis=0)
    later = dev_decay[None, :] - jnp.cumsum(totals, axis=0)
    dev_state = jnp.sum(jnp.exp(later)[:, :, None, None] * states, axis=0)
    devices = lax.axis_size("seq")
    depth = devices.bit_length() - 1
    myself = lax.axis_index("seq")
    decays = []
    running = dev_decay
    for bit_pos in range(depth - 1):
        decays.append(from_partner(running, "seq", bit_pos))
        running = running + decays[-1]
    chunks = 2 if heads % 2 == 0 else 1
    width = heads // chunks
    pieces = [
        exchange(
            dev_state[k * width : (k + 1) * width],
            dev_decay[k * width : (k + 1) * width],
            depth,
            myself,
            [decay[k * width : (k + 1) * width] for decay in decays],
        )
        for k in range(chunks)
    ]
    cross = jnp.concatenate([piece for piece, _ in pieces], axis=1)
    late_cotangent = lax.optimization_barrier((cotangent, pieces[0][1]))[0]
    grad_groups = late_cotangent.reshape(groups, group_len, heads, head_dim)
    y_inner, grad_inner, level_zero = jax.vmap(local_group)(
        x_groups, b_groups, c_groups, cumuls, grad_groups, weight_rows[:, 0]
    )
    low_levels = groups.bit_length() - 1
    local_ids = jnp.arange(groups, dtype=jnp.int32)
    differ = jnp.bitwise_xor(local_ids[:, None], local_ids[None, :])
    lower = local_ids[:, None] > local_ids[None, :]
    slot_of = jnp.zeros((groups, groups), jnp.int32)
    onehot = (
        (slot_of[:, :, None] == jnp.arange(low_levels, dtype=jnp.int32)[None, None, :])
        & lower[:, :, None]
    ).astype(jnp.float32)
    before = jnp.cumsum(totals, axis=0) - totals
    gap = before[:, None, :] - before[None, :, :] - totals[None, :, :]
    below = lower[:, :, None]
    fade_pairs = jnp.where(below, jnp.exp(jnp.where(below, gap, 0.0)), 0.0)
    local_weight = exact("cds,csh->cdh", onehot, weight_rows[:, 1 : 1 + low_levels]) * fade_pairs
    lead_fade = jnp.exp(before)
    cross_weight = weight_rows[:, 1 + low_levels : 1 + low_levels + depth] * lead_fade[:, None, :]
    terms = [local_weight[:, d, :, None, None] * states[d][None] for d in range(groups)]
    terms += [cross_weight[:, l, :, None, None] * cross[l][None] for l in range(depth)]
    mixed = sum(terms[1:], terms[0]).astype(jnp.bfloat16)
    scaled = jnp.exp(cumuls) / state_dim
    query_faded = (c_groups[:, :, None, :] * scaled[:, :, :, None]).astype(jnp.bfloat16)
    y_cross = contract("cthn,chnp->cthp", query_faded, mixed)
    backed = contract("chnp,cthp->cthn", mixed, grad_groups)
    grad_cross = jnp.sum(backed * scaled[:, :, :, None], axis=2)
    gram = contract("cthn,cthp->chnp", query_faded, grad_groups)
    inner_pairs = jnp.sum(states[None] * gram[:, None], axis=(3, 4))
    level_local = exact("cds,cdh->csh", onehot, fade_pairs * inner_pairs)
    level_cross = lead_fade[:, None, :] * jnp.sum(cross[None] * gram[:, None], axis=(3, 4))
    level_rest = jnp.concatenate(
        [
            level_local,
            level_cross,
            jnp.zeros((groups, levels - 1 - low_levels - depth, heads), jnp.float32),
        ],
        axis=1,
    )
    grads = exact("ck,clh->klh", picked, level_rest)
    ssm_out = (
        (y_inner + y_cross + skip[None, None, :, None] * x_groups)
        .astype(jnp.bfloat16)
        .reshape(length, inner)
    )
    grad_query = (grad_inner + grad_cross).reshape(length, state_dim)
    after_rows = shifted(grad_query[: taps - 1], "seq", -1)
    extended = jnp.concatenate([grad_query, after_rows], axis=0)
    query_taps = conv_weight[:, inner + state_dim :]
    grad_c_in = jnp.zeros((length, state_dim), jnp.float32)
    for offset in range(taps):
        lagged = taps - 1 - offset
        grad_c_in = grad_c_in + query_taps[offset][None, :] * extended[lagged : lagged + length]
    grad_first = exact("gk,gh->kh", picked, level_zero)
    local_grads = jnp.concatenate([grad_first[:, None, :], grads], axis=1)
    summed = all_sum(local_grads, "seq")
    level_update = level_table + summed / math.sqrt(length * devices)
    return (ssm_out, grad_c_in, level_update)


def solution(mesh):
    placed = (
        P(("grp", "seq"), None),
        P(),
        P(),
        P(("grp", "seq"), None),
        P(),
        P(),
        P(),
        P(("grp", "seq")),
        P(("grp", "seq"), None),
    )
    return jax.shard_map(
        local,
        mesh=mesh,
        in_specs=placed,
        out_specs=(P(("grp", "seq"), None), P(("grp", "seq"), None), P("grp", None, None)),
        check_vma=False,
    )
```

```python
import math

import jax
import jax.numpy as jnp
from jax import lax
from jax.sharding import PartitionSpec as P


def shifted(value, axis, steps):
    count = lax.axis_size(axis)
    leading, last = (max(0, -steps), min(count, count - steps))
    return lax.ppermute(value, axis, [(source, source + steps) for source in range(leading, last)])


def from_partner(value, axis, distance):
    mask = 2**distance
    pairs = [(source, source ^ mask) for source in range(lax.axis_size(axis))]
    return lax.ppermute(value, axis, pairs)


def upward(value, axis, distance):
    mask = 2**distance
    count = lax.axis_size(axis)
    pairs = [(source, source | mask) for source in range(count) if not source & mask]
    return lax.ppermute(value, axis, pairs)


def all_sum(value, axis):
    for distance in range(lax.axis_size(axis).bit_length() - 1):
        value = value + from_partner(value, axis, distance)
    return value


def contract(form, left, right):
    return jnp.einsum(form, left, right, preferred_element_type=jnp.float32)


def exact(form, left, right):
    return jnp.einsum(form, left, right, precision=lax.Precision.HIGHEST)


def conv_forward(window, conv_weight, conv_bias, length):
    result = jnp.zeros((length, window.shape[1]), jnp.float32) + conv_bias[None, :]
    for offset in range(conv_weight.shape[0]):
        result = (
            result
            + window[offset : offset + length].astype(jnp.float32) * conv_weight[offset][None, :]
        )
    return result


def split_act(preact, heads, head_dim, state_dim):
    length = preact.shape[0]
    inner = heads * head_dim
    x_act = jax.nn.silu(preact[:, :inner]).astype(jnp.bfloat16).reshape(length, heads, head_dim)
    b_key = preact[:, inner : inner + state_dim].astype(jnp.bfloat16)
    c_query = preact[:, inner + state_dim :].astype(jnp.bfloat16)
    return (x_act, b_key, c_query)


def group_state_of(x_part, b_part, decay_part):
    cumul = jnp.cumsum(decay_part, axis=0)
    x_faded = (x_part * jnp.exp(cumul[-1][None, :] - cumul)[:, :, None]).astype(jnp.bfloat16)
    group_state = contract("sn,shp->hnp", b_part, x_faded)
    return (group_state, cumul)


def local_group(x_part, b_part, c_part, cumul, grad_part, weight_zero):
    length = x_part.shape[0]
    state_dim = b_part.shape[1]
    scores = jnp.dot(c_part, b_part.T, preferred_element_type=jnp.float32)
    causal = (jnp.arange(length)[:, None] >= jnp.arange(length)[None, :])[None]
    across = jnp.transpose(cumul)
    spread = across[:, :, None] - across[:, None, :]
    fading = jnp.where(causal, jnp.exp(jnp.where(causal, spread, 0.0)), 0.0)
    basic = fading * scores[None] / state_dim
    intra = (weight_zero[:, None, None] * basic).astype(jnp.bfloat16)
    y_inner = contract("hts,shp->thp", intra, x_part)
    products = contract("thp,shp->hts", grad_part, x_part)
    grad_weight = (
        jnp.sum(weight_zero[:, None, None] * fading * products, axis=0) / state_dim
    ).astype(jnp.bfloat16)
    grad_inner = jnp.dot(grad_weight, b_part, preferred_element_type=jnp.float32)
    level_zero = jnp.sum(basic * products, axis=(1, 2))
    return (y_inner, grad_inner, level_zero)


def combine(block, block_decay, other, other_decay, leading, upper):
    grown = upper[..., None, None]
    found = grown * jnp.exp(leading)[..., None, None] * other
    joined = grown * (other * jnp.exp(block_decay)[..., None, None] + block) + (1.0 - grown) * (
        block * jnp.exp(other_decay)[..., None, None] + other
    )
    return (joined, block_decay + other_decay, leading + upper * other_decay, found)


def relay(value, axis, bit_pos):
    half = 2**bit_pos
    step = half // 2
    parts = 4 if value.shape[0] % 4 == 0 else 1
    size = value.shape[0] // parts
    received = []
    for index in range(parts):
        piece = value[index * size : (index + 1) * size]
        first = lax.ppermute(piece, axis, [(source, source + step) for source in range(half - step, half)])
        second = lax.ppermute(first, axis, [(source, source + step) for source in range(half, half + step)])
        received.append(first + second)
    return jnp.concatenate(received, axis=0)


def exchange(block, block_decay, depth, myself, decays):
    leading = jnp.zeros_like(block_decay)
    found_all = []
    first = None
    for bit_pos in range(depth):
        if bit_pos == depth - 1:
            if bit_pos == 0:
                sent = upward(block.astype(jnp.bfloat16), "seq", bit_pos)
            else:
                sent = relay(block.astype(jnp.bfloat16), "seq", bit_pos)
            other, other_decay = (sent.astype(jnp.float32), jnp.zeros_like(block_decay))
        else:
            sent = from_partner(block.astype(jnp.bfloat16), "seq", bit_pos)
            other, other_decay = (sent.astype(jnp.float32), decays[bit_pos])
        first = sent if first is None else first
        upper = jnp.zeros_like(block_decay) + (jnp.right_shift(myself, bit_pos) & 1).astype(
            jnp.float32
        )
        block, block_decay, leading, found = combine(
            block, block_decay, other, other_decay, leading, upper
        )
        found_all.append(found)
    first = block if first is None else first
    return (jnp.stack(found_all, axis=0), first)


def local(
    xbc_in, conv_weight, conv_bias, dt_raw, decay_rate, skip, level_table, group_class, cotangent
):
    length = xbc_in.shape[0]
    taps = conv_weight.shape[0]
    heads = dt_raw.shape[1]
    inner = cotangent.shape[1]
    head_dim = inner // heads
    state_dim = (xbc_in.shape[1] - inner) // 2
    classes = level_table.shape[0]
    levels = level_table.shape[1]
    groups = group_class.shape[0]
    group_len = length // groups
    edge_part = shifted(xbc_in[length - taps + 1 :], "seq", 1)
    window = jnp.concatenate([edge_part, xbc_in], axis=0)
    preact = conv_forward(window, conv_weight, conv_bias, length)
    x_act, b_key, c_query = split_act(preact, heads, head_dim, state_dim)
    log_decay = -decay_rate[None, :] * jax.nn.softplus(dt_raw)
    grad_out = cotangent.reshape(length, heads, head_dim)
    picked = (group_class[:, None] == jnp.arange(classes, dtype=jnp.int32)[None, :]).astype(
        jnp.float32
    )
    weight_rows = exact("gk,klh->glh", picked, level_table)
    x_groups = x_act.reshape(groups, group_len, heads, head_dim)
    c_groups = c_query.reshape(groups, group_len, state_dim)
    grad_groups = grad_out.reshape(groups, group_len, heads, head_dim)
    b_groups = b_key.reshape(groups, group_len, state_dim)
    states, cumuls = jax.vmap(group_state_of)(
        x_groups, b_groups, log_decay.reshape(groups, group_len, heads)
    )
    totals = cumuls[:, -1]
    dev_decay = jnp.sum(totals, axis=0)
    later = dev_decay[None, :] - jnp.cumsum(totals, axis=0)
    dev_state = jnp.sum(jnp.exp(later)[:, :, None, None] * states, axis=0)
    devices = lax.axis_size("seq")
    depth = devices.bit_length() - 1
    myself = lax.axis_index("seq")
    decays = []
    running = dev_decay
    for bit_pos in range(depth - 1):
        decays.append(from_partner(running, "seq", bit_pos))
        running = running + decays[-1]
    chunks = 2 if heads % 2 == 0 else 1
    width = heads // chunks
    pieces = [
        exchange(
            dev_state[k * width : (k + 1) * width],
            dev_decay[k * width : (k + 1) * width],
            depth,
            myself,
            [decay[k * width : (k + 1) * width] for decay in decays],
        )
        for k in range(chunks)
    ]
    cross = jnp.concatenate([piece for piece, _ in pieces], axis=1)
    late_cotangent = lax.optimization_barrier((cotangent, pieces[0][1]))[0]
    grad_groups = late_cotangent.reshape(groups, group_len, heads, head_dim)
    y_inner, grad_inner, level_zero = jax.vmap(local_group)(
        x_groups, b_groups, c_groups, cumuls, grad_groups, weight_rows[:, 0]
    )
    low_levels = groups.bit_length() - 1
    local_ids = jnp.arange(groups, dtype=jnp.int32)
    differ = jnp.bitwise_xor(local_ids[:, None], local_ids[None, :])
    lower = local_ids[:, None] > local_ids[None, :]
    slot_of = jnp.zeros((groups, groups), jnp.int32)
    onehot = (
        (slot_of[:, :, None] == jnp.arange(low_levels, dtype=jnp.int32)[None, None, :])
        & lower[:, :, None]
    ).astype(jnp.float32)
    before = jnp.cumsum(totals, axis=0) - totals
    gap = before[:, None, :] - before[None, :, :] - totals[None, :, :]
    below = lower[:, :, None]
    fade_pairs = jnp.where(below, jnp.exp(jnp.where(below, gap, 0.0)), 0.0)
    local_weight = exact("cds,csh->cdh", onehot, weight_rows[:, 1 : 1 + low_levels]) * fade_pairs
    lead_fade = jnp.exp(before)
    cross_weight = weight_rows[:, 1 + low_levels : 1 + low_levels + depth] * lead_fade[:, None, :]
    terms = [local_weight[:, d, :, None, None] * states[d][None] for d in range(groups)]
    terms += [cross_weight[:, l, :, None, None] * cross[l][None] for l in range(depth)]
    mixed = sum(terms[1:], terms[0]).astype(jnp.bfloat16)
    scaled = jnp.exp(cumuls) / state_dim
    query_faded = (c_groups[:, :, None, :] * scaled[:, :, :, None]).astype(jnp.bfloat16)
    y_cross = contract("cthn,chnp->cthp", query_faded, mixed)
    backed = contract("chnp,cthp->cthn", mixed, grad_groups)
    grad_cross = jnp.sum(backed * scaled[:, :, :, None], axis=2)
    gram = contract("cthn,cthp->chnp", query_faded, grad_groups)
    inner_pairs = jnp.sum(states[None] * gram[:, None], axis=(3, 4))
    level_local = exact("cds,cdh->csh", onehot, fade_pairs * inner_pairs)
    level_cross = lead_fade[:, None, :] * jnp.sum(cross[None] * gram[:, None], axis=(3, 4))
    level_rest = jnp.concatenate(
        [
            level_local,
            level_cross,
            jnp.zeros((groups, levels - 1 - low_levels - depth, heads), jnp.float32),
        ],
        axis=1,
    )
    grads = exact("ck,clh->klh", picked, level_rest)
    ssm_out = (
        (y_inner + y_cross + skip[None, None, :, None] * x_groups)
        .astype(jnp.bfloat16)
        .reshape(length, inner)
    )
    grad_query = (grad_inner + grad_cross).reshape(length, state_dim)
    after_rows = shifted(grad_query[: taps - 1], "seq", -1)
    extended = jnp.concatenate([grad_query, after_rows], axis=0)
    query_taps = conv_weight[:, inner + state_dim :]
    grad_c_in = jnp.zeros((length, state_dim), jnp.float32)
    for offset in range(taps):
        lagged = taps - 1 - offset
        grad_c_in = grad_c_in + query_taps[offset][None, :] * extended[lagged : lagged + length]
    grad_first = exact("gk,gh->kh", picked, level_zero)
    local_grads = jnp.concatenate([grad_first[:, None, :], grads], axis=1)
    summed = all_sum(local_grads, "seq")
    level_update = level_table + summed / math.sqrt(length * devices)
    return (ssm_out, grad_c_in, level_update)


def solution(mesh):
    placed = (
        P(("grp", "seq"), None),
        P(),
        P(),
        P(("grp", "seq"), None),
        P(),
        P(),
        P(),
        P(("grp", "seq")),
        P(("grp", "seq"), None),
    )
    return jax.shard_map(
        local,
        mesh=mesh,
        in_specs=placed,
        out_specs=(P(("grp", "seq"), None), P(("grp", "seq"), None), P("grp", None, None)),
        check_vma=False,
    )
```

```python
import math

import jax
import jax.numpy as jnp
from jax import lax
from jax.sharding import PartitionSpec as P


def shifted(value, axis, steps):
    count = lax.axis_size(axis)
    leading, last = (max(0, -steps), min(count, count - steps))
    return lax.ppermute(value, axis, [(source, source + steps) for source in range(leading, last)])


def from_partner(value, axis, distance):
    mask = 2**distance
    pairs = [(source, source ^ mask) for source in range(lax.axis_size(axis))]
    return lax.ppermute(value, axis, pairs)


def upward(value, axis, distance):
    mask = 2**distance
    count = lax.axis_size(axis)
    pairs = [(source, source | mask) for source in range(count) if not source & mask]
    return lax.ppermute(value, axis, pairs)


def all_sum(value, axis):
    count = lax.axis_size(axis)
    if count > 8:
        for distance in range(count.bit_length() - 1):
            value = value + from_partner(value, axis, distance)
        return value
    received = [value] + [
        lax.ppermute(value, axis, [(source, (source + shift) % count) for source in range(count)])
        for shift in range(1, count)
    ]
    stacked = jnp.stack(received, axis=0)
    myself = lax.axis_index(axis)
    order = (myself - jnp.arange(count, dtype=jnp.int32)) % count
    return jnp.sum(jnp.take(stacked, order, axis=0), axis=0)


def contract(form, left, right):
    return jnp.einsum(form, left, right, preferred_element_type=jnp.float32)


def exact(form, left, right):
    return jnp.einsum(form, left, right, precision=lax.Precision.HIGHEST)


def conv_forward(window, conv_weight, conv_bias, length):
    result = jnp.zeros((length, window.shape[1]), jnp.float32) + conv_bias[None, :]
    for offset in range(conv_weight.shape[0]):
        result = (
            result
            + window[offset : offset + length].astype(jnp.float32) * conv_weight[offset][None, :]
        )
    return result


def split_act(preact, heads, head_dim, state_dim):
    length = preact.shape[0]
    inner = heads * head_dim
    x_act = jax.nn.silu(preact[:, :inner]).astype(jnp.bfloat16).reshape(length, heads, head_dim)
    b_key = preact[:, inner : inner + state_dim].astype(jnp.bfloat16)
    c_query = preact[:, inner + state_dim :].astype(jnp.bfloat16)
    return (x_act, b_key, c_query)


def group_state_of(x_part, b_part, decay_part):
    cumul = jnp.cumsum(decay_part, axis=0)
    x_faded = (x_part * jnp.exp(cumul[-1][None, :] - cumul)[:, :, None]).astype(jnp.bfloat16)
    group_state = contract("sn,shp->hnp", b_part, x_faded)
    return (group_state, cumul)


def local_group(x_part, b_part, c_part, cumul, grad_part, weight_zero):
    length = x_part.shape[0]
    state_dim = b_part.shape[1]
    scores = jnp.dot(c_part, b_part.T, preferred_element_type=jnp.float32)
    causal = (jnp.arange(length)[:, None] >= jnp.arange(length)[None, :])[None]
    across = jnp.transpose(cumul)
    spread = across[:, :, None] - across[:, None, :]
    fading = jnp.where(causal, jnp.exp(jnp.where(causal, spread, 0.0)), 0.0)
    basic = fading * scores[None] / state_dim
    intra = (weight_zero[:, None, None] * basic).astype(jnp.bfloat16)
    y_inner = contract("hts,shp->thp", intra, x_part)
    products = contract("thp,shp->hts", grad_part, x_part)
    grad_weight = (
        jnp.sum(weight_zero[:, None, None] * fading * products, axis=0) / state_dim
    ).astype(jnp.bfloat16)
    grad_inner = jnp.dot(grad_weight, b_part, preferred_element_type=jnp.float32)
    level_zero = jnp.sum(basic * products, axis=(1, 2))
    return (y_inner, grad_inner, level_zero)


def combine(block, block_decay, other, other_decay, leading, upper):
    grown = upper[..., None, None]
    found = grown * jnp.exp(leading)[..., None, None] * other
    joined = grown * (other * jnp.exp(block_decay)[..., None, None] + block) + (1.0 - grown) * (
        block * jnp.exp(other_decay)[..., None, None] + other
    )
    return (joined, block_decay + other_decay, leading + upper * other_decay, found)


def relay(value, axis, bit_pos):
    half = 2**bit_pos
    step = half // 2
    parts = 2 if value.shape[0] % 2 == 0 else 1
    size = value.shape[0] // parts
    received = []
    for index in range(parts):
        piece = value[index * size : (index + 1) * size]
        first = lax.ppermute(piece, axis, [(source, source + step) for source in range(half - step, half)])
        second = lax.ppermute(first, axis, [(source, source + step) for source in range(half, half + step)])
        received.append(first + second)
    return jnp.concatenate(received, axis=0)


def exchange(block, block_decay, depth, myself, decays):
    leading = jnp.zeros_like(block_decay)
    found_all = []
    first = None
    for bit_pos in range(depth):
        if bit_pos == depth - 1:
            if bit_pos == 0:
                sent = upward(block.astype(jnp.bfloat16), "seq", bit_pos)
            else:
                sent = relay(block.astype(jnp.bfloat16), "seq", bit_pos)
            other, other_decay = (sent.astype(jnp.float32), jnp.zeros_like(block_decay))
        else:
            sent = from_partner(block.astype(jnp.bfloat16), "seq", bit_pos)
            other, other_decay = (sent.astype(jnp.float32), decays[bit_pos])
        first = sent if first is None else first
        upper = jnp.zeros_like(block_decay) + (jnp.right_shift(myself, bit_pos) & 1).astype(
            jnp.float32
        )
        block, block_decay, leading, found = combine(
            block, block_decay, other, other_decay, leading, upper
        )
        found_all.append(found)
    first = block if first is None else first
    return (jnp.stack(found_all, axis=0), first)


def local(
    xbc_in, conv_weight, conv_bias, dt_raw, decay_rate, skip, level_table, group_class, cotangent
):
    length = xbc_in.shape[0]
    taps = conv_weight.shape[0]
    heads = dt_raw.shape[1]
    inner = cotangent.shape[1]
    head_dim = inner // heads
    state_dim = (xbc_in.shape[1] - inner) // 2
    classes = level_table.shape[0]
    levels = level_table.shape[1]
    groups = group_class.shape[0]
    group_len = length // groups
    edge_part = shifted(xbc_in[length - taps + 1 :], "seq", 1)
    window = jnp.concatenate([edge_part, xbc_in], axis=0)
    preact = conv_forward(window, conv_weight, conv_bias, length)
    x_act, b_key, c_query = split_act(preact, heads, head_dim, state_dim)
    log_decay = -decay_rate[None, :] * jax.nn.softplus(dt_raw)
    grad_out = cotangent.reshape(length, heads, head_dim)
    picked = (group_class[:, None] == jnp.arange(classes, dtype=jnp.int32)[None, :]).astype(
        jnp.float32
    )
    weight_rows = exact("gk,klh->glh", picked, level_table)
    x_groups = x_act.reshape(groups, group_len, heads, head_dim)
    c_groups = c_query.reshape(groups, group_len, state_dim)
    grad_groups = grad_out.reshape(groups, group_len, heads, head_dim)
    b_groups = b_key.reshape(groups, group_len, state_dim)
    states, cumuls = jax.vmap(group_state_of)(
        x_groups, b_groups, log_decay.reshape(groups, group_len, heads)
    )
    totals = cumuls[:, -1]
    dev_decay = jnp.sum(totals, axis=0)
    later = dev_decay[None, :] - jnp.cumsum(totals, axis=0)
    dev_state = jnp.sum(jnp.exp(later)[:, :, None, None] * states, axis=0)
    devices = lax.axis_size("seq")
    depth = devices.bit_length() - 1
    myself = lax.axis_index("seq")
    decays = []
    running = dev_decay
    for bit_pos in range(depth - 1):
        decays.append(from_partner(running, "seq", bit_pos))
        running = running + decays[-1]
    chunks = 2 if heads % 2 == 0 else 1
    width = heads // chunks
    pieces = [
        exchange(
            dev_state[k * width : (k + 1) * width],
            dev_decay[k * width : (k + 1) * width],
            depth,
            myself,
            [decay[k * width : (k + 1) * width] for decay in decays],
        )
        for k in range(chunks)
    ]
    cross = jnp.concatenate([piece for piece, _ in pieces], axis=1)
    late_cotangent = lax.optimization_barrier((cotangent, pieces[0][1]))[0]
    grad_groups = late_cotangent.reshape(groups, group_len, heads, head_dim)
    y_inner, grad_inner, level_zero = jax.vmap(local_group)(
        x_groups, b_groups, c_groups, cumuls, grad_groups, weight_rows[:, 0]
    )
    low_levels = groups.bit_length() - 1
    local_ids = jnp.arange(groups, dtype=jnp.int32)
    differ = jnp.bitwise_xor(local_ids[:, None], local_ids[None, :])
    lower = local_ids[:, None] > local_ids[None, :]
    slot_of = jnp.zeros((groups, groups), jnp.int32)
    onehot = (
        (slot_of[:, :, None] == jnp.arange(low_levels, dtype=jnp.int32)[None, None, :])
        & lower[:, :, None]
    ).astype(jnp.float32)
    before = jnp.cumsum(totals, axis=0) - totals
    gap = before[:, None, :] - before[None, :, :] - totals[None, :, :]
    below = lower[:, :, None]
    fade_pairs = jnp.where(below, jnp.exp(jnp.where(below, gap, 0.0)), 0.0)
    local_weight = exact("cds,csh->cdh", onehot, weight_rows[:, 1 : 1 + low_levels]) * fade_pairs
    lead_fade = jnp.exp(before)
    cross_weight = weight_rows[:, 1 + low_levels : 1 + low_levels + depth] * lead_fade[:, None, :]
    terms = [local_weight[:, d, :, None, None] * states[d][None] for d in range(groups)]
    terms += [cross_weight[:, l, :, None, None] * cross[l][None] for l in range(depth)]
    mixed = sum(terms[1:], terms[0]).astype(jnp.bfloat16)
    scaled = jnp.exp(cumuls) / state_dim
    query_faded = (c_groups[:, :, None, :] * scaled[:, :, :, None]).astype(jnp.bfloat16)
    y_cross = contract("cthn,chnp->cthp", query_faded, mixed)
    backed = contract("chnp,cthp->cthn", mixed, grad_groups)
    grad_cross = jnp.sum(backed * scaled[:, :, :, None], axis=2)
    gram = contract("cthn,cthp->chnp", query_faded, grad_groups)
    inner_pairs = jnp.sum(states[None] * gram[:, None], axis=(3, 4))
    level_local = exact("cds,cdh->csh", onehot, fade_pairs * inner_pairs)
    level_cross = lead_fade[:, None, :] * jnp.sum(cross[None] * gram[:, None], axis=(3, 4))
    level_rest = jnp.concatenate(
        [
            level_local,
            level_cross,
            jnp.zeros((groups, levels - 1 - low_levels - depth, heads), jnp.float32),
        ],
        axis=1,
    )
    grads = exact("ck,clh->klh", picked, level_rest)
    ssm_out = (
        (y_inner + y_cross + skip[None, None, :, None] * x_groups)
        .astype(jnp.bfloat16)
        .reshape(length, inner)
    )
    grad_query = (grad_inner + grad_cross).reshape(length, state_dim)
    after_rows = shifted(grad_query[: taps - 1], "seq", -1)
    extended = jnp.concatenate([grad_query, after_rows], axis=0)
    query_taps = conv_weight[:, inner + state_dim :]
    grad_c_in = jnp.zeros((length, state_dim), jnp.float32)
    for offset in range(taps):
        lagged = taps - 1 - offset
        grad_c_in = grad_c_in + query_taps[offset][None, :] * extended[lagged : lagged + length]
    grad_first = exact("gk,gh->kh", picked, level_zero)
    local_grads = jnp.concatenate([grad_first[:, None, :], grads], axis=1)
    summed = all_sum(local_grads, "seq")
    level_update = level_table + summed / math.sqrt(length * devices)
    return (ssm_out, grad_c_in, level_update)


def solution(mesh):
    placed = (
        P(("grp", "seq"), None),
        P(),
        P(),
        P(("grp", "seq"), None),
        P(),
        P(),
        P(),
        P(("grp", "seq")),
        P(("grp", "seq"), None),
    )
    return jax.shard_map(
        local,
        mesh=mesh,
        in_specs=placed,
        out_specs=(P(("grp", "seq"), None), P(("grp", "seq"), None), P("grp", None, None)),
        check_vma=False,
    )
```

```python
import math

import jax
import jax.numpy as jnp
from jax import lax
from jax.sharding import PartitionSpec as P


def shifted(value, axis, steps):
    count = lax.axis_size(axis)
    leading, last = (max(0, -steps), min(count, count - steps))
    return lax.ppermute(value, axis, [(source, source + steps) for source in range(leading, last)])


def from_partner(value, axis, distance):
    mask = 2**distance
    pairs = [(source, source ^ mask) for source in range(lax.axis_size(axis))]
    return lax.ppermute(value, axis, pairs)


def upward(value, axis, distance):
    mask = 2**distance
    count = lax.axis_size(axis)
    pairs = [(source, source | mask) for source in range(count) if not source & mask]
    return lax.ppermute(value, axis, pairs)


def all_sum(value, axis):
    for distance in range(lax.axis_size(axis).bit_length() - 1):
        value = value + from_partner(value, axis, distance)
    return value


def contract(form, left, right):
    return jnp.einsum(form, left, right, preferred_element_type=jnp.float32)


def exact(form, left, right):
    return jnp.einsum(form, left, right, precision=lax.Precision.HIGHEST)


def conv_forward(window, conv_weight, conv_bias, length):
    result = jnp.zeros((length, window.shape[1]), jnp.float32) + conv_bias[None, :]
    for offset in range(conv_weight.shape[0]):
        result = (
            result
            + window[offset : offset + length].astype(jnp.float32) * conv_weight[offset][None, :]
        )
    return result


def split_act(preact, heads, head_dim, state_dim):
    length = preact.shape[0]
    inner = heads * head_dim
    x_act = jax.nn.silu(preact[:, :inner]).astype(jnp.bfloat16).reshape(length, heads, head_dim)
    b_key = preact[:, inner : inner + state_dim].astype(jnp.bfloat16)
    c_query = preact[:, inner + state_dim :].astype(jnp.bfloat16)
    return (x_act, b_key, c_query)


def group_state_of(x_part, b_part, decay_part):
    cumul = jnp.cumsum(decay_part, axis=0)
    x_faded = (x_part * jnp.exp(cumul[-1][None, :] - cumul)[:, :, None]).astype(jnp.bfloat16)
    group_state = contract("sn,shp->hnp", b_part, x_faded)
    return (group_state, cumul)


def local_group(x_part, b_part, c_part, cumul, grad_part, weight_zero):
    length = x_part.shape[0]
    state_dim = b_part.shape[1]
    scores = jnp.dot(c_part, b_part.T, preferred_element_type=jnp.float32)
    causal = (jnp.arange(length)[:, None] >= jnp.arange(length)[None, :])[None]
    across = jnp.transpose(cumul)
    spread = across[:, :, None] - across[:, None, :]
    fading = jnp.where(causal, jnp.exp(jnp.where(causal, spread, 0.0)), 0.0)
    basic = fading * scores[None] / state_dim
    intra = (weight_zero[:, None, None] * basic).astype(jnp.bfloat16)
    y_inner = contract("hts,shp->thp", intra, x_part)
    products = contract("thp,shp->hts", grad_part, x_part)
    grad_weight = (
        jnp.sum(weight_zero[:, None, None] * fading * products, axis=0) / state_dim
    ).astype(jnp.bfloat16)
    grad_inner = jnp.dot(grad_weight, b_part, preferred_element_type=jnp.float32)
    level_zero = jnp.sum(basic * products, axis=(1, 2))
    return (y_inner, grad_inner, level_zero)


def combine(block, block_decay, other, other_decay, leading, upper):
    grown = upper[..., None, None]
    found = grown * jnp.exp(leading)[..., None, None] * other
    joined = grown * (other * jnp.exp(block_decay)[..., None, None] + block) + (1.0 - grown) * (
        block * jnp.exp(other_decay)[..., None, None] + other
    )
    return (joined, block_decay + other_decay, leading + upper * other_decay, found)


def relay(value, axis, bit_pos, parts):
    half = 2**bit_pos
    step = half // 2
    size = value.shape[0] // parts
    received = []
    for index in range(parts):
        piece = value[index * size : (index + 1) * size]
        first = lax.ppermute(piece, axis, [(source, source + step) for source in range(half - step, half)])
        second = lax.ppermute(first, axis, [(source, source + step) for source in range(half, half + step)])
        received.append(first + second)
    return jnp.concatenate(received, axis=0)


def exchange(block, block_decay, depth, myself, decays, start=0, leading=None):
    leading = jnp.zeros_like(block_decay) if leading is None else leading
    found_all = []
    first = None
    for bit_pos in range(start, depth):
        if start == 0 and bit_pos == 1 and depth > 2 and block.shape[0] % 2 == 0:
            size = block.shape[0] // 2
            rest = [
                exchange(
                    block[index * size : (index + 1) * size],
                    block_decay[index * size : (index + 1) * size],
                    depth,
                    myself,
                    [decay[index * size : (index + 1) * size] for decay in decays],
                    1,
                    leading[index * size : (index + 1) * size],
                )[0]
                for index in range(2)
            ]
            later_found = jnp.concatenate(rest, axis=1)
            found_all.extend(later_found[index] for index in range(depth - 1))
            break
        if bit_pos == depth - 1:
            if bit_pos == 0:
                sent = upward(block.astype(jnp.bfloat16), "seq", bit_pos)
            else:
                parts = 2 if start == 0 and block.shape[0] % 2 == 0 else 1
                sent = relay(block.astype(jnp.bfloat16), "seq", bit_pos, parts)
            other, other_decay = (sent.astype(jnp.float32), jnp.zeros_like(block_decay))
        else:
            sent = from_partner(block.astype(jnp.bfloat16), "seq", bit_pos)
            other, other_decay = (sent.astype(jnp.float32), decays[bit_pos])
        first = sent if first is None else first
        upper = jnp.zeros_like(block_decay) + (jnp.right_shift(myself, bit_pos) & 1).astype(
            jnp.float32
        )
        block, block_decay, leading, found = combine(
            block, block_decay, other, other_decay, leading, upper
        )
        found_all.append(found)
    first = block if first is None else first
    return (jnp.stack(found_all, axis=0), first)


def local(
    xbc_in, conv_weight, conv_bias, dt_raw, decay_rate, skip, level_table, group_class, cotangent
):
    length = xbc_in.shape[0]
    taps = conv_weight.shape[0]
    heads = dt_raw.shape[1]
    inner = cotangent.shape[1]
    head_dim = inner // heads
    state_dim = (xbc_in.shape[1] - inner) // 2
    classes = level_table.shape[0]
    levels = level_table.shape[1]
    groups = group_class.shape[0]
    group_len = length // groups
    edge_part = shifted(xbc_in[length - taps + 1 :], "seq", 1)
    window = jnp.concatenate([edge_part, xbc_in], axis=0)
    preact = conv_forward(window, conv_weight, conv_bias, length)
    x_act, b_key, c_query = split_act(preact, heads, head_dim, state_dim)
    log_decay = -decay_rate[None, :] * jax.nn.softplus(dt_raw)
    grad_out = cotangent.reshape(length, heads, head_dim)
    picked = (group_class[:, None] == jnp.arange(classes, dtype=jnp.int32)[None, :]).astype(
        jnp.float32
    )
    weight_rows = exact("gk,klh->glh", picked, level_table)
    x_groups = x_act.reshape(groups, group_len, heads, head_dim)
    c_groups = c_query.reshape(groups, group_len, state_dim)
    grad_groups = grad_out.reshape(groups, group_len, heads, head_dim)
    b_groups = b_key.reshape(groups, group_len, state_dim)
    states, cumuls = jax.vmap(group_state_of)(
        x_groups, b_groups, log_decay.reshape(groups, group_len, heads)
    )
    totals = cumuls[:, -1]
    dev_decay = jnp.sum(totals, axis=0)
    later = dev_decay[None, :] - jnp.cumsum(totals, axis=0)
    dev_state = jnp.sum(jnp.exp(later)[:, :, None, None] * states, axis=0)
    devices = lax.axis_size("seq")
    depth = devices.bit_length() - 1
    myself = lax.axis_index("seq")
    decays = []
    running = dev_decay
    for bit_pos in range(depth - 1):
        decays.append(from_partner(running, "seq", bit_pos))
        running = running + decays[-1]
    chunks = 2 if heads % 2 == 0 else 1
    width = heads // chunks
    pieces = [
        exchange(
            dev_state[k * width : (k + 1) * width],
            dev_decay[k * width : (k + 1) * width],
            depth,
            myself,
            [decay[k * width : (k + 1) * width] for decay in decays],
        )
        for k in range(chunks)
    ]
    cross = jnp.concatenate([piece for piece, _ in pieces], axis=1)
    late_cotangent = lax.optimization_barrier((cotangent, pieces[0][1]))[0]
    grad_groups = late_cotangent.reshape(groups, group_len, heads, head_dim)
    y_inner, grad_inner, level_zero = jax.vmap(local_group)(
        x_groups, b_groups, c_groups, cumuls, grad_groups, weight_rows[:, 0]
    )
    low_levels = groups.bit_length() - 1
    local_ids = jnp.arange(groups, dtype=jnp.int32)
    differ = jnp.bitwise_xor(local_ids[:, None], local_ids[None, :])
    lower = local_ids[:, None] > local_ids[None, :]
    slot_of = jnp.zeros((groups, groups), jnp.int32)
    onehot = (
        (slot_of[:, :, None] == jnp.arange(low_levels, dtype=jnp.int32)[None, None, :])
        & lower[:, :, None]
    ).astype(jnp.float32)
    before = jnp.cumsum(totals, axis=0) - totals
    gap = before[:, None, :] - before[None, :, :] - totals[None, :, :]
    below = lower[:, :, None]
    fade_pairs = jnp.where(below, jnp.exp(jnp.where(below, gap, 0.0)), 0.0)
    local_weight = exact("cds,csh->cdh", onehot, weight_rows[:, 1 : 1 + low_levels]) * fade_pairs
    lead_fade = jnp.exp(before)
    cross_weight = weight_rows[:, 1 + low_levels : 1 + low_levels + depth] * lead_fade[:, None, :]
    terms = [local_weight[:, d, :, None, None] * states[d][None] for d in range(groups)]
    terms += [cross_weight[:, l, :, None, None] * cross[l][None] for l in range(depth)]
    mixed = sum(terms[1:], terms[0]).astype(jnp.bfloat16)
    scaled = jnp.exp(cumuls) / state_dim
    query_faded = (c_groups[:, :, None, :] * scaled[:, :, :, None]).astype(jnp.bfloat16)
    y_cross = contract("cthn,chnp->cthp", query_faded, mixed)
    backed = contract("chnp,cthp->cthn", mixed, grad_groups)
    grad_cross = jnp.sum(backed * scaled[:, :, :, None], axis=2)
    gram = contract("cthn,cthp->chnp", query_faded, grad_groups)
    inner_pairs = jnp.sum(states[None] * gram[:, None], axis=(3, 4))
    level_local = exact("cds,cdh->csh", onehot, fade_pairs * inner_pairs)
    level_cross = lead_fade[:, None, :] * jnp.sum(cross[None] * gram[:, None], axis=(3, 4))
    level_rest = jnp.concatenate(
        [
            level_local,
            level_cross,
            jnp.zeros((groups, levels - 1 - low_levels - depth, heads), jnp.float32),
        ],
        axis=1,
    )
    grads = exact("ck,clh->klh", picked, level_rest)
    ssm_out = (
        (y_inner + y_cross + skip[None, None, :, None] * x_groups)
        .astype(jnp.bfloat16)
        .reshape(length, inner)
    )
    grad_query = (grad_inner + grad_cross).reshape(length, state_dim)
    after_rows = shifted(grad_query[: taps - 1], "seq", -1)
    extended = jnp.concatenate([grad_query, after_rows], axis=0)
    query_taps = conv_weight[:, inner + state_dim :]
    grad_c_in = jnp.zeros((length, state_dim), jnp.float32)
    for offset in range(taps):
        lagged = taps - 1 - offset
        grad_c_in = grad_c_in + query_taps[offset][None, :] * extended[lagged : lagged + length]
    grad_first = exact("gk,gh->kh", picked, level_zero)
    local_grads = jnp.concatenate([grad_first[:, None, :], grads], axis=1)
    summed = all_sum(local_grads, "seq")
    level_update = level_table + summed / math.sqrt(length * devices)
    return (ssm_out, grad_c_in, level_update)


def solution(mesh):
    placed = (
        P(("grp", "seq"), None),
        P(),
        P(),
        P(("grp", "seq"), None),
        P(),
        P(),
        P(),
        P(("grp", "seq")),
        P(("grp", "seq"), None),
    )
    return jax.shard_map(
        local,
        mesh=mesh,
        in_specs=placed,
        out_specs=(P(("grp", "seq"), None), P(("grp", "seq"), None), P("grp", None, None)),
        check_vma=False,
    )
```

```python
import math

import jax
import jax.numpy as jnp
from jax import lax
from jax.sharding import PartitionSpec as P


def shifted(value, axis, steps):
    count = lax.axis_size(axis)
    leading, last = (max(0, -steps), min(count, count - steps))
    return lax.ppermute(value, axis, [(source, source + steps) for source in range(leading, last)])


def from_partner(value, axis, distance):
    mask = 2**distance
    pairs = [(source, source ^ mask) for source in range(lax.axis_size(axis))]
    return lax.ppermute(value, axis, pairs)


def upward(value, axis, distance):
    mask = 2**distance
    count = lax.axis_size(axis)
    pairs = [(source, source | mask) for source in range(count) if not source & mask]
    return lax.ppermute(value, axis, pairs)


def all_sum(value, axis):
    for distance in range(lax.axis_size(axis).bit_length() - 1):
        value = value + from_partner(value, axis, distance)
    return value


def contract(form, left, right):
    return jnp.einsum(form, left, right, preferred_element_type=jnp.float32)


def exact(form, left, right):
    return jnp.einsum(form, left, right, precision=lax.Precision.HIGHEST)


def conv_forward(window, conv_weight, conv_bias, length):
    result = jnp.zeros((length, window.shape[1]), jnp.float32) + conv_bias[None, :]
    for offset in range(conv_weight.shape[0]):
        result = (
            result
            + window[offset : offset + length].astype(jnp.float32) * conv_weight[offset][None, :]
        )
    return result


def split_act(preact, heads, head_dim, state_dim):
    length = preact.shape[0]
    inner = heads * head_dim
    x_act = jax.nn.silu(preact[:, :inner]).astype(jnp.bfloat16).reshape(length, heads, head_dim)
    b_key = preact[:, inner : inner + state_dim].astype(jnp.bfloat16)
    c_query = preact[:, inner + state_dim :].astype(jnp.bfloat16)
    return (x_act, b_key, c_query)


def group_state_of(x_part, b_part, decay_part):
    cumul = jnp.cumsum(decay_part, axis=0)
    x_faded = (x_part * jnp.exp(cumul[-1][None, :] - cumul)[:, :, None]).astype(jnp.bfloat16)
    group_state = contract("sn,shp->hnp", b_part, x_faded)
    return (group_state, cumul)


def local_group(x_part, b_part, c_part, cumul, grad_part, weight_zero):
    length = x_part.shape[0]
    state_dim = b_part.shape[1]
    scores = jnp.dot(c_part, b_part.T, preferred_element_type=jnp.float32)
    causal = (jnp.arange(length)[:, None] >= jnp.arange(length)[None, :])[None]
    across = jnp.transpose(cumul)
    spread = across[:, :, None] - across[:, None, :]
    fading = jnp.where(causal, jnp.exp(jnp.where(causal, spread, 0.0)), 0.0)
    basic = fading * scores[None] / state_dim
    intra = (weight_zero[:, None, None] * basic).astype(jnp.bfloat16)
    y_inner = contract("hts,shp->thp", intra, x_part)
    products = contract("thp,shp->hts", grad_part, x_part)
    grad_weight = (
        jnp.sum(weight_zero[:, None, None] * fading * products, axis=0) / state_dim
    ).astype(jnp.bfloat16)
    grad_inner = jnp.dot(grad_weight, b_part, preferred_element_type=jnp.float32)
    level_zero = jnp.sum(basic * products, axis=(1, 2))
    return (y_inner, grad_inner, level_zero)


def combine(block, block_decay, other, other_decay, leading, upper):
    grown = upper[..., None, None]
    found = grown * jnp.exp(leading)[..., None, None] * other
    joined = grown * (other * jnp.exp(block_decay)[..., None, None] + block) + (1.0 - grown) * (
        block * jnp.exp(other_decay)[..., None, None] + other
    )
    return (joined, block_decay + other_decay, leading + upper * other_decay, found)


def relay(value, axis, bit_pos):
    half = 2**bit_pos
    step = half // 2
    parts = 2 if value.shape[0] % 2 == 0 else 1
    size = value.shape[0] // parts
    received = []
    for index in range(parts):
        piece = value[index * size : (index + 1) * size]
        first = lax.ppermute(piece, axis, [(source, source + step) for source in range(half - step, half)])
        second = lax.ppermute(first, axis, [(source, source + step) for source in range(half, half + step)])
        received.append(first + second)
    return jnp.concatenate(received, axis=0)


def exchange(block, block_decay, depth, myself, decays):
    leading = jnp.zeros_like(block_decay)
    found_all = []
    first = None
    for bit_pos in range(depth):
        if bit_pos == depth - 1:
            if bit_pos == 0:
                sent = upward(block.astype(jnp.bfloat16), "seq", bit_pos)
            else:
                sent = relay(block.astype(jnp.bfloat16), "seq", bit_pos)
            other, other_decay = (sent.astype(jnp.float32), jnp.zeros_like(block_decay))
        else:
            sent = from_partner(block.astype(jnp.bfloat16), "seq", bit_pos)
            other, other_decay = (sent.astype(jnp.float32), decays[bit_pos])
        first = sent if first is None else first
        upper = jnp.zeros_like(block_decay) + (jnp.right_shift(myself, bit_pos) & 1).astype(
            jnp.float32
        )
        block, block_decay, leading, found = combine(
            block, block_decay, other, other_decay, leading, upper
        )
        found_all.append(found)
    first = block if first is None else first
    return (jnp.stack(found_all, axis=0), first)


def local(
    xbc_in, conv_weight, conv_bias, dt_raw, decay_rate, skip, level_table, group_class, cotangent
):
    length = xbc_in.shape[0]
    taps = conv_weight.shape[0]
    heads = dt_raw.shape[1]
    inner = cotangent.shape[1]
    head_dim = inner // heads
    state_dim = (xbc_in.shape[1] - inner) // 2
    classes = level_table.shape[0]
    levels = level_table.shape[1]
    groups = group_class.shape[0]
    group_len = length // groups
    edge_part = shifted(xbc_in[length - taps + 1 :], "seq", 1)
    window = jnp.concatenate([edge_part, xbc_in], axis=0)
    preact = conv_forward(window, conv_weight, conv_bias, length)
    x_act, b_key, c_query = split_act(preact, heads, head_dim, state_dim)
    log_decay = -decay_rate[None, :] * jax.nn.softplus(dt_raw)
    grad_out = cotangent.reshape(length, heads, head_dim)
    picked = (group_class[:, None] == jnp.arange(classes, dtype=jnp.int32)[None, :]).astype(
        jnp.float32
    )
    weight_rows = exact("gk,klh->glh", picked, level_table)
    x_groups = x_act.reshape(groups, group_len, heads, head_dim)
    c_groups = c_query.reshape(groups, group_len, state_dim)
    grad_groups = grad_out.reshape(groups, group_len, heads, head_dim)
    b_groups = b_key.reshape(groups, group_len, state_dim)
    states, cumuls = jax.vmap(group_state_of)(
        x_groups, b_groups, log_decay.reshape(groups, group_len, heads)
    )
    totals = cumuls[:, -1]
    dev_decay = jnp.sum(totals, axis=0)
    later = dev_decay[None, :] - jnp.cumsum(totals, axis=0)
    dev_state = jnp.sum(jnp.exp(later)[:, :, None, None] * states, axis=0)
    devices = lax.axis_size("seq")
    depth = devices.bit_length() - 1
    myself = lax.axis_index("seq")
    decays = []
    running = dev_decay
    for bit_pos in range(depth - 1):
        decays.append(from_partner(running, "seq", bit_pos))
        running = running + decays[-1]
    chunks = 2 if heads % 2 == 0 else 1
    width = heads // chunks
    pieces = [
        exchange(
            dev_state[k * width : (k + 1) * width],
            dev_decay[k * width : (k + 1) * width],
            depth,
            myself,
            [decay[k * width : (k + 1) * width] for decay in decays],
        )
        for k in range(chunks)
    ]
    cross = jnp.concatenate([piece for piece, _ in pieces], axis=1)
    late_cotangent = lax.optimization_barrier((cotangent, pieces[-1][1]))[0]
    grad_groups = late_cotangent.reshape(groups, group_len, heads, head_dim)
    y_inner, grad_inner, level_zero = jax.vmap(local_group)(
        x_groups, b_groups, c_groups, cumuls, grad_groups, weight_rows[:, 0]
    )
    low_levels = groups.bit_length() - 1
    local_ids = jnp.arange(groups, dtype=jnp.int32)
    differ = jnp.bitwise_xor(local_ids[:, None], local_ids[None, :])
    lower = local_ids[:, None] > local_ids[None, :]
    slot_of = jnp.zeros((groups, groups), jnp.int32)
    onehot = (
        (slot_of[:, :, None] == jnp.arange(low_levels, dtype=jnp.int32)[None, None, :])
        & lower[:, :, None]
    ).astype(jnp.float32)
    before = jnp.cumsum(totals, axis=0) - totals
    gap = before[:, None, :] - before[None, :, :] - totals[None, :, :]
    below = lower[:, :, None]
    fade_pairs = jnp.where(below, jnp.exp(jnp.where(below, gap, 0.0)), 0.0)
    local_weight = exact("cds,csh->cdh", onehot, weight_rows[:, 1 : 1 + low_levels]) * fade_pairs
    lead_fade = jnp.exp(before)
    cross_weight = weight_rows[:, 1 + low_levels : 1 + low_levels + depth] * lead_fade[:, None, :]
    terms = [local_weight[:, d, :, None, None] * states[d][None] for d in range(groups)]
    terms += [cross_weight[:, l, :, None, None] * cross[l][None] for l in range(depth)]
    mixed = sum(terms[1:], terms[0]).astype(jnp.bfloat16)
    scaled = jnp.exp(cumuls) / state_dim
    query_faded = (c_groups[:, :, None, :] * scaled[:, :, :, None]).astype(jnp.bfloat16)
    y_cross = contract("cthn,chnp->cthp", query_faded, mixed)
    backed = contract("chnp,cthp->cthn", mixed, grad_groups)
    grad_cross = jnp.sum(backed * scaled[:, :, :, None], axis=2)
    gram = contract("cthn,cthp->chnp", query_faded, grad_groups)
    inner_pairs = jnp.sum(states[None] * gram[:, None], axis=(3, 4))
    level_local = exact("cds,cdh->csh", onehot, fade_pairs * inner_pairs)
    level_cross = lead_fade[:, None, :] * jnp.sum(cross[None] * gram[:, None], axis=(3, 4))
    level_rest = jnp.concatenate(
        [
            level_local,
            level_cross,
            jnp.zeros((groups, levels - 1 - low_levels - depth, heads), jnp.float32),
        ],
        axis=1,
    )
    grads = exact("ck,clh->klh", picked, level_rest)
    ssm_out = (
        (y_inner + y_cross + skip[None, None, :, None] * x_groups)
        .astype(jnp.bfloat16)
        .reshape(length, inner)
    )
    grad_query = (grad_inner + grad_cross).reshape(length, state_dim)
    after_rows = shifted(grad_query[: taps - 1], "seq", -1)
    extended = jnp.concatenate([grad_query, after_rows], axis=0)
    query_taps = conv_weight[:, inner + state_dim :]
    grad_c_in = jnp.zeros((length, state_dim), jnp.float32)
    for offset in range(taps):
        lagged = taps - 1 - offset
        grad_c_in = grad_c_in + query_taps[offset][None, :] * extended[lagged : lagged + length]
    grad_first = exact("gk,gh->kh", picked, level_zero)
    local_grads = jnp.concatenate([grad_first[:, None, :], grads], axis=1)
    summed = all_sum(local_grads, "seq")
    level_update = level_table + summed / math.sqrt(length * devices)
    return (ssm_out, grad_c_in, level_update)


def solution(mesh):
    placed = (
        P(("grp", "seq"), None),
        P(),
        P(),
        P(("grp", "seq"), None),
        P(),
        P(),
        P(),
        P(("grp", "seq")),
        P(("grp", "seq"), None),
    )
    return jax.shard_map(
        local,
        mesh=mesh,
        in_specs=placed,
        out_specs=(P(("grp", "seq"), None), P(("grp", "seq"), None), P("grp", None, None)),
        check_vma=False,
    )
```
